128 devices in a mesh: frames: 8 (over y, core), space: 16 (over x, z).
Axes of the slice: x: 4, y: 4, z: 4, core: 2. Of those that a mesh axis runs over, the one named last changes fastest.
Arguments:
- latent: bfloat16 [8, 32, 256, 1152], P('frames', 'space'), may hold values from -6 to 6
- query_rows: bfloat16 [8, 32, 256, 1152], P('frames', 'space'), may hold values from -5.5 to 5.5
- key_rows: bfloat16 [8, 32, 256, 1152], P('frames', 'space'), may hold values from -5.5 to 5.5
- value_rows: bfloat16 [8, 32, 256, 1152], P('frames', 'space'), may hold values from -6 to 6
- cached_out: bfloat16 [8, 32, 256, 1152], P('frames', 'space'), may hold values from -4 to 4
- refreshed: int32 [8, 32], P('frames', 'space'), may hold values from 0 to 1, as said below
- band_width: int32 [16], replicated, may hold values from 1 to 7, as said below
- out_weight: bfloat16 [1152, 1152], replicated, may hold values from -0.1875 to 0.1875
- temporal_weight: bfloat16 [1152, 3456], replicated, may hold values from -0.1360803 to 0.1360803
Outputs:
- mixed: bfloat16 [8, 32, 256, 1152], P('frames', 'space')
The draws below stay inside these ranges and needn't reach their ends.
Inputs may be any that keep to these rules, and one draw needn't show every extreme that they name: `refreshed`: 1 marks a tile that is recomputed; tiles further down a frame are recomputed more often. `band_width`: at least one head reaches 7 frames.
All inputs are finite; a program needn't handle non-finite values.
Results may differ from the reference program's by a relative error of at most 0.008.
Values may be sent and summed in bfloat16 or wider, within the bound.
No kernel may reach another device: no remote copies, remote signals or barrier semaphores. Data moves between devices by JAX's collectives and lax.ppermute only.
A program may use at most 128 MiB of HBM per device.

```python
import math
import jax
import jax.numpy as jnp
from jax import lax

D = 1152
HEADS = 16
TILE_TOK = 256
EDGE = 64
FRAMES = 8
TILES = 32


def drawn_pair(key):
    shape_full = (FRAMES, TILES, TILE_TOK, D)
    query = jnp.clip(jax.random.normal(jax.random.fold_in(key, 11), shape_full, jnp.float32), -5.5, 5.5)
    keys = jnp.clip(jax.random.normal(jax.random.fold_in(key, 12), shape_full, jnp.float32), -5.5, 5.5)
    return (query, keys)


def draw_query_rows(key, part):
    return drawn_pair(key)[0].astype(jnp.bfloat16)


def draw_key_rows(key, part):
    return drawn_pair(key)[1].astype(jnp.bfloat16)


def draw_latent(key, part):
    shape_full = (FRAMES, TILES, TILE_TOK, D)
    base = jnp.clip(jax.random.normal(jax.random.fold_in(key, 31), shape_full, jnp.float32), -6.0, 6.0)
    return base.astype(jnp.bfloat16)


def draw_temporal_weight(key, part):
    base = jnp.clip(jax.random.normal(jax.random.fold_in(key, 41), (D, 3 * D), jnp.float32), -4.0, 4.0) / math.sqrt(D)
    return base.astype(jnp.bfloat16)


def draw_refreshed(key, part):
    level = jax.random.randint(key, (FRAMES, TILES), 0, 8)
    threshold = 1 + 6 * jnp.arange(TILES, dtype=jnp.int32) // TILES
    return (level < threshold[None, :]).astype(jnp.int32)


def draw_band_width(key, part):
    widest = jax.random.randint(jax.random.fold_in(key, 51), (), 0, HEADS)
    reach = jax.random.randint(jax.random.fold_in(key, 52), (HEADS,), 1, FRAMES)
    return jnp.where(jnp.arange(HEADS, dtype=jnp.int32) == widest, FRAMES - 1, reach).astype(jnp.int32)


def block_levels(key, dims, pieces, low, high):
    gain = 1.0
    for axis_at, blocks in pieces:
        heights = jax.random.uniform(jax.random.fold_in(jax.random.fold_in(key, 6), axis_at), (blocks,), jnp.float32, low / len(pieces), high / len(pieces))
        gain = gain * jnp.repeat(jnp.exp(heights), dims[axis_at] // blocks).reshape((-1,) + (1,) * (len(dims) - 1 - axis_at))
    return gain


def gaussian(rng, dims, spread, limit, split=(), held_as=jnp.bfloat16):
    gain = block_levels(rng, dims, split, -0.22, 0.18) if split else 1.0
    entries = jax.random.normal(rng, dims, jnp.float32) * spread * gain
    return jnp.minimum(jnp.maximum(entries, -limit), limit).astype(held_as)


def setup_inputs(seed: int = 0) -> dict:
    streams_of = jax.random.split(jax.random.key(seed), 10)
    latent = draw_latent(jax.random.fold_in(streams_of[9], 71), 0)
    query_rows = draw_query_rows(jax.random.fold_in(streams_of[9], 71), 0)
    key_rows = draw_key_rows(jax.random.fold_in(streams_of[9], 71), 0)
    value_rows = gaussian(streams_of[3], (FRAMES, TILES, TILE_TOK, D), 1.0, 6.0, ((0, 8), (1, 16)))
    cached_out = gaussian(streams_of[4], (FRAMES, TILES, TILE_TOK, D), 0.3, 4.0, ((0, 8), (1, 16)))
    refreshed = draw_refreshed(jax.random.fold_in(streams_of[9], 71), 0)
    band_width = draw_band_width(jax.random.fold_in(streams_of[9], 71), 0)
    out_weight = gaussian(streams_of[7], (D, D), D ** -0.5, 0.1875)
    temporal_weight = draw_temporal_weight(jax.random.fold_in(streams_of[9], 71), 0)
    return {"latent": latent, "query_rows": query_rows, "key_rows": key_rows, "value_rows": value_rows, "cached_out": cached_out, "refreshed": refreshed, "band_width": band_width, "out_weight": out_weight, "temporal_weight": temporal_weight}


def soft_rows(scores):
    top = lax.optimization_barrier(jnp.max(scores, axis=-1, keepdims=True))
    expo = jnp.exp(scores - top)
    return expo / lax.optimization_barrier(jnp.sum(expo, axis=-1, keepdims=True))

def temporal_block(block, band_width, head_count, width):
    adim, sdim, bdim, idim, pdim, _ = block.shape
    head_dim = width // head_count
    scaling = 1.0 / math.sqrt(head_dim)
    query6 = block[..., :width].reshape(adim, sdim, bdim, idim, pdim, head_count, head_dim).astype(jnp.float32)
    key6 = block[..., width:2 * width].reshape(adim, sdim, bdim, idim, pdim, head_count, head_dim).astype(jnp.float32)
    value6 = block[..., 2 * width:].reshape(adim, sdim, bdim, idim, pdim, head_count, head_dim).astype(jnp.float32)
    scores = jnp.einsum('asbiphe,csuiphe->siphabcu', query6, key6) * scaling
    frame_index = jnp.arange(adim, dtype=jnp.int32)[:, None] * bdim + jnp.arange(bdim, dtype=jnp.int32)[None, :]
    frame_gap = jnp.abs(frame_index[:, :, None, None] - frame_index[None, None, :, :])
    allowed = frame_gap[None] <= band_width[:, None, None, None, None]
    scores = jnp.where(allowed, scores, -jnp.inf)
    flat_scores = scores.reshape(sdim, idim, pdim, head_count, adim, bdim, adim * bdim)
    weights = soft_rows(flat_scores).astype(jnp.bfloat16)
    weights = weights.reshape(sdim, idim, pdim, head_count, adim, bdim, adim, bdim).astype(jnp.float32)
    result = jnp.einsum('siphabcu,csuiphe->asbiphe', weights, value6)
    return result.astype(jnp.bfloat16).reshape(adim * sdim * bdim, idim, pdim, width)

def spatial_frame(items, out_weight, temporal_weight):
    latent, query_rows, key_rows, value_rows, cached_out, refreshed = items
    tile_count, tok_count, width = latent.shape
    head_count = HEADS
    head_dim = width // head_count
    scaling = 1.0 / math.sqrt(head_dim)
    zero_edge = jnp.zeros((1, EDGE, width), jnp.bfloat16)
    prev_key = jnp.concatenate([zero_edge, key_rows[:-1, -EDGE:]], axis=0)
    next_key = jnp.concatenate([key_rows[1:, :EDGE], zero_edge], axis=0)
    prev_value = jnp.concatenate([zero_edge, value_rows[:-1, -EDGE:]], axis=0)
    next_value = jnp.concatenate([value_rows[1:, :EDGE], zero_edge], axis=0)
    key_ext = jnp.concatenate([prev_key, key_rows, next_key], axis=1)
    value_ext = jnp.concatenate([prev_value, value_rows, next_value], axis=1)
    span = tok_count + 2 * EDGE
    position = jnp.arange(span, dtype=jnp.int32)
    tile_index = jnp.arange(tile_count, dtype=jnp.int32)[:, None]
    usable = ((position[None, :] >= EDGE) | (tile_index > 0)) & ((position[None, :] < EDGE + tok_count) | (tile_index < tile_count - 1))
    query5 = query_rows.reshape(tile_count, tok_count, head_count, head_dim).astype(jnp.float32)
    key5 = key_ext.reshape(tile_count, span, head_count, head_dim).astype(jnp.float32)
    value5 = value_ext.reshape(tile_count, span, head_count, head_dim).astype(jnp.float32)
    scores = jnp.einsum('tqhe,tkhe->thqk', query5, key5) * scaling
    scores = jnp.where(usable[:, None, None, :], scores, -jnp.inf)
    weights = soft_rows(scores).astype(jnp.bfloat16).astype(jnp.float32)
    fresh = jnp.einsum('thqk,tkhe->tqhe', weights, value5).astype(jnp.bfloat16).reshape(tile_count, tok_count, width)
    spatial = jnp.where(refreshed[:, None, None] == 1, fresh, cached_out)
    projected = jnp.dot(spatial.reshape(-1, width), out_weight, preferred_element_type=jnp.float32)
    hidden = (latent.astype(jnp.float32) + projected.reshape(tile_count, tok_count, width)).astype(jnp.bfloat16)
    hidden32 = hidden.astype(jnp.float32)
    normed = (hidden32 * lax.rsqrt(lax.optimization_barrier(jnp.mean(hidden32 * hidden32, axis=-1, keepdims=True)) + 1e-06)).astype(jnp.bfloat16)
    packed = jnp.dot(normed.reshape(-1, width), temporal_weight, preferred_element_type=jnp.float32).astype(jnp.bfloat16)
    return (hidden, packed.reshape(tile_count, tok_count, 3 * width))

def reference(latent, query_rows, key_rows, value_rows, cached_out, refreshed, band_width, out_weight, temporal_weight):
    width = latent.shape[-1]
    hidden, packed = lax.map(lambda items: spatial_frame(items, out_weight, temporal_weight), (latent, query_rows, key_rows, value_rows, cached_out, refreshed))
    by_tile = jnp.moveaxis(packed, 1, 0)

    def one_tile(block):
        frame_count, tok_count, _ = block.shape
        result = temporal_block(block.reshape(1, 1, frame_count, 1, tok_count, 3 * width), band_width, HEADS, width)
        return result.reshape(frame_count, tok_count, width)
    temporal = jnp.moveaxis(lax.map(one_tile, by_tile), 0, 1)
    return (hidden.astype(jnp.float32) + temporal.astype(jnp.float32)).astype(jnp.bfloat16)
```

```python
import functools
import math

import jax
import jax.numpy as jnp
from jax import lax
from jax.experimental import pallas as pl
from jax.experimental.pallas import tpu as pltpu
from jax.sharding import PartitionSpec as P

EDGE = 64
HEADS = 16


def shifted(block, axis, distance):
    devices = range(lax.axis_size(axis))
    route = [(i - distance, i) for i in devices if i - distance in devices]
    return lax.ppermute(block, axis, route)


def head_window(h, head_dim, width):
    lo = h * head_dim
    start = min((lo // 128) * 128, width - 256)
    return lo, start


def spatial_kernel(flags_ref, q_ref, k_ref, v_ref, kp_ref, kn_ref, vp_ref, vn_ref,
                   lat_ref, cache_ref, wo_ref, hid_ref, nrm_ref, acc_ref, sp_ref):
    i = pl.program_id(0)
    refreshed = flags_ref[i, 0]
    prev_ok = flags_ref[i, 1] == 1
    next_ok = flags_ref[i, 2] == 1
    width = q_ref.shape[-1]
    head_dim = width // HEADS
    scaling = 1.0 / math.sqrt(head_dim)
    nt = (((1,), (1,)), ((), ()))

    @pl.when(refreshed == 1)
    def _():
        acc_ref[...] = jnp.zeros_like(acc_ref)
        for h in range(HEADS):
            lo, start = head_window(h, head_dim, width)
            win = pl.ds(start, 256)
            lane = lax.broadcasted_iota(jnp.int32, (1, 256), 1) + start
            mask = (lane >= lo) & (lane < lo + head_dim)
            qh = jnp.where(mask, q_ref[0, :, win], jnp.zeros((), q_ref.dtype))
            s_mid = lax.dot_general(qh, k_ref[0, :, win], nt,
                                    preferred_element_type=jnp.float32) * scaling
            s_prev = lax.dot_general(qh, kp_ref[0, :, win], nt,
                                     preferred_element_type=jnp.float32) * scaling
            s_next = lax.dot_general(qh, kn_ref[0, :, win], nt,
                                     preferred_element_type=jnp.float32) * scaling
            s_prev = jnp.where(prev_ok, s_prev, -jnp.inf)
            s_next = jnp.where(next_ok, s_next, -jnp.inf)
            top = jnp.maximum(
                jnp.maximum(jnp.max(s_mid, axis=1, keepdims=True),
                            jnp.max(s_prev, axis=1, keepdims=True)),
                jnp.max(s_next, axis=1, keepdims=True))
            e_mid = jnp.exp(s_mid - top)
            e_prev = jnp.exp(s_prev - top)
            e_next = jnp.exp(s_next - top)
            total = (jnp.sum(e_mid, axis=1, keepdims=True)
                     + jnp.sum(e_prev, axis=1, keepdims=True)
                     + jnp.sum(e_next, axis=1, keepdims=True))
            p_mid = (e_mid / total).astype(jnp.bfloat16)
            p_prev = (e_prev / total).astype(jnp.bfloat16)
            p_next = (e_next / total).astype(jnp.bfloat16)
            out = jnp.dot(p_mid, v_ref[0, :, win], preferred_element_type=jnp.float32)
            out = out + jnp.dot(p_prev, vp_ref[0, :, win], preferred_element_type=jnp.float32)
            out = out + jnp.dot(p_next, vn_ref[0, :, win], preferred_element_type=jnp.float32)
            acc_ref[:, win] += jnp.where(mask, out, 0.0)
        sp_ref[...] = acc_ref[...].astype(sp_ref.dtype)

    @pl.when(refreshed != 1)
    def _():
        sp_ref[...] = cache_ref[0]

    projected = jnp.dot(sp_ref[...], wo_ref[...], preferred_element_type=jnp.float32)
    hidden = (lat_ref[0].astype(jnp.float32) + projected).astype(jnp.bfloat16)
    hid_ref[0] = hidden
    h32 = hidden.astype(jnp.float32)
    ms = jnp.mean(h32 * h32, axis=-1, keepdims=True)
    nrm_ref[0] = (h32 * lax.rsqrt(ms + 1e-06)).astype(nrm_ref.dtype)


def spatial_block(flags, q, k, v, kp, kn, vp, vn, lat, cache, wo):
    tiles, tok, width = q.shape
    tile_spec = pl.BlockSpec((1, tok, width), lambda i, f: (i, 0, 0))
    edge_spec = pl.BlockSpec((1, EDGE, width), lambda i, f: (i, 0, 0))
    w_spec = pl.BlockSpec((width, width), lambda i, f: (0, 0))
    out_shape = [jax.ShapeDtypeStruct((tiles, tok, width), jnp.bfloat16)] * 2
    flops = tiles * (HEADS * 4 * tok * (tok + 2 * EDGE) * 256 + 2 * tok * width * width)
    cost = pl.CostEstimate(flops=flops, transcendentals=tiles * HEADS * tok * (tok + 2 * EDGE),
                           bytes_accessed=2 * (7 * tiles * tok * width + width * width))
    return pl.pallas_call(
        spatial_kernel,
        grid_spec=pltpu.PrefetchScalarGridSpec(
            num_scalar_prefetch=1,
            grid=(tiles,),
            in_specs=[tile_spec] * 3 + [edge_spec] * 4 + [tile_spec] * 2 + [w_spec],
            out_specs=[tile_spec, tile_spec],
            scratch_shapes=[pltpu.VMEM((tok, width), jnp.float32),
                            pltpu.VMEM((tok, width), jnp.bfloat16)],
        ),
        out_shape=out_shape,
        compiler_params=pltpu.CompilerParams(dimension_semantics=("arbitrary",),
                                             vmem_limit_bytes=48 * 1024 * 1024),
        cost_estimate=cost,
    )(flags, q, k, v, kp, kn, vp, vn, lat, cache, wo)


def temporal_kernel(bw_ref, q_ref, k_ref, v_ref, ind_ref, indt_ref, o_ref):
    frames, tok, width = q_ref.shape
    head_dim = width // HEADS
    scaling = 1.0 / math.sqrt(head_dim)
    bw = bw_ref[...]
    ind = ind_ref[...]
    indt = indt_ref[...]

    def body(f, carry):
        qf = q_ref[f].astype(jnp.float32)
        scores = []
        for g in range(frames):
            prod = qf * k_ref[g].astype(jnp.float32)
            s = jnp.dot(prod, ind, preferred_element_type=jnp.float32,
                        precision=lax.Precision.HIGHEST) * scaling
            allowed = jnp.abs(f - g) <= bw
            scores.append(jnp.where(allowed, s, -jnp.inf))
        top = scores[0]
        for s in scores[1:]:
            top = jnp.maximum(top, s)
        expo = [jnp.exp(s - top) for s in scores]
        total = expo[0]
        for e in expo[1:]:
            total = total + e
        out = jnp.zeros((tok, width), jnp.float32)
        for g in range(frames):
            p = (expo[g] / total).astype(jnp.bfloat16)
            wide = jnp.dot(p, indt, preferred_element_type=jnp.float32)
            out = out + wide * v_ref[g].astype(jnp.float32)
        o_ref[f] = out.astype(o_ref.dtype)
        return carry

    lax.fori_loop(0, frames, body, 0)


def temporal_attend(packed, band_width):
    frames, tok, wide = packed.shape
    width = wide // 3
    q = packed[..., :width]
    k = packed[..., width:2 * width]
    v = packed[..., 2 * width:]
    head_dim = width // HEADS
    ind = (jnp.arange(width, dtype=jnp.int32)[:, None] // head_dim
           == jnp.arange(HEADS, dtype=jnp.int32)[None, :])
    vspec = pl.BlockSpec(memory_space=pltpu.VMEM)
    cost = pl.CostEstimate(flops=frames * frames * tok * width * 40,
                           transcendentals=frames * frames * tok * HEADS,
                           bytes_accessed=2 * 4 * frames * tok * width)
    return pl.pallas_call(
        temporal_kernel,
        in_specs=[vspec] * 6,
        out_specs=vspec,
        out_shape=jax.ShapeDtypeStruct((frames, tok, width), jnp.bfloat16),
        compiler_params=pltpu.CompilerParams(vmem_limit_bytes=48 * 1024 * 1024),
        cost_estimate=cost,
    )(band_width.reshape(1, HEADS), q, k, v, ind.astype(jnp.float32),
      ind.T.astype(jnp.bfloat16))


def local(latent, query_rows, key_rows, value_rows, cached_out, refreshed, band_width,
          out_weight, temporal_weight):
    _, tile_count, tok_count, width = latent.shape
    lat = latent[0]
    q = query_rows[0]
    k = key_rows[0]
    v = value_rows[0]
    cache = cached_out[0]
    last_edges = jnp.stack([k[-1, -EDGE:], v[-1, -EDGE:]])
    first_edges = jnp.stack([k[0, :EDGE], v[0, :EDGE]])
    from_above = shifted(last_edges, "space", 1)
    from_below = shifted(first_edges, "space", -1)
    kp = jnp.concatenate([from_above[0][None], k[:-1, -EDGE:]], axis=0)
    vp = jnp.concatenate([from_above[1][None], v[:-1, -EDGE:]], axis=0)
    kn = jnp.concatenate([k[1:, :EDGE], from_below[0][None]], axis=0)
    vn = jnp.concatenate([v[1:, :EDGE], from_below[1][None]], axis=0)
    total_tiles = tile_count * lax.axis_size("space")
    tile_index = lax.axis_index("space") * tile_count + jnp.arange(tile_count, dtype=jnp.int32)
    flags = jnp.stack([refreshed[0].astype(jnp.int32),
                       (tile_index > 0).astype(jnp.int32),
                       (tile_index < total_tiles - 1).astype(jnp.int32)], axis=1)
    hidden, normed = spatial_block(flags, q, k, v, kp, kn, vp, vn, lat, cache, out_weight)

    frame_groups = lax.axis_size("frames")
    block = lax.all_to_all(normed[None], "frames", split_axis=2, concat_axis=0, tiled=True)
    rows = block.shape[1] * block.shape[2]
    flat = jnp.dot(block.reshape(-1, width), temporal_weight,
                   preferred_element_type=jnp.float32).astype(jnp.bfloat16)
    packed = flat.reshape(frame_groups, rows, 3 * width)
    attended = temporal_attend(packed, band_width)
    attended = attended.reshape(frame_groups, tile_count, -1, width)
    temporal = lax.all_to_all(attended, "frames", split_axis=0, concat_axis=2, tiled=True)
    mixed = (hidden.astype(jnp.float32) + temporal[0].astype(jnp.float32)).astype(jnp.bfloat16)
    return mixed[None]


def solution(mesh):
    return jax.shard_map(
        local,
        mesh=mesh,
        in_specs=(
            P("frames", "space", None, None),
            P("frames", "space", None, None),
            P("frames", "space", None, None),
            P("frames", "space", None, None),
            P("frames", "space", None, None),
            P("frames", "space"),
            P(),
            P(),
            P(),
        ),
        out_specs=P("frames", "space", None, None),
        check_vma=False,
    )
```

```python
import functools
import math

import jax
import jax.numpy as jnp
from jax import lax
from jax.experimental import pallas as pl
from jax.experimental.pallas import tpu as pltpu
from jax.sharding import PartitionSpec as P

EDGE = 64
HEADS = 16


def shifted(block, axis, distance):
    devices = range(lax.axis_size(axis))
    route = [(i - distance, i) for i in devices if i - distance in devices]
    return lax.ppermute(block, axis, route)


def head_window(h, head_dim, width):
    lo = h * head_dim
    start = min((lo // 128) * 128, width - 256)
    return lo, start


def spatial_kernel(flags_ref, q_ref, k_ref, v_ref, kp_ref, kn_ref, vp_ref, vn_ref,
                   lat_ref, cache_ref, wo_ref, hid_ref, nrm_ref, acc_ref, sp_ref):
    i = pl.program_id(0)
    refreshed = flags_ref[i, 0]
    prev_ok = flags_ref[i, 1] == 1
    next_ok = flags_ref[i, 2] == 1
    width = q_ref.shape[-1]
    head_dim = width // HEADS
    scaling = 1.0 / math.sqrt(head_dim)
    nt = (((1,), (1,)), ((), ()))

    @pl.when(refreshed == 1)
    def _():
        acc_ref[...] = jnp.zeros_like(acc_ref)
        for h in range(HEADS):
            lo, start = head_window(h, head_dim, width)
            win = pl.ds(start, 256)
            lane = lax.broadcasted_iota(jnp.int32, (1, 256), 1) + start
            mask = (lane >= lo) & (lane < lo + head_dim)
            qh = jnp.where(mask, q_ref[0, :, win], jnp.zeros((), q_ref.dtype))
            s_mid = lax.dot_general(qh, k_ref[0, :, win], nt,
                                    preferred_element_type=jnp.float32) * scaling
            s_prev = lax.dot_general(qh, kp_ref[0, :, win], nt,
                                     preferred_element_type=jnp.float32) * scaling
            s_next = lax.dot_general(qh, kn_ref[0, :, win], nt,
                                     preferred_element_type=jnp.float32) * scaling
            s_prev = jnp.where(prev_ok, s_prev, -jnp.inf)
            s_next = jnp.where(next_ok, s_next, -jnp.inf)
            top = jnp.maximum(
                jnp.maximum(jnp.max(s_mid, axis=1, keepdims=True),
                            jnp.max(s_prev, axis=1, keepdims=True)),
                jnp.max(s_next, axis=1, keepdims=True))
            e_mid = jnp.exp(s_mid - top)
            e_prev = jnp.exp(s_prev - top)
            e_next = jnp.exp(s_next - top)
            total = (jnp.sum(e_mid, axis=1, keepdims=True)
                     + jnp.sum(e_prev, axis=1, keepdims=True)
                     + jnp.sum(e_next, axis=1, keepdims=True))
            p_mid = (e_mid / total).astype(jnp.bfloat16)
            p_prev = (e_prev / total).astype(jnp.bfloat16)
            p_next = (e_next / total).astype(jnp.bfloat16)
            out = jnp.dot(p_mid, v_ref[0, :, win], preferred_element_type=jnp.float32)
            out = out + jnp.dot(p_prev, vp_ref[0, :, win], preferred_element_type=jnp.float32)
            out = out + jnp.dot(p_next, vn_ref[0, :, win], preferred_element_type=jnp.float32)
            acc_ref[:, win] += jnp.where(mask, out, 0.0)
        sp_ref[...] = acc_ref[...].astype(sp_ref.dtype)

    @pl.when(refreshed != 1)
    def _():
        sp_ref[...] = cache_ref[0]

    projected = jnp.dot(sp_ref[...], wo_ref[...], preferred_element_type=jnp.float32)
    hidden = (lat_ref[0].astype(jnp.float32) + projected).astype(jnp.bfloat16)
    hid_ref[0] = hidden
    h32 = hidden.astype(jnp.float32)
    ms = jnp.mean(h32 * h32, axis=-1, keepdims=True)
    nrm_ref[0] = (h32 * lax.rsqrt(ms + 1e-06)).astype(nrm_ref.dtype)


def spatial_block(flags, q, k, v, kp, kn, vp, vn, lat, cache, wo):
    tiles, tok, width = q.shape
    tile_spec = pl.BlockSpec((1, tok, width), lambda i, f: (i, 0, 0))
    edge_spec = pl.BlockSpec((1, EDGE, width), lambda i, f: (i, 0, 0))
    w_spec = pl.BlockSpec((width, width), lambda i, f: (0, 0))
    out_shape = [jax.ShapeDtypeStruct((tiles, tok, width), jnp.bfloat16)] * 2
    flops = tiles * (HEADS * 4 * tok * (tok + 2 * EDGE) * 256 + 2 * tok * width * width)
    cost = pl.CostEstimate(flops=flops, transcendentals=tiles * HEADS * tok * (tok + 2 * EDGE),
                           bytes_accessed=2 * (7 * tiles * tok * width + width * width))
    return pl.pallas_call(
        spatial_kernel,
        grid_spec=pltpu.PrefetchScalarGridSpec(
            num_scalar_prefetch=1,
            grid=(tiles,),
            in_specs=[tile_spec] * 3 + [edge_spec] * 4 + [tile_spec] * 2 + [w_spec],
            out_specs=[tile_spec, tile_spec],
            scratch_shapes=[pltpu.VMEM((tok, width), jnp.float32),
                            pltpu.VMEM((tok, width), jnp.bfloat16)],
        ),
        out_shape=out_shape,
        compiler_params=pltpu.CompilerParams(dimension_semantics=("arbitrary",),
                                             vmem_limit_bytes=48 * 1024 * 1024),
        cost_estimate=cost,
    )(flags, q, k, v, kp, kn, vp, vn, lat, cache, wo)


def temporal_kernel(fid_ref, bw_ref, q_ref, k_ref, v_ref, ind_ref, indt_ref, o_ref):
    frames, tok, width = q_ref.shape
    head_dim = width // HEADS
    scaling = 1.0 / math.sqrt(head_dim)
    bw = bw_ref[...].reshape(1, 1, HEADS)
    ind = ind_ref[...]
    indt = indt_ref[...]
    fids = jnp.concatenate(
        [jnp.full((1, 1, 1), fid_ref[g], jnp.int32) for g in range(frames)], axis=0)

    def body(f, carry):
        qf = q_ref[f].astype(jnp.float32)
        prod = (qf[None] * k_ref[...].astype(jnp.float32)).reshape(frames * tok, width)
        hi = prod.astype(jnp.bfloat16)
        lo = (prod - hi.astype(jnp.float32)).astype(jnp.bfloat16)
        s = (jnp.dot(hi, ind, preferred_element_type=jnp.float32)
             + jnp.dot(lo, ind, preferred_element_type=jnp.float32))
        s = s.reshape(frames, tok, HEADS) * scaling
        allowed = jnp.abs(fids - fid_ref[f]) <= bw
        s = jnp.where(allowed, s, -jnp.inf)
        top = jnp.max(s, axis=0, keepdims=True)
        expo = jnp.exp(s - top)
        total = jnp.sum(expo, axis=0, keepdims=True)
        p = (expo / total).astype(jnp.bfloat16).reshape(frames * tok, HEADS)
        wide = jnp.dot(p, indt, preferred_element_type=jnp.float32).reshape(frames, tok, width)
        out = jnp.sum(wide * v_ref[...].astype(jnp.float32), axis=0)
        o_ref[f] = out.astype(o_ref.dtype)
        return carry

    lax.fori_loop(0, frames, body, 0)


def temporal_attend(packed, band_width, fids):
    frames, tok, wide = packed.shape
    width = wide // 3
    q = packed[..., :width]
    k = packed[..., width:2 * width]
    v = packed[..., 2 * width:]
    head_dim = width // HEADS
    ind = (jnp.arange(width, dtype=jnp.int32)[:, None] // head_dim
           == jnp.arange(HEADS, dtype=jnp.int32)[None, :])
    vspec = pl.BlockSpec(memory_space=pltpu.VMEM)
    sspec = pl.BlockSpec(memory_space=pltpu.SMEM)
    cost = pl.CostEstimate(flops=frames * frames * tok * width * 40,
                           transcendentals=frames * frames * tok * HEADS,
                           bytes_accessed=2 * 4 * frames * tok * width)
    return pl.pallas_call(
        temporal_kernel,
        in_specs=[sspec] + [vspec] * 6,
        out_specs=vspec,
        out_shape=jax.ShapeDtypeStruct((frames, tok, width), jnp.bfloat16),
        compiler_params=pltpu.CompilerParams(vmem_limit_bytes=48 * 1024 * 1024),
        cost_estimate=cost,
    )(fids, band_width.reshape(1, HEADS), q, k, v, ind.astype(jnp.bfloat16),
      ind.T.astype(jnp.bfloat16))


OFFSETS = ((0, 1), (-1, 0), (-1, 1), (1, 0), (1, 1), (2, 0), (2, 1))


def frame_dest(d, dy, dc, chips):
    return ((d // 2 + dy) % chips) * 2 + ((d % 2) ^ dc)


def frame_perm(dy, dc, n):
    chips = n // 2
    return [(d, frame_dest(d, dy, dc, chips)) for d in range(n)]


def exchange(send, n):
    recv = {}
    recv[(0, 1)] = lax.ppermute(send[(0, 1)], "frames", frame_perm(0, 1, n))
    for dc in (0, 1):
        recv[(-1, dc)] = lax.ppermute(send[(1, dc)], "frames", frame_perm(1, dc, n))
        recv[(1, dc)] = lax.ppermute(send[(-1, dc)], "frames", frame_perm(-1, dc, n))
    hop = lax.ppermute(send[(2, 0)], "frames", frame_perm(1, 0, n))
    recv[(2, 0)] = lax.ppermute(hop, "frames", frame_perm(1, 0, n))
    hop = lax.ppermute(send[(2, 1)], "frames", frame_perm(-1, 0, n))
    recv[(2, 1)] = lax.ppermute(hop, "frames", frame_perm(-1, 1, n))
    return recv


def local(latent, query_rows, key_rows, value_rows, cached_out, refreshed, band_width,
          out_weight, temporal_weight):
    _, tile_count, tok_count, width = latent.shape
    lat = latent[0]
    q = query_rows[0]
    k = key_rows[0]
    v = value_rows[0]
    cache = cached_out[0]
    last_edges = jnp.stack([k[-1, -EDGE:], v[-1, -EDGE:]])
    first_edges = jnp.stack([k[0, :EDGE], v[0, :EDGE]])
    from_above = shifted(last_edges, "space", 1)
    from_below = shifted(first_edges, "space", -1)
    kp = jnp.concatenate([from_above[0][None], k[:-1, -EDGE:]], axis=0)
    vp = jnp.concatenate([from_above[1][None], v[:-1, -EDGE:]], axis=0)
    kn = jnp.concatenate([k[1:, :EDGE], from_below[0][None]], axis=0)
    vn = jnp.concatenate([v[1:, :EDGE], from_below[1][None]], axis=0)
    total_tiles = tile_count * lax.axis_size("space")
    tile_index = lax.axis_index("space") * tile_count + jnp.arange(tile_count, dtype=jnp.int32)
    flags = jnp.stack([refreshed[0].astype(jnp.int32),
                       (tile_index > 0).astype(jnp.int32),
                       (tile_index < total_tiles - 1).astype(jnp.int32)], axis=1)
    hidden, normed = spatial_block(flags, q, k, v, kp, kn, vp, vn, lat, cache, out_weight)

    n = lax.axis_size("frames")
    chips = n // 2
    chunk = tok_count // n
    me = lax.axis_index("frames")
    dests = {o: frame_dest(me, o[0], o[1], chips) for o in OFFSETS}
    send = {o: lax.dynamic_slice_in_dim(normed, dests[o] * chunk, chunk, axis=1) for o in OFFSETS}
    recv = exchange(send, n)
    own = lax.dynamic_slice_in_dim(normed, me * chunk, chunk, axis=1)
    block = jnp.stack([own] + [recv[o] for o in OFFSETS])
    fids = jnp.stack([me] + [dests[o] for o in OFFSETS]).astype(jnp.int32)
    rows = tile_count * chunk
    flat = jnp.dot(block.reshape(-1, width), temporal_weight,
                   preferred_element_type=jnp.float32).astype(jnp.bfloat16)
    packed = flat.reshape(n, rows, 3 * width)
    attended = temporal_attend(packed, band_width, fids)
    attended = attended.reshape(n, tile_count, chunk, width)
    back = exchange({o: attended[1 + i] for i, o in enumerate(OFFSETS)}, n)
    temporal = lax.dynamic_update_slice_in_dim(
        jnp.zeros_like(hidden), attended[0], me * chunk, axis=1)
    for o in OFFSETS:
        temporal = lax.dynamic_update_slice_in_dim(temporal, back[o], dests[o] * chunk, axis=1)
    mixed = (hidden.astype(jnp.float32) + temporal.astype(jnp.float32)).astype(jnp.bfloat16)
    return mixed[None]


def solution(mesh):
    return jax.shard_map(
        local,
        mesh=mesh,
        in_specs=(
            P("frames", "space", None, None),
            P("frames", "space", None, None),
            P("frames", "space", None, None),
            P("frames", "space", None, None),
            P("frames", "space", None, None),
            P("frames", "space"),
            P(),
            P(),
            P(),
        ),
        out_specs=P("frames", "space", None, None),
        check_vma=False,
    )
```

```python
import functools
import math

import jax
import jax.numpy as jnp
from jax import lax
from jax.experimental import pallas as pl
from jax.experimental.pallas import tpu as pltpu
from jax.sharding import PartitionSpec as P

EDGE = 64
HEADS = 16


def shifted(block, axis, distance):
    devices = range(lax.axis_size(axis))
    route = [(i - distance, i) for i in devices if i - distance in devices]
    return lax.ppermute(block, axis, route)


def head_window(h, head_dim, width):
    lo = h * head_dim
    start = min((lo // 128) * 128, width - 256)
    return lo, start


def spatial_kernel(flags_ref, q_ref, k_ref, v_ref, ke_ref, ve_ref,
                   lat_ref, cache_ref, wo_ref, hid_ref, nrm_ref, acc_ref, sp_ref):
    i = pl.program_id(0)
    refreshed = flags_ref[i, 0]
    prev_ok = flags_ref[i, 1]
    next_ok = flags_ref[i, 2]
    width = q_ref.shape[-1]
    head_dim = width // HEADS
    scaling = 1.0 / math.sqrt(head_dim)
    nt = (((1,), (1,)), ((), ()))

    @pl.when(refreshed == 1)
    def _():
        acc_ref[...] = jnp.zeros_like(acc_ref)
        edge_lane = lax.broadcasted_iota(jnp.int32, (1, 2 * EDGE), 1)
        edge_ok = jnp.where(edge_lane < EDGE, prev_ok, next_ok) == 1
        for h in range(HEADS):
            lo, start = head_window(h, head_dim, width)
            win = pl.ds(start, 256)
            lane = lax.broadcasted_iota(jnp.int32, (1, 256), 1) + start
            mask = (lane >= lo) & (lane < lo + head_dim)
            qh = jnp.where(mask, q_ref[0, :, win], jnp.zeros((), q_ref.dtype))
            s_mid = lax.dot_general(qh, k_ref[0, :, win], nt,
                                    preferred_element_type=jnp.float32) * scaling
            s_edge = lax.dot_general(qh, ke_ref[0, :, win], nt,
                                     preferred_element_type=jnp.float32) * scaling
            s_edge = jnp.where(edge_ok, s_edge, -jnp.inf)
            top = jnp.maximum(jnp.max(s_mid, axis=1, keepdims=True),
                              jnp.max(s_edge, axis=1, keepdims=True))
            e_mid = jnp.exp(s_mid - top)
            e_edge = jnp.exp(s_edge - top)
            total = (jnp.sum(e_mid, axis=1, keepdims=True)
                     + jnp.sum(e_edge, axis=1, keepdims=True))
            inv = 1.0 / total
            p_mid = (e_mid * inv).astype(jnp.bfloat16)
            p_edge = (e_edge * inv).astype(jnp.bfloat16)
            out = jnp.dot(p_mid, v_ref[0, :, win], preferred_element_type=jnp.float32)
            out = out + jnp.dot(p_edge, ve_ref[0, :, win], preferred_element_type=jnp.float32)
            acc_ref[:, win] += jnp.where(mask, out, 0.0)
        sp_ref[...] = acc_ref[...].astype(sp_ref.dtype)

    @pl.when(refreshed != 1)
    def _():
        sp_ref[...] = cache_ref[0]

    projected = jnp.dot(sp_ref[...], wo_ref[...], preferred_element_type=jnp.float32)
    hidden = (lat_ref[0].astype(jnp.float32) + projected).astype(jnp.bfloat16)
    hid_ref[0] = hidden
    h32 = hidden.astype(jnp.float32)
    ms = jnp.mean(h32 * h32, axis=-1, keepdims=True)
    nrm_ref[0] = (h32 * lax.rsqrt(ms + 1e-06)).astype(nrm_ref.dtype)


def spatial_block(flags, q, k, v, ke, ve, lat, cache, wo):
    tiles, tok, width = q.shape
    tile_spec = pl.BlockSpec((1, tok, width), lambda i, f: (i, 0, 0))
    edge_spec = pl.BlockSpec((1, 2 * EDGE, width), lambda i, f: (i, 0, 0))
    w_spec = pl.BlockSpec((width, width), lambda i, f: (0, 0))
    out_shape = [jax.ShapeDtypeStruct((tiles, tok, width), jnp.bfloat16)] * 2
    flops = tiles * (HEADS * 4 * tok * (tok + 2 * EDGE) * 256 + 2 * tok * width * width)
    cost = pl.CostEstimate(flops=flops, transcendentals=tiles * HEADS * tok * (tok + 2 * EDGE),
                           bytes_accessed=2 * (7 * tiles * tok * width + width * width))
    return pl.pallas_call(
        spatial_kernel,
        grid_spec=pltpu.PrefetchScalarGridSpec(
            num_scalar_prefetch=1,
            grid=(tiles,),
            in_specs=[tile_spec] * 3 + [edge_spec] * 2 + [tile_spec] * 2 + [w_spec],
            out_specs=[tile_spec, tile_spec],
            scratch_shapes=[pltpu.VMEM((tok, width), jnp.float32),
                            pltpu.VMEM((tok, width), jnp.bfloat16)],
        ),
        out_shape=out_shape,
        compiler_params=pltpu.CompilerParams(dimension_semantics=("arbitrary",),
                                             vmem_limit_bytes=48 * 1024 * 1024),
        cost_estimate=cost,
    )(flags, q, k, v, ke, ve, lat, cache, wo)


def temporal_kernel(fid_ref, bw_ref, q_ref, k_ref, v_ref, ind_ref, indt_ref, o_ref):
    frames, tok, width = q_ref.shape
    head_dim = width // HEADS
    scaling = 1.0 / math.sqrt(head_dim)
    bw = bw_ref[...].reshape(1, 1, HEADS)
    ind = ind_ref[...]
    indt = indt_ref[...]
    fids = jnp.concatenate(
        [jnp.full((1, 1, 1), fid_ref[g], jnp.int32) for g in range(frames)], axis=0)

    def body(f, carry):
        qf = q_ref[f].astype(jnp.float32)
        prod = (qf[None] * k_ref[...].astype(jnp.float32)).reshape(frames * tok, width)
        hi = prod.astype(jnp.bfloat16)
        lo = (prod - hi.astype(jnp.float32)).astype(jnp.bfloat16)
        s = (jnp.dot(hi, ind, preferred_element_type=jnp.float32)
             + jnp.dot(lo, ind, preferred_element_type=jnp.float32))
        s = s.reshape(frames, tok, HEADS) * scaling
        allowed = jnp.abs(fids - fid_ref[f]) <= bw
        s = jnp.where(allowed, s, -jnp.inf)
        top = jnp.max(s, axis=0, keepdims=True)
        expo = jnp.exp(s - top)
        total = jnp.sum(expo, axis=0, keepdims=True)
        p = (expo / total).astype(jnp.bfloat16).reshape(frames * tok, HEADS)
        wide = jnp.dot(p, indt, preferred_element_type=jnp.float32).reshape(frames, tok, width)
        out = jnp.sum(wide * v_ref[...].astype(jnp.float32), axis=0)
        o_ref[f] = out.astype(o_ref.dtype)
        return carry

    lax.fori_loop(0, frames, body, 0)


def temporal_attend(packed, band_width, fids):
    frames, tok, wide = packed.shape
    width = wide // 3
    q = packed[..., :width]
    k = packed[..., width:2 * width]
    v = packed[..., 2 * width:]
    head_dim = width // HEADS
    ind = (jnp.arange(width, dtype=jnp.int32)[:, None] // head_dim
           == jnp.arange(HEADS, dtype=jnp.int32)[None, :])
    vspec = pl.BlockSpec(memory_space=pltpu.VMEM)
    sspec = pl.BlockSpec(memory_space=pltpu.SMEM)
    cost = pl.CostEstimate(flops=frames * frames * tok * width * 40,
                           transcendentals=frames * frames * tok * HEADS,
                           bytes_accessed=2 * 4 * frames * tok * width)
    return pl.pallas_call(
        temporal_kernel,
        in_specs=[sspec] + [vspec] * 6,
        out_specs=vspec,
        out_shape=jax.ShapeDtypeStruct((frames, tok, width), jnp.bfloat16),
        compiler_params=pltpu.CompilerParams(vmem_limit_bytes=48 * 1024 * 1024),
        cost_estimate=cost,
    )(fids, band_width.reshape(1, HEADS), q, k, v, ind.astype(jnp.bfloat16),
      ind.T.astype(jnp.bfloat16))


OFFSETS = ((0, 1), (-1, 0), (-1, 1), (1, 0), (1, 1), (2, 0), (2, 1))


def frame_dest(d, dy, dc, chips):
    return ((d // 2 + dy) % chips) * 2 + ((d % 2) ^ dc)


def frame_perm(dy, dc, n):
    chips = n // 2
    return [(d, frame_dest(d, dy, dc, chips)) for d in range(n)]


def exchange(send, n):
    recv = {}
    recv[(0, 1)] = lax.ppermute(send[(0, 1)], "frames", frame_perm(0, 1, n))
    for dc in (0, 1):
        recv[(-1, dc)] = lax.ppermute(send[(1, dc)], "frames", frame_perm(1, dc, n))
        recv[(1, dc)] = lax.ppermute(send[(-1, dc)], "frames", frame_perm(-1, dc, n))
    hop = lax.ppermute(send[(2, 0)], "frames", frame_perm(1, 0, n))
    recv[(2, 0)] = lax.ppermute(hop, "frames", frame_perm(1, 0, n))
    hop = lax.ppermute(send[(2, 1)], "frames", frame_perm(-1, 0, n))
    recv[(2, 1)] = lax.ppermute(hop, "frames", frame_perm(-1, 1, n))
    return recv


def local(latent, query_rows, key_rows, value_rows, cached_out, refreshed, band_width,
          out_weight, temporal_weight):
    _, tile_count, tok_count, width = latent.shape
    lat = latent[0]
    q = query_rows[0]
    k = key_rows[0]
    v = value_rows[0]
    cache = cached_out[0]
    last_edges = jnp.stack([k[-1, -EDGE:], v[-1, -EDGE:]])
    first_edges = jnp.stack([k[0, :EDGE], v[0, :EDGE]])
    from_above = shifted(last_edges, "space", 1)
    from_below = shifted(first_edges, "space", -1)
    kp = jnp.concatenate([from_above[0][None], k[:-1, -EDGE:]], axis=0)
    vp = jnp.concatenate([from_above[1][None], v[:-1, -EDGE:]], axis=0)
    kn = jnp.concatenate([k[1:, :EDGE], from_below[0][None]], axis=0)
    vn = jnp.concatenate([v[1:, :EDGE], from_below[1][None]], axis=0)
    total_tiles = tile_count * lax.axis_size("space")
    tile_index = lax.axis_index("space") * tile_count + jnp.arange(tile_count, dtype=jnp.int32)
    flags = jnp.stack([refreshed[0].astype(jnp.int32),
                       (tile_index > 0).astype(jnp.int32),
                       (tile_index < total_tiles - 1).astype(jnp.int32)], axis=1)
    ke = jnp.concatenate([kp, kn], axis=1)
    ve = jnp.concatenate([vp, vn], axis=1)
    hidden, normed = spatial_block(flags, q, k, v, ke, ve, lat, cache, out_weight)

    n = lax.axis_size("frames")
    chips = n // 2
    chunk = tok_count // n
    me = lax.axis_index("frames")
    dests = {o: frame_dest(me, o[0], o[1], chips) for o in OFFSETS}
    send = {o: lax.dynamic_slice_in_dim(normed, dests[o] * chunk, chunk, axis=1) for o in OFFSETS}
    recv = exchange(send, n)
    own = lax.dynamic_slice_in_dim(normed, me * chunk, chunk, axis=1)
    block = jnp.stack([own] + [recv[o] for o in OFFSETS])
    fids = jnp.stack([me] + [dests[o] for o in OFFSETS]).astype(jnp.int32)
    rows = tile_count * chunk
    flat = jnp.dot(block.reshape(-1, width), temporal_weight,
                   preferred_element_type=jnp.float32).astype(jnp.bfloat16)
    packed = flat.reshape(n, rows, 3 * width)
    attended = temporal_attend(packed, band_width, fids)
    attended = attended.reshape(n, tile_count, chunk, width)
    back = exchange({o: attended[1 + i] for i, o in enumerate(OFFSETS)}, n)
    temporal = lax.dynamic_update_slice_in_dim(
        jnp.zeros_like(hidden), attended[0], me * chunk, axis=1)
    for o in OFFSETS:
        temporal = lax.dynamic_update_slice_in_dim(temporal, back[o], dests[o] * chunk, axis=1)
    mixed = (hidden.astype(jnp.float32) + temporal.astype(jnp.float32)).astype(jnp.bfloat16)
    return mixed[None]


def solution(mesh):
    return jax.shard_map(
        local,
        mesh=mesh,
        in_specs=(
            P("frames", "space", None, None),
            P("frames", "space", None, None),
            P("frames", "space", None, None),
            P("frames", "space", None, None),
            P("frames", "space", None, None),
            P("frames", "space"),
            P(),
            P(),
            P(),
        ),
        out_specs=P("frames", "space", None, None),
        check_vma=False,
    )
```

```python
import functools
import math

import jax
import jax.numpy as jnp
from jax import lax
from jax.experimental import pallas as pl
from jax.experimental.pallas import tpu as pltpu
from jax.sharding import PartitionSpec as P

EDGE = 64
HEADS = 16


def shifted(block, axis, distance):
    devices = range(lax.axis_size(axis))
    route = [(i - distance, i) for i in devices if i - distance in devices]
    return lax.ppermute(block, axis, route)


def head_window(h, head_dim, width):
    lo = h * head_dim
    start = min((lo // 128) * 128, width - 256)
    return lo, start


def spatial_kernel(flags_ref, q_ref, k_ref, v_ref, ke_ref, ve_ref,
                   lat_ref, cache_ref, wo_ref, hid_ref, nrm_ref, acc_ref, sp_ref):
    i = pl.program_id(0)
    refreshed = flags_ref[i, 0]
    prev_ok = flags_ref[i, 1]
    next_ok = flags_ref[i, 2]
    width = q_ref.shape[-1]
    head_dim = width // HEADS
    scaling = 1.0 / math.sqrt(head_dim)
    nt = (((1,), (1,)), ((), ()))

    @pl.when(refreshed == 1)
    def _():
        acc_ref[...] = jnp.zeros_like(acc_ref)
        edge_lane = lax.broadcasted_iota(jnp.int32, (1, 2 * EDGE), 1)
        edge_ok = jnp.where(edge_lane < EDGE, prev_ok, next_ok) == 1
        for h in range(HEADS):
            lo, start = head_window(h, head_dim, width)
            win = pl.ds(start, 256)
            lane = lax.broadcasted_iota(jnp.int32, (1, 256), 1) + start
            mask = (lane >= lo) & (lane < lo + head_dim)
            qh = jnp.where(mask, q_ref[0, :, win], jnp.zeros((), q_ref.dtype))
            s_mid = lax.dot_general(qh, k_ref[0, :, win], nt,
                                    preferred_element_type=jnp.float32) * scaling
            s_edge = lax.dot_general(qh, ke_ref[0, :, win], nt,
                                     preferred_element_type=jnp.float32) * scaling
            s_edge = jnp.where(edge_ok, s_edge, -jnp.inf)
            top = jnp.maximum(jnp.max(s_mid, axis=1, keepdims=True),
                              jnp.max(s_edge, axis=1, keepdims=True))
            e_mid = jnp.exp(s_mid - top)
            e_edge = jnp.exp(s_edge - top)
            total = (jnp.sum(e_mid, axis=1, keepdims=True)
                     + jnp.sum(e_edge, axis=1, keepdims=True))
            inv = 1.0 / total
            p_mid = (e_mid * inv).astype(jnp.bfloat16)
            p_edge = (e_edge * inv).astype(jnp.bfloat16)
            out = jnp.dot(p_mid, v_ref[0, :, win], preferred_element_type=jnp.float32)
            out = out + jnp.dot(p_edge, ve_ref[0, :, win], preferred_element_type=jnp.float32)
            acc_ref[:, win] += jnp.where(mask, out, 0.0)
        sp_ref[...] = acc_ref[...].astype(sp_ref.dtype)

    @pl.when(refreshed != 1)
    def _():
        sp_ref[...] = cache_ref[0]

    projected = jnp.dot(sp_ref[...], wo_ref[...], preferred_element_type=jnp.float32)
    hidden = (lat_ref[0].astype(jnp.float32) + projected).astype(jnp.bfloat16)
    hid_ref[0] = hidden
    h32 = hidden.astype(jnp.float32)
    ms = jnp.mean(h32 * h32, axis=-1, keepdims=True)
    nrm_ref[0] = (h32 * lax.rsqrt(ms + 1e-06)).astype(nrm_ref.dtype)


def spatial_block(flags, q, k, v, ke, ve, lat, cache, wo):
    tiles, tok, width = q.shape
    tile_spec = pl.BlockSpec((1, tok, width), lambda i, f: (i, 0, 0))
    edge_spec = pl.BlockSpec((1, 2 * EDGE, width), lambda i, f: (i, 0, 0))
    w_spec = pl.BlockSpec((width, width), lambda i, f: (0, 0))
    out_shape = [jax.ShapeDtypeStruct((tiles, tok, width), jnp.bfloat16)] * 2
    flops = tiles * (HEADS * 4 * tok * (tok + 2 * EDGE) * 256 + 2 * tok * width * width)
    cost = pl.CostEstimate(flops=flops, transcendentals=tiles * HEADS * tok * (tok + 2 * EDGE),
                           bytes_accessed=2 * (7 * tiles * tok * width + width * width))
    return pl.pallas_call(
        spatial_kernel,
        grid_spec=pltpu.PrefetchScalarGridSpec(
            num_scalar_prefetch=1,
            grid=(tiles,),
            in_specs=[tile_spec] * 3 + [edge_spec] * 2 + [tile_spec] * 2 + [w_spec],
            out_specs=[tile_spec, tile_spec],
            scratch_shapes=[pltpu.VMEM((tok, width), jnp.float32),
                            pltpu.VMEM((tok, width), jnp.bfloat16)],
        ),
        out_shape=out_shape,
        compiler_params=pltpu.CompilerParams(dimension_semantics=("arbitrary",),
                                             vmem_limit_bytes=48 * 1024 * 1024),
        cost_estimate=cost,
    )(flags, q, k, v, ke, ve, lat, cache, wo)


def temporal_kernel(fid_ref, bw_ref, q_ref, k_ref, v_ref, ind_ref, indt_ref, o_ref):
    frames, tok, width = q_ref.shape
    head_dim = width // HEADS
    scaling = 1.0 / math.sqrt(head_dim)
    bw = bw_ref[...].reshape(1, 1, HEADS)
    ind = ind_ref[...]
    indt = indt_ref[...]
    fids = jnp.concatenate(
        [jnp.full((1, 1, 1), fid_ref[g], jnp.int32) for g in range(frames)], axis=0)

    def body(f, carry):
        qf = q_ref[f].astype(jnp.float32)
        prod = (qf[None] * k_ref[...].astype(jnp.float32)).reshape(frames * tok, width)
        hi = prod.astype(jnp.bfloat16)
        lo = (prod - hi.astype(jnp.float32)).astype(jnp.bfloat16)
        s = (jnp.dot(hi, ind, preferred_element_type=jnp.float32)
             + jnp.dot(lo, ind, preferred_element_type=jnp.float32))
        s = s.reshape(frames, tok, HEADS) * scaling
        allowed = jnp.abs(fids - fid_ref[f]) <= bw
        s = jnp.where(allowed, s, -jnp.inf)
        top = jnp.max(s, axis=0, keepdims=True)
        expo = jnp.exp(s - top)
        total = jnp.sum(expo, axis=0, keepdims=True)
        p = (expo / total).astype(jnp.bfloat16).reshape(frames * tok, HEADS)
        wide = jnp.dot(p, indt, preferred_element_type=jnp.float32).reshape(frames, tok, width)
        out = jnp.sum(wide * v_ref[...].astype(jnp.float32), axis=0)
        o_ref[f] = out.astype(o_ref.dtype)
        return carry

    lax.fori_loop(0, frames, body, 0)


def temporal_attend(packed, band_width, fids):
    frames, tok, wide = packed.shape
    width = wide // 3
    q = packed[..., :width]
    k = packed[..., width:2 * width]
    v = packed[..., 2 * width:]
    head_dim = width // HEADS
    ind = (jnp.arange(width, dtype=jnp.int32)[:, None] // head_dim
           == jnp.arange(HEADS, dtype=jnp.int32)[None, :])
    vspec = pl.BlockSpec(memory_space=pltpu.VMEM)
    sspec = pl.BlockSpec(memory_space=pltpu.SMEM)
    cost = pl.CostEstimate(flops=frames * frames * tok * width * 40,
                           transcendentals=frames * frames * tok * HEADS,
                           bytes_accessed=2 * 4 * frames * tok * width)
    return pl.pallas_call(
        temporal_kernel,
        in_specs=[sspec] + [vspec] * 6,
        out_specs=vspec,
        out_shape=jax.ShapeDtypeStruct((frames, tok, width), jnp.bfloat16),
        compiler_params=pltpu.CompilerParams(vmem_limit_bytes=48 * 1024 * 1024),
        cost_estimate=cost,
    )(fids, band_width.reshape(1, HEADS), q, k, v, ind.astype(jnp.bfloat16),
      ind.T.astype(jnp.bfloat16))


OFFSETS = ((0, 1), (-1, 0), (-1, 1), (1, 0), (1, 1), (2, 0), (2, 1))


def frame_dest(d, dy, dc, chips):
    return ((d // 2 + dy) % chips) * 2 + ((d % 2) ^ dc)


def frame_perm(dy, dc, n):
    chips = n // 2
    return [(d, frame_dest(d, dy, dc, chips)) for d in range(n)]


def exchange(send, n):
    hop_up = lax.ppermute(send[(2, 0)], "frames", frame_perm(1, 0, n))
    hop_down = lax.ppermute(send[(2, 1)], "frames", frame_perm(-1, 0, n))
    direct = {o: send[o] for o in OFFSETS[:5]}
    hop_up, hop_down, direct = lax.optimization_barrier((hop_up, hop_down, direct))
    recv = {}
    recv[(2, 0)] = lax.ppermute(hop_up, "frames", frame_perm(1, 0, n))
    recv[(2, 1)] = lax.ppermute(hop_down, "frames", frame_perm(-1, 1, n))
    for dc in (0, 1):
        recv[(-1, dc)] = lax.ppermute(direct[(1, dc)], "frames", frame_perm(1, dc, n))
        recv[(1, dc)] = lax.ppermute(direct[(-1, dc)], "frames", frame_perm(-1, dc, n))
    recv[(0, 1)] = lax.ppermute(direct[(0, 1)], "frames", frame_perm(0, 1, n))
    return recv


def local(latent, query_rows, key_rows, value_rows, cached_out, refreshed, band_width,
          out_weight, temporal_weight):
    _, tile_count, tok_count, width = latent.shape
    lat = latent[0]
    q = query_rows[0]
    k = key_rows[0]
    v = value_rows[0]
    cache = cached_out[0]
    last_edges = jnp.stack([k[-1, -EDGE:], v[-1, -EDGE:]])
    first_edges = jnp.stack([k[0, :EDGE], v[0, :EDGE]])
    from_above = shifted(last_edges, "space", 1)
    from_below = shifted(first_edges, "space", -1)
    kp = jnp.concatenate([from_above[0][None], k[:-1, -EDGE:]], axis=0)
    vp = jnp.concatenate([from_above[1][None], v[:-1, -EDGE:]], axis=0)
    kn = jnp.concatenate([k[1:, :EDGE], from_below[0][None]], axis=0)
    vn = jnp.concatenate([v[1:, :EDGE], from_below[1][None]], axis=0)
    total_tiles = tile_count * lax.axis_size("space")
    tile_index = lax.axis_index("space") * tile_count + jnp.arange(tile_count, dtype=jnp.int32)
    flags = jnp.stack([refreshed[0].astype(jnp.int32),
                       (tile_index > 0).astype(jnp.int32),
                       (tile_index < total_tiles - 1).astype(jnp.int32)], axis=1)
    ke = jnp.concatenate([kp, kn], axis=1)
    ve = jnp.concatenate([vp, vn], axis=1)
    hidden, normed = spatial_block(flags, q, k, v, ke, ve, lat, cache, out_weight)

    n = lax.axis_size("frames")
    chips = n // 2
    chunk = tok_count // n
    me = lax.axis_index("frames")
    dests = {o: frame_dest(me, o[0], o[1], chips) for o in OFFSETS}
    send = {o: lax.dynamic_slice_in_dim(normed, dests[o] * chunk, chunk, axis=1) for o in OFFSETS}
    recv = exchange(send, n)
    own = lax.dynamic_slice_in_dim(normed, me * chunk, chunk, axis=1)
    block = jnp.stack([own] + [recv[o] for o in OFFSETS])
    fids = jnp.stack([me] + [dests[o] for o in OFFSETS]).astype(jnp.int32)
    rows = tile_count * chunk
    flat = jnp.dot(block.reshape(-1, width), temporal_weight,
                   preferred_element_type=jnp.float32).astype(jnp.bfloat16)
    packed = flat.reshape(n, rows, 3 * width)
    attended = temporal_attend(packed, band_width, fids)
    attended = attended.reshape(n, tile_count, chunk, width)
    back = exchange({o: attended[1 + i] for i, o in enumerate(OFFSETS)}, n)
    temporal = lax.dynamic_update_slice_in_dim(
        jnp.zeros_like(hidden), attended[0], me * chunk, axis=1)
    for o in OFFSETS:
        temporal = lax.dynamic_update_slice_in_dim(temporal, back[o], dests[o] * chunk, axis=1)
    mixed = (hidden.astype(jnp.float32) + temporal.astype(jnp.float32)).astype(jnp.bfloat16)
    return mixed[None]


def solution(mesh):
    return jax.shard_map(
        local,
        mesh=mesh,
        in_specs=(
            P("frames", "space", None, None),
            P("frames", "space", None, None),
            P("frames", "space", None, None),
            P("frames", "space", None, None),
            P("frames", "space", None, None),
            P("frames", "space"),
            P(),
            P(),
            P(),
        ),
        out_specs=P("frames", "space", None, None),
        check_vma=False,
    )
```

```python
import functools
import math

import jax
import jax.numpy as jnp
from jax import lax
from jax.experimental import pallas as pl
from jax.experimental.pallas import tpu as pltpu
from jax.sharding import PartitionSpec as P

EDGE = 64
HEADS = 16


def shifted(block, axis, distance):
    devices = range(lax.axis_size(axis))
    route = [(i - distance, i) for i in devices if i - distance in devices]
    return lax.ppermute(block, axis, route)


def head_window(h, head_dim, width):
    lo = h * head_dim
    start = min((lo // 128) * 128, width - 256)
    return lo, start


def spatial_kernel(flags_ref, q_ref, k_ref, v_ref, ke_ref, ve_ref,
                   lat_ref, cache_ref, wo_ref, hid_ref, nrm_ref, acc_ref, sp_ref):
    i = pl.program_id(0)
    refreshed = flags_ref[i, 0]
    prev_ok = flags_ref[i, 1]
    next_ok = flags_ref[i, 2]
    width = q_ref.shape[-1]
    head_dim = width // HEADS
    scaling = 1.0 / math.sqrt(head_dim)
    nt = (((1,), (1,)), ((), ()))

    @pl.when(refreshed == 1)
    def _():
        acc_ref[...] = jnp.zeros_like(acc_ref)
        edge_lane = lax.broadcasted_iota(jnp.int32, (1, 2 * EDGE), 1)
        edge_ok = jnp.where(edge_lane < EDGE, prev_ok, next_ok) == 1
        for h in range(HEADS):
            lo, start = head_window(h, head_dim, width)
            win = pl.ds(start, 256)
            lane = lax.broadcasted_iota(jnp.int32, (1, 256), 1) + start
            mask = (lane >= lo) & (lane < lo + head_dim)
            qh = jnp.where(mask, q_ref[0, :, win], jnp.zeros((), q_ref.dtype))
            s_mid = lax.dot_general(qh, k_ref[0, :, win], nt,
                                    preferred_element_type=jnp.float32) * scaling
            s_edge = lax.dot_general(qh, ke_ref[0, :, win], nt,
                                     preferred_element_type=jnp.float32) * scaling
            s_edge = jnp.where(edge_ok, s_edge, -jnp.inf)
            top = jnp.maximum(jnp.max(s_mid, axis=1, keepdims=True),
                              jnp.max(s_edge, axis=1, keepdims=True))
            e_mid = jnp.exp(s_mid - top)
            e_edge = jnp.exp(s_edge - top)
            total = (jnp.sum(e_mid, axis=1, keepdims=True)
                     + jnp.sum(e_edge, axis=1, keepdims=True))
            inv = 1.0 / total
            p_mid = (e_mid * inv).astype(jnp.bfloat16)
            p_edge = (e_edge * inv).astype(jnp.bfloat16)
            out = jnp.dot(p_mid, v_ref[0, :, win], preferred_element_type=jnp.float32)
            out = out + jnp.dot(p_edge, ve_ref[0, :, win], preferred_element_type=jnp.float32)
            acc_ref[:, win] += jnp.where(mask, out, 0.0)
        sp_ref[...] = acc_ref[...].astype(sp_ref.dtype)

    @pl.when(refreshed != 1)
    def _():
        sp_ref[...] = cache_ref[0]

    projected = jnp.dot(sp_ref[...], wo_ref[...], preferred_element_type=jnp.float32)
    hidden = (lat_ref[0].astype(jnp.float32) + projected).astype(jnp.bfloat16)
    hid_ref[0] = hidden
    h32 = hidden.astype(jnp.float32)
    ms = jnp.mean(h32 * h32, axis=-1, keepdims=True)
    nrm_ref[0] = (h32 * lax.rsqrt(ms + 1e-06)).astype(nrm_ref.dtype)


def spatial_block(flags, q, k, v, ke, ve, lat, cache, wo):
    tiles, tok, width = q.shape
    tile_spec = pl.BlockSpec((1, tok, width), lambda i, f: (i, 0, 0))
    edge_spec = pl.BlockSpec((1, 2 * EDGE, width), lambda i, f: (i, 0, 0))
    w_spec = pl.BlockSpec((width, width), lambda i, f: (0, 0))
    out_shape = [jax.ShapeDtypeStruct((tiles, tok, width), jnp.bfloat16)] * 2
    flops = tiles * (HEADS * 4 * tok * (tok + 2 * EDGE) * 256 + 2 * tok * width * width)
    cost = pl.CostEstimate(flops=flops, transcendentals=tiles * HEADS * tok * (tok + 2 * EDGE),
                           bytes_accessed=2 * (7 * tiles * tok * width + width * width))
    return pl.pallas_call(
        spatial_kernel,
        grid_spec=pltpu.PrefetchScalarGridSpec(
            num_scalar_prefetch=1,
            grid=(tiles,),
            in_specs=[tile_spec] * 3 + [edge_spec] * 2 + [tile_spec] * 2 + [w_spec],
            out_specs=[tile_spec, tile_spec],
            scratch_shapes=[pltpu.VMEM((tok, width), jnp.float32),
                            pltpu.VMEM((tok, width), jnp.bfloat16)],
        ),
        out_shape=out_shape,
        compiler_params=pltpu.CompilerParams(dimension_semantics=("arbitrary",),
                                             vmem_limit_bytes=48 * 1024 * 1024),
        cost_estimate=cost,
    )(flags, q, k, v, ke, ve, lat, cache, wo)


def temporal_kernel(fid_ref, bw_ref, q_ref, k_ref, v_ref, ind_ref, indt_ref, o_ref):
    frames, tok, width = q_ref.shape
    head_dim = width // HEADS
    scaling = 1.0 / math.sqrt(head_dim)
    bw = bw_ref[...].reshape(1, 1, HEADS)
    ind = ind_ref[...]
    indt = indt_ref[...]
    fids = jnp.concatenate(
        [jnp.full((1, 1, 1), fid_ref[g], jnp.int32) for g in range(frames)], axis=0)

    def body(f, carry):
        qf = q_ref[f].astype(jnp.float32)
        prod = (qf[None] * k_ref[...].astype(jnp.float32)).reshape(frames * tok, width)
        hi = prod.astype(jnp.bfloat16)
        lo = (prod - hi.astype(jnp.float32)).astype(jnp.bfloat16)
        s = (jnp.dot(hi, ind, preferred_element_type=jnp.float32)
             + jnp.dot(lo, ind, preferred_element_type=jnp.float32))
        s = s.reshape(frames, tok, HEADS) * scaling
        allowed = jnp.abs(fids - fid_ref[f]) <= bw
        s = jnp.where(allowed, s, -jnp.inf)
        top = jnp.max(s, axis=0, keepdims=True)
        expo = jnp.exp(s - top)
        total = jnp.sum(expo, axis=0, keepdims=True)
        p = (expo / total).astype(jnp.bfloat16).reshape(frames * tok, HEADS)
        wide = jnp.dot(p, indt, preferred_element_type=jnp.float32).reshape(frames, tok, width)
        out = jnp.sum(wide * v_ref[...].astype(jnp.float32), axis=0)
        o_ref[f] = out.astype(o_ref.dtype)
        return carry

    lax.fori_loop(0, frames, body, 0)


def temporal_attend(packed, band_width, fids):
    frames, tok, wide = packed.shape
    width = wide // 3
    q = packed[..., :width]
    k = packed[..., width:2 * width]
    v = packed[..., 2 * width:]
    head_dim = width // HEADS
    ind = (jnp.arange(width, dtype=jnp.int32)[:, None] // head_dim
           == jnp.arange(HEADS, dtype=jnp.int32)[None, :])
    vspec = pl.BlockSpec(memory_space=pltpu.VMEM)
    sspec = pl.BlockSpec(memory_space=pltpu.SMEM)
    cost = pl.CostEstimate(flops=frames * frames * tok * width * 40,
                           transcendentals=frames * frames * tok * HEADS,
                           bytes_accessed=2 * 4 * frames * tok * width)
    return pl.pallas_call(
        temporal_kernel,
        in_specs=[sspec] + [vspec] * 6,
        out_specs=vspec,
        out_shape=jax.ShapeDtypeStruct((frames, tok, width), jnp.bfloat16),
        compiler_params=pltpu.CompilerParams(vmem_limit_bytes=48 * 1024 * 1024),
        cost_estimate=cost,
    )(fids, band_width.reshape(1, HEADS), q, k, v, ind.astype(jnp.bfloat16),
      ind.T.astype(jnp.bfloat16))


OFFSETS = ((0, 1), (-1, 0), (-1, 1), (1, 0), (1, 1), (2, 0), (2, 1))


def frame_dest(d, dy, dc, chips):
    return ((d // 2 + dy) % chips) * 2 + ((d % 2) ^ dc)


def frame_perm(dy, dc, n):
    chips = n // 2
    return [(d, frame_dest(d, dy, dc, chips)) for d in range(n)]


def exchange(send, n):
    across = lax.ppermute(jnp.stack([send[(0, 1)], send[(1, 1)], send[(-1, 1)], send[(2, 1)]]),
                          "frames", frame_perm(0, 1, n))
    up = lax.ppermute(jnp.stack([send[(1, 0)], across[1], send[(2, 0)]]),
                      "frames", frame_perm(1, 0, n))
    down = lax.ppermute(jnp.stack([send[(-1, 0)], across[2], across[3]]),
                        "frames", frame_perm(-1, 0, n))
    recv = {(0, 1): across[0], (-1, 0): up[0], (-1, 1): up[1], (1, 0): down[0], (1, 1): down[1]}
    recv[(2, 0)] = lax.ppermute(up[2], "frames", frame_perm(1, 0, n))
    recv[(2, 1)] = lax.ppermute(down[2], "frames", frame_perm(-1, 0, n))
    return recv


def local(latent, query_rows, key_rows, value_rows, cached_out, refreshed, band_width,
          out_weight, temporal_weight):
    _, tile_count, tok_count, width = latent.shape
    lat = latent[0]
    q = query_rows[0]
    k = key_rows[0]
    v = value_rows[0]
    cache = cached_out[0]
    last_edges = jnp.stack([k[-1, -EDGE:], v[-1, -EDGE:]])
    first_edges = jnp.stack([k[0, :EDGE], v[0, :EDGE]])
    from_above = shifted(last_edges, "space", 1)
    from_below = shifted(first_edges, "space", -1)
    kp = jnp.concatenate([from_above[0][None], k[:-1, -EDGE:]], axis=0)
    vp = jnp.concatenate([from_above[1][None], v[:-1, -EDGE:]], axis=0)
    kn = jnp.concatenate([k[1:, :EDGE], from_below[0][None]], axis=0)
    vn = jnp.concatenate([v[1:, :EDGE], from_below[1][None]], axis=0)
    total_tiles = tile_count * lax.axis_size("space")
    tile_index = lax.axis_index("space") * tile_count + jnp.arange(tile_count, dtype=jnp.int32)
    flags = jnp.stack([refreshed[0].astype(jnp.int32),
                       (tile_index > 0).astype(jnp.int32),
                       (tile_index < total_tiles - 1).astype(jnp.int32)], axis=1)
    ke = jnp.concatenate([kp, kn], axis=1)
    ve = jnp.concatenate([vp, vn], axis=1)
    hidden, normed = spatial_block(flags, q, k, v, ke, ve, lat, cache, out_weight)

    n = lax.axis_size("frames")
    chips = n // 2
    chunk = tok_count // n
    me = lax.axis_index("frames")
    dests = {o: frame_dest(me, o[0], o[1], chips) for o in OFFSETS}
    send = {o: lax.dynamic_slice_in_dim(normed, dests[o] * chunk, chunk, axis=1) for o in OFFSETS}
    recv = exchange(send, n)
    own = lax.dynamic_slice_in_dim(normed, me * chunk, chunk, axis=1)
    block = jnp.stack([own] + [recv[o] for o in OFFSETS])
    fids = jnp.stack([me] + [dests[o] for o in OFFSETS]).astype(jnp.int32)
    rows = tile_count * chunk
    flat = jnp.dot(block.reshape(-1, width), temporal_weight,
                   preferred_element_type=jnp.float32).astype(jnp.bfloat16)
    packed = flat.reshape(n, rows, 3 * width)
    attended = temporal_attend(packed, band_width, fids)
    attended = attended.reshape(n, tile_count, chunk, width)
    back = exchange({o: attended[1 + i] for i, o in enumerate(OFFSETS)}, n)
    temporal = lax.dynamic_update_slice_in_dim(
        jnp.zeros_like(hidden), attended[0], me * chunk, axis=1)
    for o in OFFSETS:
        temporal = lax.dynamic_update_slice_in_dim(temporal, back[o], dests[o] * chunk, axis=1)
    mixed = (hidden.astype(jnp.float32) + temporal.astype(jnp.float32)).astype(jnp.bfloat16)
    return mixed[None]


def solution(mesh):
    return jax.shard_map(
        local,
        mesh=mesh,
        in_specs=(
            P("frames", "space", None, None),
            P("frames", "space", None, None),
            P("frames", "space", None, None),
            P("frames", "space", None, None),
            P("frames", "space", None, None),
            P("frames", "space"),
            P(),
            P(),
            P(),
        ),
        out_specs=P("frames", "space", None, None),
        check_vma=False,
    )
```

```python
import functools
import math

import jax
import jax.numpy as jnp
from jax import lax
from jax.experimental import pallas as pl
from jax.experimental.pallas import tpu as pltpu
from jax.sharding import PartitionSpec as P

EDGE = 64
HEADS = 16


def shifted(block, axis, distance):
    devices = range(lax.axis_size(axis))
    route = [(i - distance, i) for i in devices if i - distance in devices]
    return lax.ppermute(block, axis, route)


def head_window(h, head_dim, width):
    lo = h * head_dim
    start = min((lo // 128) * 128, width - 256)
    return lo, start


def spatial_kernel(flags_ref, q_ref, k_ref, v_ref, ke_ref, ve_ref,
                   lat_ref, cache_ref, wo_ref, hid_ref, nrm_ref, acc_ref, sp_ref):
    i = pl.program_id(0)
    refreshed = flags_ref[i, 0]
    prev_ok = flags_ref[i, 1]
    next_ok = flags_ref[i, 2]
    width = q_ref.shape[-1]
    head_dim = width // HEADS
    scaling = 1.0 / math.sqrt(head_dim)
    nt = (((1,), (1,)), ((), ()))

    @pl.when(refreshed == 1)
    def _():
        acc_ref[...] = jnp.zeros_like(acc_ref)
        edge_lane = lax.broadcasted_iota(jnp.int32, (1, 2 * EDGE), 1)
        edge_ok = jnp.where(edge_lane < EDGE, prev_ok, next_ok) == 1
        for h in range(HEADS):
            lo, start = head_window(h, head_dim, width)
            win = pl.ds(start, 256)
            lane = lax.broadcasted_iota(jnp.int32, (1, 256), 1) + start
            mask = (lane >= lo) & (lane < lo + head_dim)
            qh = jnp.where(mask, q_ref[0, :, win], jnp.zeros((), q_ref.dtype))
            s_mid = lax.dot_general(qh, k_ref[0, :, win], nt,
                                    preferred_element_type=jnp.float32) * scaling
            s_edge = lax.dot_general(qh, ke_ref[0, :, win], nt,
                                     preferred_element_type=jnp.float32) * scaling
            s_edge = jnp.where(edge_ok, s_edge, -jnp.inf)
            top = jnp.maximum(jnp.max(s_mid, axis=1, keepdims=True),
                              jnp.max(s_edge, axis=1, keepdims=True))
            e_mid = jnp.exp(s_mid - top)
            e_edge = jnp.exp(s_edge - top)
            total = (jnp.sum(e_mid, axis=1, keepdims=True)
                     + jnp.sum(e_edge, axis=1, keepdims=True))
            inv = 1.0 / total
            p_mid = (e_mid * inv).astype(jnp.bfloat16)
            p_edge = (e_edge * inv).astype(jnp.bfloat16)
            out = jnp.dot(p_mid, v_ref[0, :, win], preferred_element_type=jnp.float32)
            out = out + jnp.dot(p_edge, ve_ref[0, :, win], preferred_element_type=jnp.float32)
            acc_ref[:, win] += jnp.where(mask, out, 0.0)
        sp_ref[...] = acc_ref[...].astype(sp_ref.dtype)

    @pl.when(refreshed != 1)
    def _():
        sp_ref[...] = cache_ref[0]

    projected = jnp.dot(sp_ref[...], wo_ref[...], preferred_element_type=jnp.float32)
    hidden = (lat_ref[0].astype(jnp.float32) + projected).astype(jnp.bfloat16)
    hid_ref[0] = hidden
    h32 = hidden.astype(jnp.float32)
    ms = jnp.mean(h32 * h32, axis=-1, keepdims=True)
    nrm_ref[0] = (h32 * lax.rsqrt(ms + 1e-06)).astype(nrm_ref.dtype)


def spatial_block(flags, q, k, v, ke, ve, lat, cache, wo):
    tiles, tok, width = q.shape
    tile_spec = pl.BlockSpec((1, tok, width), lambda i, f: (i, 0, 0))
    edge_spec = pl.BlockSpec((1, 2 * EDGE, width), lambda i, f: (i, 0, 0))
    w_spec = pl.BlockSpec((width, width), lambda i, f: (0, 0))
    out_shape = [jax.ShapeDtypeStruct((tiles, tok, width), jnp.bfloat16)] * 2
    flops = tiles * (HEADS * 4 * tok * (tok + 2 * EDGE) * 256 + 2 * tok * width * width)
    cost = pl.CostEstimate(flops=flops, transcendentals=tiles * HEADS * tok * (tok + 2 * EDGE),
                           bytes_accessed=2 * (7 * tiles * tok * width + width * width))
    return pl.pallas_call(
        spatial_kernel,
        grid_spec=pltpu.PrefetchScalarGridSpec(
            num_scalar_prefetch=1,
            grid=(tiles,),
            in_specs=[tile_spec] * 3 + [edge_spec] * 2 + [tile_spec] * 2 + [w_spec],
            out_specs=[tile_spec, tile_spec],
            scratch_shapes=[pltpu.VMEM((tok, width), jnp.float32),
                            pltpu.VMEM((tok, width), jnp.bfloat16)],
        ),
        out_shape=out_shape,
        compiler_params=pltpu.CompilerParams(dimension_semantics=("arbitrary",),
                                             vmem_limit_bytes=48 * 1024 * 1024),
        cost_estimate=cost,
    )(flags, q, k, v, ke, ve, lat, cache, wo)


def temporal_kernel(fid_ref, bw_ref, q_ref, k_ref, v_ref, ind_ref, indt_ref, o_ref):
    frames, tok, width = q_ref.shape
    head_dim = width // HEADS
    scaling = 1.0 / math.sqrt(head_dim)
    bw = bw_ref[...].reshape(1, 1, HEADS)
    ind = ind_ref[...]
    indt = indt_ref[...]
    fids = jnp.concatenate(
        [jnp.full((1, 1, 1), fid_ref[g], jnp.int32) for g in range(frames)], axis=0)

    def body(f, carry):
        qf = q_ref[f].astype(jnp.float32)
        prod = (qf[None] * k_ref[...].astype(jnp.float32)).reshape(frames * tok, width)
        hi = prod.astype(jnp.bfloat16)
        lo = (prod - hi.astype(jnp.float32)).astype(jnp.bfloat16)
        s = (jnp.dot(hi, ind, preferred_element_type=jnp.float32)
             + jnp.dot(lo, ind, preferred_element_type=jnp.float32))
        s = s.reshape(frames, tok, HEADS) * scaling
        allowed = jnp.abs(fids - fid_ref[f]) <= bw
        s = jnp.where(allowed, s, -jnp.inf)
        top = jnp.max(s, axis=0, keepdims=True)
        expo = jnp.exp(s - top)
        total = jnp.sum(expo, axis=0, keepdims=True)
        p = (expo / total).astype(jnp.bfloat16).reshape(frames * tok, HEADS)
        wide = jnp.dot(p, indt, preferred_element_type=jnp.float32).reshape(frames, tok, width)
        out = jnp.sum(wide * v_ref[...].astype(jnp.float32), axis=0)
        o_ref[f] = out.astype(o_ref.dtype)
        return carry

    lax.fori_loop(0, frames, body, 0)


def temporal_attend(packed, band_width, fids):
    frames, tok, wide = packed.shape
    width = wide // 3
    q = packed[..., :width]
    k = packed[..., width:2 * width]
    v = packed[..., 2 * width:]
    head_dim = width // HEADS
    ind = (jnp.arange(width, dtype=jnp.int32)[:, None] // head_dim
           == jnp.arange(HEADS, dtype=jnp.int32)[None, :])
    vspec = pl.BlockSpec(memory_space=pltpu.VMEM)
    sspec = pl.BlockSpec(memory_space=pltpu.SMEM)
    cost = pl.CostEstimate(flops=frames * frames * tok * width * 40,
                           transcendentals=frames * frames * tok * HEADS,
                           bytes_accessed=2 * 4 * frames * tok * width)
    return pl.pallas_call(
        temporal_kernel,
        in_specs=[sspec] + [vspec] * 6,
        out_specs=vspec,
        out_shape=jax.ShapeDtypeStruct((frames, tok, width), jnp.bfloat16),
        compiler_params=pltpu.CompilerParams(vmem_limit_bytes=48 * 1024 * 1024),
        cost_estimate=cost,
    )(fids, band_width.reshape(1, HEADS), q, k, v, ind.astype(jnp.bfloat16),
      ind.T.astype(jnp.bfloat16))


OFFSETS = ((0, 1), (-1, 0), (-1, 1), (1, 0), (1, 1), (2, 0), (2, 1))


def frame_dest(d, dy, dc, chips):
    return ((d // 2 + dy) % chips) * 2 + ((d % 2) ^ dc)


def frame_perm(dy, dc, n):
    chips = n // 2
    return [(d, frame_dest(d, dy, dc, chips)) for d in range(n)]


def exchange(send, n):
    across = lax.ppermute(jnp.stack([send[(0, 1)], send[(1, 1)], send[(-1, 1)], send[(2, 1)]]),
                          "frames", frame_perm(0, 1, n))
    up = lax.ppermute(jnp.stack([send[(1, 0)], across[1], send[(2, 0)]]),
                      "frames", frame_perm(1, 0, n))
    down = lax.ppermute(jnp.stack([send[(-1, 0)], across[2], across[3]]),
                        "frames", frame_perm(-1, 0, n))
    recv = {(0, 1): across[0], (-1, 0): up[0], (-1, 1): up[1], (1, 0): down[0], (1, 1): down[1]}
    recv[(2, 0)] = lax.ppermute(up[2], "frames", frame_perm(1, 0, n))
    recv[(2, 1)] = lax.ppermute(down[2], "frames", frame_perm(-1, 0, n))
    return recv


def local(latent, query_rows, key_rows, value_rows, cached_out, refreshed, band_width,
          out_weight, temporal_weight):
    _, tile_count, tok_count, width = latent.shape
    lat = latent[0]
    q = query_rows[0]
    k = key_rows[0]
    v = value_rows[0]
    cache = cached_out[0]
    last_edges = jnp.stack([k[-1, -EDGE:], v[-1, -EDGE:]])
    first_edges = jnp.stack([k[0, :EDGE], v[0, :EDGE]])
    from_above = shifted(last_edges, "space", 1)
    from_below = shifted(first_edges, "space", -1)
    kp = jnp.concatenate([from_above[0][None], k[:-1, -EDGE:]], axis=0)
    vp = jnp.concatenate([from_above[1][None], v[:-1, -EDGE:]], axis=0)
    kn = jnp.concatenate([k[1:, :EDGE], from_below[0][None]], axis=0)
    vn = jnp.concatenate([v[1:, :EDGE], from_below[1][None]], axis=0)
    total_tiles = tile_count * lax.axis_size("space")
    tile_index = lax.axis_index("space") * tile_count + jnp.arange(tile_count, dtype=jnp.int32)
    flags = jnp.stack([refreshed[0].astype(jnp.int32),
                       (tile_index > 0).astype(jnp.int32),
                       (tile_index < total_tiles - 1).astype(jnp.int32)], axis=1)
    ke = jnp.concatenate([kp, kn], axis=1)
    ve = jnp.concatenate([vp, vn], axis=1)
    n = lax.axis_size("frames")
    fids = jnp.arange(n, dtype=jnp.int32)
    parts = []
    for t in range(tile_count):
        one = slice(t, t + 1)
        hidden, normed = spatial_block(flags[one], q[one], k[one], v[one], ke[one], ve[one],
                                       lat[one], cache[one], out_weight)
        block = lax.all_to_all(normed, "frames", split_axis=1, concat_axis=0, tiled=True)
        flat = jnp.dot(block.reshape(-1, width), temporal_weight,
                       preferred_element_type=jnp.float32).astype(jnp.bfloat16)
        packed = flat.reshape(n, -1, 3 * width)
        attended = temporal_attend(packed, band_width, fids)
        temporal = lax.all_to_all(attended, "frames", split_axis=0, concat_axis=1, tiled=True)
        parts.append((hidden.astype(jnp.float32) + temporal.astype(jnp.float32)).astype(jnp.bfloat16))
    mixed = jnp.concatenate(parts, axis=0)
    return mixed[None]


def solution(mesh):
    return jax.shard_map(
        local,
        mesh=mesh,
        in_specs=(
            P("frames", "space", None, None),
            P("frames", "space", None, None),
            P("frames", "space", None, None),
            P("frames", "space", None, None),
            P("frames", "space", None, None),
            P("frames", "space"),
            P(),
            P(),
            P(),
        ),
        out_specs=P("frames", "space", None, None),
        check_vma=False,
    )
```

```python
import functools
import math

import jax
import jax.numpy as jnp
from jax import lax
from jax.experimental import pallas as pl
from jax.experimental.pallas import tpu as pltpu
from jax.sharding import PartitionSpec as P

EDGE = 64
HEADS = 16


def shifted(block, axis, distance):
    devices = range(lax.axis_size(axis))
    route = [(i - distance, i) for i in devices if i - distance in devices]
    return lax.ppermute(block, axis, route)


def head_window(h, head_dim, width):
    lo = h * head_dim
    start = min((lo // 128) * 128, width - 256)
    return lo, start


def local_attend_kernel(flags_ref, q_ref, k_ref, v_ref, acc_ref, m_ref, l_ref):
    i = pl.program_id(0)
    width = q_ref.shape[-1]
    head_dim = width // HEADS
    scaling = 1.0 / math.sqrt(head_dim)
    nt = (((1,), (1,)), ((), ()))

    @pl.when(flags_ref[i, 0] == 1)
    def _():
        acc_ref[...] = jnp.zeros_like(acc_ref)
        for h in range(HEADS):
            lo, start = head_window(h, head_dim, width)
            win = pl.ds(start, 256)
            lane = lax.broadcasted_iota(jnp.int32, (1, 256), 1) + start
            mask = (lane >= lo) & (lane < lo + head_dim)
            qh = jnp.where(mask, q_ref[0, :, win], jnp.zeros((), q_ref.dtype))
            s = lax.dot_general(qh, k_ref[0, :, win], nt,
                                preferred_element_type=jnp.float32) * scaling
            top = jnp.max(s, axis=1, keepdims=True)
            e = jnp.exp(s - top)
            m_ref[0, :, h:h + 1] = top
            l_ref[0, :, h:h + 1] = jnp.sum(e, axis=1, keepdims=True)
            out = jnp.dot(e.astype(jnp.bfloat16), v_ref[0, :, win],
                          preferred_element_type=jnp.float32)
            acc_ref[0, :, win] = jnp.where(mask, out, acc_ref[0, :, win])


def local_attend(flags, q, k, v):
    tiles, tok, width = q.shape
    tile_spec = pl.BlockSpec((1, tok, width), lambda i, f: (i, 0, 0))
    stat_spec = pl.BlockSpec((1, tok, HEADS), lambda i, f: (i, 0, 0))
    cost = pl.CostEstimate(flops=tiles * HEADS * 4 * tok * tok * 256,
                           transcendentals=tiles * HEADS * tok * tok,
                           bytes_accessed=2 * 3 * tiles * tok * width + 4 * tiles * tok * width)
    return pl.pallas_call(
        local_attend_kernel,
        grid_spec=pltpu.PrefetchScalarGridSpec(
            num_scalar_prefetch=1,
            grid=(tiles,),
            in_specs=[tile_spec] * 3,
            out_specs=[tile_spec, stat_spec, stat_spec],
        ),
        out_shape=[jax.ShapeDtypeStruct((tiles, tok, width), jnp.float32),
                   jax.ShapeDtypeStruct((tiles, tok, HEADS), jnp.float32),
                   jax.ShapeDtypeStruct((tiles, tok, HEADS), jnp.float32)],
        compiler_params=pltpu.CompilerParams(dimension_semantics=("arbitrary",),
                                             vmem_limit_bytes=48 * 1024 * 1024),
        cost_estimate=cost,
    )(flags, q, k, v)


def spatial_kernel(flags_ref, q_ref, ke_ref, ve_ref, part_ref, m_ref, l_ref,
                   lat_ref, cache_ref, wo_ref, hid_ref, nrm_ref, acc_ref, sp_ref):
    i = pl.program_id(0)
    refreshed = flags_ref[i, 0]
    prev_ok = flags_ref[i, 1]
    next_ok = flags_ref[i, 2]
    width = q_ref.shape[-1]
    head_dim = width // HEADS
    scaling = 1.0 / math.sqrt(head_dim)
    nt = (((1,), (1,)), ((), ()))

    @pl.when(refreshed == 1)
    def _():
        acc_ref[...] = jnp.zeros_like(acc_ref)
        edge_lane = lax.broadcasted_iota(jnp.int32, (1, 2 * EDGE), 1)
        edge_ok = jnp.where(edge_lane < EDGE, prev_ok, next_ok) == 1
        for h in range(HEADS):
            lo, start = head_window(h, head_dim, width)
            win = pl.ds(start, 256)
            lane = lax.broadcasted_iota(jnp.int32, (1, 256), 1) + start
            mask = (lane >= lo) & (lane < lo + head_dim)
            qh = jnp.where(mask, q_ref[0, :, win], jnp.zeros((), q_ref.dtype))
            s_edge = lax.dot_general(qh, ke_ref[0, :, win], nt,
                                     preferred_element_type=jnp.float32) * scaling
            s_edge = jnp.where(edge_ok, s_edge, -jnp.inf)
            m_mid = m_ref[0, :, h:h + 1]
            top = jnp.maximum(m_mid, jnp.max(s_edge, axis=1, keepdims=True))
            alpha = jnp.exp(m_mid - top)
            e_edge = jnp.exp(s_edge - top)
            total = l_ref[0, :, h:h + 1] * alpha + jnp.sum(e_edge, axis=1, keepdims=True)
            inv = 1.0 / total
            out = jnp.dot(e_edge.astype(jnp.bfloat16), ve_ref[0, :, win],
                          preferred_element_type=jnp.float32)
            val = (part_ref[0, :, win] * alpha + out) * inv
            acc_ref[:, win] = jnp.where(mask, val, acc_ref[:, win])
        sp_ref[...] = acc_ref[...].astype(sp_ref.dtype)

    @pl.when(refreshed != 1)
    def _():
        sp_ref[...] = cache_ref[0]

    projected = jnp.dot(sp_ref[...], wo_ref[...], preferred_element_type=jnp.float32)
    hidden = (lat_ref[0].astype(jnp.float32) + projected).astype(jnp.bfloat16)
    hid_ref[0] = hidden
    h32 = hidden.astype(jnp.float32)
    ms = jnp.mean(h32 * h32, axis=-1, keepdims=True)
    nrm_ref[0] = (h32 * lax.rsqrt(ms + 1e-06)).astype(nrm_ref.dtype)


def spatial_block(flags, q, ke, ve, part, m, l, lat, cache, wo):
    tiles, tok, width = q.shape
    tile_spec = pl.BlockSpec((1, tok, width), lambda i, f: (i, 0, 0))
    edge_spec = pl.BlockSpec((1, 2 * EDGE, width), lambda i, f: (i, 0, 0))
    stat_spec = pl.BlockSpec((1, tok, HEADS), lambda i, f: (i, 0, 0))
    w_spec = pl.BlockSpec((width, width), lambda i, f: (0, 0))
    out_shape = [jax.ShapeDtypeStruct((tiles, tok, width), jnp.bfloat16)] * 2
    flops = tiles * (HEADS * 4 * tok * 2 * EDGE * 256 + 2 * tok * width * width)
    cost = pl.CostEstimate(flops=flops, transcendentals=tiles * HEADS * tok * 2 * EDGE,
                           bytes_accessed=2 * (5 * tiles * tok * width + width * width)
                           + 4 * tiles * tok * width)
    return pl.pallas_call(
        spatial_kernel,
        grid_spec=pltpu.PrefetchScalarGridSpec(
            num_scalar_prefetch=1,
            grid=(tiles,),
            in_specs=[tile_spec] + [edge_spec] * 2 + [tile_spec, stat_spec, stat_spec]
            + [tile_spec] * 2 + [w_spec],
            out_specs=[tile_spec, tile_spec],
            scratch_shapes=[pltpu.VMEM((tok, width), jnp.float32),
                            pltpu.VMEM((tok, width), jnp.bfloat16)],
        ),
        out_shape=out_shape,
        compiler_params=pltpu.CompilerParams(dimension_semantics=("arbitrary",),
                                             vmem_limit_bytes=48 * 1024 * 1024),
        cost_estimate=cost,
    )(flags, q, ke, ve, part, m, l, lat, cache, wo)


def temporal_kernel(fid_ref, bw_ref, q_ref, k_ref, v_ref, ind_ref, indt_ref, o_ref):
    frames, tok, width = q_ref.shape
    head_dim = width // HEADS
    scaling = 1.0 / math.sqrt(head_dim)
    bw = bw_ref[...].reshape(1, 1, HEADS)
    ind = ind_ref[...]
    indt = indt_ref[...]
    fids = jnp.concatenate(
        [jnp.full((1, 1, 1), fid_ref[g], jnp.int32) for g in range(frames)], axis=0)

    def body(f, carry):
        qf = q_ref[f].astype(jnp.float32)
        prod = (qf[None] * k_ref[...].astype(jnp.float32)).reshape(frames * tok, width)
        hi = prod.astype(jnp.bfloat16)
        lo = (prod - hi.astype(jnp.float32)).astype(jnp.bfloat16)
        s = (jnp.dot(hi, ind, preferred_element_type=jnp.float32)
             + jnp.dot(lo, ind, preferred_element_type=jnp.float32))
        s = s.reshape(frames, tok, HEADS) * scaling
        allowed = jnp.abs(fids - fid_ref[f]) <= bw
        s = jnp.where(allowed, s, -jnp.inf)
        top = jnp.max(s, axis=0, keepdims=True)
        expo = jnp.exp(s - top)
        total = jnp.sum(expo, axis=0, keepdims=True)
        p = (expo / total).astype(jnp.bfloat16).reshape(frames * tok, HEADS)
        wide = jnp.dot(p, indt, preferred_element_type=jnp.float32).reshape(frames, tok, width)
        out = jnp.sum(wide * v_ref[...].astype(jnp.float32), axis=0)
        o_ref[f] = out.astype(o_ref.dtype)
        return carry

    lax.fori_loop(0, frames, body, 0)


def temporal_attend(packed, band_width, fids):
    frames, tok, wide = packed.shape
    width = wide // 3
    q = packed[..., :width]
    k = packed[..., width:2 * width]
    v = packed[..., 2 * width:]
    head_dim = width // HEADS
    ind = (jnp.arange(width, dtype=jnp.int32)[:, None] // head_dim
           == jnp.arange(HEADS, dtype=jnp.int32)[None, :])
    vspec = pl.BlockSpec(memory_space=pltpu.VMEM)
    sspec = pl.BlockSpec(memory_space=pltpu.SMEM)
    cost = pl.CostEstimate(flops=frames * frames * tok * width * 40,
                           transcendentals=frames * frames * tok * HEADS,
                           bytes_accessed=2 * 4 * frames * tok * width)
    return pl.pallas_call(
        temporal_kernel,
        in_specs=[sspec] + [vspec] * 6,
        out_specs=vspec,
        out_shape=jax.ShapeDtypeStruct((frames, tok, width), jnp.bfloat16),
        compiler_params=pltpu.CompilerParams(vmem_limit_bytes=48 * 1024 * 1024),
        cost_estimate=cost,
    )(fids, band_width.reshape(1, HEADS), q, k, v, ind.astype(jnp.bfloat16),
      ind.T.astype(jnp.bfloat16))


OFFSETS = ((0, 1), (-1, 0), (-1, 1), (1, 0), (1, 1), (2, 0), (2, 1))


def frame_dest(d, dy, dc, chips):
    return ((d // 2 + dy) % chips) * 2 + ((d % 2) ^ dc)


def frame_perm(dy, dc, n):
    chips = n // 2
    return [(d, frame_dest(d, dy, dc, chips)) for d in range(n)]


def exchange(send, n):
    recv = {}
    recv[(0, 1)] = lax.ppermute(send[(0, 1)], "frames", frame_perm(0, 1, n))
    for dc in (0, 1):
        recv[(-1, dc)] = lax.ppermute(send[(1, dc)], "frames", frame_perm(1, dc, n))
        recv[(1, dc)] = lax.ppermute(send[(-1, dc)], "frames", frame_perm(-1, dc, n))
    hop = lax.ppermute(send[(2, 0)], "frames", frame_perm(1, 0, n))
    recv[(2, 0)] = lax.ppermute(hop, "frames", frame_perm(1, 0, n))
    hop = lax.ppermute(send[(2, 1)], "frames", frame_perm(-1, 0, n))
    recv[(2, 1)] = lax.ppermute(hop, "frames", frame_perm(-1, 1, n))
    return recv


def local(latent, query_rows, key_rows, value_rows, cached_out, refreshed, band_width,
          out_weight, temporal_weight):
    _, tile_count, tok_count, width = latent.shape
    lat = latent[0]
    q = query_rows[0]
    k = key_rows[0]
    v = value_rows[0]
    cache = cached_out[0]
    last_edges = jnp.stack([k[-1, -EDGE:], v[-1, -EDGE:]])
    first_edges = jnp.stack([k[0, :EDGE], v[0, :EDGE]])
    from_above = shifted(last_edges, "space", 1)
    from_below = shifted(first_edges, "space", -1)
    kp = jnp.concatenate([from_above[0][None], k[:-1, -EDGE:]], axis=0)
    vp = jnp.concatenate([from_above[1][None], v[:-1, -EDGE:]], axis=0)
    kn = jnp.concatenate([k[1:, :EDGE], from_below[0][None]], axis=0)
    vn = jnp.concatenate([v[1:, :EDGE], from_below[1][None]], axis=0)
    total_tiles = tile_count * lax.axis_size("space")
    tile_index = lax.axis_index("space") * tile_count + jnp.arange(tile_count, dtype=jnp.int32)
    flags = jnp.stack([refreshed[0].astype(jnp.int32),
                       (tile_index > 0).astype(jnp.int32),
                       (tile_index < total_tiles - 1).astype(jnp.int32)], axis=1)
    ke = jnp.concatenate([kp, kn], axis=1)
    ve = jnp.concatenate([vp, vn], axis=1)
    part, m_mid, l_mid = local_attend(flags, q, k, v)
    hidden, normed = spatial_block(flags, q, ke, ve, part, m_mid, l_mid, lat, cache, out_weight)

    n = lax.axis_size("frames")
    chips = n // 2
    chunk = tok_count // n
    me = lax.axis_index("frames")
    dests = {o: frame_dest(me, o[0], o[1], chips) for o in OFFSETS}
    send = {o: lax.dynamic_slice_in_dim(normed, dests[o] * chunk, chunk, axis=1) for o in OFFSETS}
    recv = exchange(send, n)
    own = lax.dynamic_slice_in_dim(normed, me * chunk, chunk, axis=1)
    block = jnp.stack([own] + [recv[o] for o in OFFSETS])
    fids = jnp.stack([me] + [dests[o] for o in OFFSETS]).astype(jnp.int32)
    rows = tile_count * chunk
    flat = jnp.dot(block.reshape(-1, width), temporal_weight,
                   preferred_element_type=jnp.float32).astype(jnp.bfloat16)
    packed = flat.reshape(n, rows, 3 * width)
    attended = temporal_attend(packed, band_width, fids)
    attended = attended.reshape(n, tile_count, chunk, width)
    back = exchange({o: attended[1 + i] for i, o in enumerate(OFFSETS)}, n)
    temporal = lax.dynamic_update_slice_in_dim(
        jnp.zeros_like(hidden), attended[0], me * chunk, axis=1)
    for o in OFFSETS:
        temporal = lax.dynamic_update_slice_in_dim(temporal, back[o], dests[o] * chunk, axis=1)
    mixed = (hidden.astype(jnp.float32) + temporal.astype(jnp.float32)).astype(jnp.bfloat16)
    return mixed[None]


def solution(mesh):
    return jax.shard_map(
        local,
        mesh=mesh,
        in_specs=(
            P("frames", "space", None, None),
            P("frames", "space", None, None),
            P("frames", "space", None, None),
            P("frames", "space", None, None),
            P("frames", "space", None, None),
            P("frames", "space"),
            P(),
            P(),
            P(),
        ),
        out_specs=P("frames", "space", None, None),
        check_vma=False,
    )
```

```python
import functools
import math

import jax
import jax.numpy as jnp
from jax import lax
from jax.experimental import pallas as pl
from jax.experimental.pallas import tpu as pltpu
from jax.sharding import PartitionSpec as P

EDGE = 64
HEADS = 16


def shifted(block, axis, distance):
    devices = range(lax.axis_size(axis))
    route = [(i - distance, i) for i in devices if i - distance in devices]
    return lax.ppermute(block, axis, route)


def head_window(h, head_dim, width):
    lo = h * head_dim
    start = min((lo // 128) * 128, width - 256)
    return lo, start


def spatial_kernel(flags_ref, q_ref, k_ref, v_ref, ke_ref, ve_ref,
                   lat_ref, cache_ref, wo_ref, hid_ref, nrm_ref, acc_ref, sp_ref):
    i = pl.program_id(0)
    refreshed = flags_ref[i, 0]
    prev_ok = flags_ref[i, 1]
    next_ok = flags_ref[i, 2]
    width = q_ref.shape[-1]
    head_dim = width // HEADS
    scaling = 1.0 / math.sqrt(head_dim)
    nt = (((1,), (1,)), ((), ()))

    @pl.when(refreshed == 1)
    def _():
        acc_ref[...] = jnp.zeros_like(acc_ref)
        edge_lane = lax.broadcasted_iota(jnp.int32, (1, 2 * EDGE), 1)
        edge_ok = jnp.where(edge_lane < EDGE, prev_ok, next_ok) == 1
        for h in range(HEADS):
            lo, start = head_window(h, head_dim, width)
            win = pl.ds(start, 256)
            lane = lax.broadcasted_iota(jnp.int32, (1, 256), 1) + start
            mask = (lane >= lo) & (lane < lo + head_dim)
            qh = jnp.where(mask, q_ref[0, :, win], jnp.zeros((), q_ref.dtype))
            s_mid = lax.dot_general(qh, k_ref[0, :, win], nt,
                                    preferred_element_type=jnp.float32) * scaling
            s_edge = lax.dot_general(qh, ke_ref[0, :, win], nt,
                                     preferred_element_type=jnp.float32) * scaling
            s_edge = jnp.where(edge_ok, s_edge, -jnp.inf)
            top = jnp.maximum(jnp.max(s_mid, axis=1, keepdims=True),
                              jnp.max(s_edge, axis=1, keepdims=True))
            e_mid = jnp.exp(s_mid - top)
            e_edge = jnp.exp(s_edge - top)
            total = (jnp.sum(e_mid, axis=1, keepdims=True)
                     + jnp.sum(e_edge, axis=1, keepdims=True))
            inv = 1.0 / total
            p_mid = (e_mid * inv).astype(jnp.bfloat16)
            p_edge = (e_edge * inv).astype(jnp.bfloat16)
            out = jnp.dot(p_mid, v_ref[0, :, win], preferred_element_type=jnp.float32)
            out = out + jnp.dot(p_edge, ve_ref[0, :, win], preferred_element_type=jnp.float32)
            acc_ref[:, win] += jnp.where(mask, out, 0.0)
        sp_ref[...] = acc_ref[...].astype(sp_ref.dtype)

    @pl.when(refreshed != 1)
    def _():
        sp_ref[...] = cache_ref[0]

    projected = jnp.dot(sp_ref[...], wo_ref[...], preferred_element_type=jnp.float32)
    hidden = (lat_ref[0].astype(jnp.float32) + projected).astype(jnp.bfloat16)
    hid_ref[0] = hidden
    h32 = hidden.astype(jnp.float32)
    ms = jnp.mean(h32 * h32, axis=-1, keepdims=True)
    nrm_ref[0] = (h32 * lax.rsqrt(ms + 1e-06)).astype(nrm_ref.dtype)


def spatial_block(flags, q, k, v, ke, ve, lat, cache, wo):
    tiles, tok, width = q.shape
    tile_spec = pl.BlockSpec((1, tok, width), lambda i, f: (i, 0, 0))
    edge_spec = pl.BlockSpec((1, 2 * EDGE, width), lambda i, f: (i, 0, 0))
    w_spec = pl.BlockSpec((width, width), lambda i, f: (0, 0))
    out_shape = [jax.ShapeDtypeStruct((tiles, tok, width), jnp.bfloat16)] * 2
    flops = tiles * (HEADS * 4 * tok * (tok + 2 * EDGE) * 256 + 2 * tok * width * width)
    cost = pl.CostEstimate(flops=flops, transcendentals=tiles * HEADS * tok * (tok + 2 * EDGE),
                           bytes_accessed=2 * (7 * tiles * tok * width + width * width))
    return pl.pallas_call(
        spatial_kernel,
        grid_spec=pltpu.PrefetchScalarGridSpec(
            num_scalar_prefetch=1,
            grid=(tiles,),
            in_specs=[tile_spec] * 3 + [edge_spec] * 2 + [tile_spec] * 2 + [w_spec],
            out_specs=[tile_spec, tile_spec],
            scratch_shapes=[pltpu.VMEM((tok, width), jnp.float32),
                            pltpu.VMEM((tok, width), jnp.bfloat16)],
        ),
        out_shape=out_shape,
        compiler_params=pltpu.CompilerParams(dimension_semantics=("arbitrary",),
                                             vmem_limit_bytes=48 * 1024 * 1024),
        cost_estimate=cost,
    )(flags, q, k, v, ke, ve, lat, cache, wo)


def temporal_kernel(fid_ref, bw_ref, q_ref, k_ref, v_ref, ind_ref, indt_ref, o_ref,
                    k32_ref, v32_ref):
    frames, tok, width = q_ref.shape
    k32_ref[...] = k_ref[...].astype(jnp.float32)
    v32_ref[...] = v_ref[...].astype(jnp.float32)
    head_dim = width // HEADS
    scaling = 1.0 / math.sqrt(head_dim)
    bw = bw_ref[...].reshape(1, 1, HEADS)
    ind = ind_ref[...]
    indt = indt_ref[...]
    fids = jnp.concatenate(
        [jnp.full((1, 1, 1), fid_ref[g], jnp.int32) for g in range(frames)], axis=0)

    def body(f, carry):
        qf = q_ref[f].astype(jnp.float32)
        prod = (qf[None] * k32_ref[...]).reshape(frames * tok, width)
        hi = prod.astype(jnp.bfloat16)
        lo = (prod - hi.astype(jnp.float32)).astype(jnp.bfloat16)
        s = (jnp.dot(hi, ind, preferred_element_type=jnp.float32)
             + jnp.dot(lo, ind, preferred_element_type=jnp.float32))
        s = s.reshape(frames, tok, HEADS) * scaling
        allowed = jnp.abs(fids - fid_ref[f]) <= bw
        s = jnp.where(allowed, s, -jnp.inf)
        top = jnp.max(s, axis=0, keepdims=True)
        expo = jnp.exp(s - top)
        total = jnp.sum(expo, axis=0, keepdims=True)
        p = (expo / total).astype(jnp.bfloat16).reshape(frames * tok, HEADS)
        wide = jnp.dot(p, indt, preferred_element_type=jnp.float32).reshape(frames, tok, width)
        out = jnp.sum(wide * v32_ref[...], axis=0)
        o_ref[f] = out.astype(o_ref.dtype)
        return carry

    lax.fori_loop(0, frames, body, 0)


def temporal_attend(packed, band_width, fids):
    frames, tok, wide = packed.shape
    width = wide // 3
    q = packed[..., :width]
    k = packed[..., width:2 * width]
    v = packed[..., 2 * width:]
    head_dim = width // HEADS
    ind = (jnp.arange(width, dtype=jnp.int32)[:, None] // head_dim
           == jnp.arange(HEADS, dtype=jnp.int32)[None, :])
    vspec = pl.BlockSpec(memory_space=pltpu.VMEM)
    sspec = pl.BlockSpec(memory_space=pltpu.SMEM)
    cost = pl.CostEstimate(flops=frames * frames * tok * width * 40,
                           transcendentals=frames * frames * tok * HEADS,
                           bytes_accessed=2 * 4 * frames * tok * width)
    return pl.pallas_call(
        temporal_kernel,
        in_specs=[sspec] + [vspec] * 6,
        out_specs=vspec,
        out_shape=jax.ShapeDtypeStruct((frames, tok, width), jnp.bfloat16),
        scratch_shapes=[pltpu.VMEM((frames, tok, width), jnp.float32)] * 2,
        compiler_params=pltpu.CompilerParams(vmem_limit_bytes=48 * 1024 * 1024),
        cost_estimate=cost,
    )(fids, band_width.reshape(1, HEADS), q, k, v, ind.astype(jnp.bfloat16),
      ind.T.astype(jnp.bfloat16))


OFFSETS = ((0, 1), (-1, 0), (-1, 1), (1, 0), (1, 1), (2, 0), (2, 1))


def frame_dest(d, dy, dc, chips):
    return ((d // 2 + dy) % chips) * 2 + ((d % 2) ^ dc)


def frame_perm(dy, dc, n):
    chips = n // 2
    return [(d, frame_dest(d, dy, dc, chips)) for d in range(n)]


def exchange(send, n):
    recv = {}
    recv[(0, 1)] = lax.ppermute(send[(0, 1)], "frames", frame_perm(0, 1, n))
    for dc in (0, 1):
        recv[(-1, dc)] = lax.ppermute(send[(1, dc)], "frames", frame_perm(1, dc, n))
        recv[(1, dc)] = lax.ppermute(send[(-1, dc)], "frames", frame_perm(-1, dc, n))
    hop = lax.ppermute(send[(2, 0)], "frames", frame_perm(1, 0, n))
    recv[(2, 0)] = lax.ppermute(hop, "frames", frame_perm(1, 0, n))
    hop = lax.ppermute(send[(2, 1)], "frames", frame_perm(-1, 0, n))
    recv[(2, 1)] = lax.ppermute(hop, "frames", frame_perm(-1, 1, n))
    return recv


def local(latent, query_rows, key_rows, value_rows, cached_out, refreshed, band_width,
          out_weight, temporal_weight):
    _, tile_count, tok_count, width = latent.shape
    lat = latent[0]
    q = query_rows[0]
    k = key_rows[0]
    v = value_rows[0]
    cache = cached_out[0]
    last_edges = jnp.stack([k[-1, -EDGE:], v[-1, -EDGE:]])
    first_edges = jnp.stack([k[0, :EDGE], v[0, :EDGE]])
    from_above = shifted(last_edges, "space", 1)
    from_below = shifted(first_edges, "space", -1)
    kp = jnp.concatenate([from_above[0][None], k[:-1, -EDGE:]], axis=0)
    vp = jnp.concatenate([from_above[1][None], v[:-1, -EDGE:]], axis=0)
    kn = jnp.concatenate([k[1:, :EDGE], from_below[0][None]], axis=0)
    vn = jnp.concatenate([v[1:, :EDGE], from_below[1][None]], axis=0)
    total_tiles = tile_count * lax.axis_size("space")
    tile_index = lax.axis_index("space") * tile_count + jnp.arange(tile_count, dtype=jnp.int32)
    flags = jnp.stack([refreshed[0].astype(jnp.int32),
                       (tile_index > 0).astype(jnp.int32),
                       (tile_index < total_tiles - 1).astype(jnp.int32)], axis=1)
    ke = jnp.concatenate([kp, kn], axis=1)
    ve = jnp.concatenate([vp, vn], axis=1)
    hidden, normed = spatial_block(flags, q, k, v, ke, ve, lat, cache, out_weight)

    n = lax.axis_size("frames")
    chips = n // 2
    chunk = tok_count // n
    me = lax.axis_index("frames")
    dests = {o: frame_dest(me, o[0], o[1], chips) for o in OFFSETS}
    send = {o: lax.dynamic_slice_in_dim(normed, dests[o] * chunk, chunk, axis=1) for o in OFFSETS}
    recv = exchange(send, n)
    own = lax.dynamic_slice_in_dim(normed, me * chunk, chunk, axis=1)
    block = jnp.stack([own] + [recv[o] for o in OFFSETS])
    fids = jnp.stack([me] + [dests[o] for o in OFFSETS]).astype(jnp.int32)
    rows = tile_count * chunk
    flat = jnp.dot(block.reshape(-1, width), temporal_weight,
                   preferred_element_type=jnp.float32).astype(jnp.bfloat16)
    packed = flat.reshape(n, rows, 3 * width)
    attended = temporal_attend(packed, band_width, fids)
    attended = attended.reshape(n, tile_count, chunk, width)
    back = exchange({o: attended[1 + i] for i, o in enumerate(OFFSETS)}, n)
    temporal = lax.dynamic_update_slice_in_dim(
        jnp.zeros_like(hidden), attended[0], me * chunk, axis=1)
    for o in OFFSETS:
        temporal = lax.dynamic_update_slice_in_dim(temporal, back[o], dests[o] * chunk, axis=1)
    mixed = (hidden.astype(jnp.float32) + temporal.astype(jnp.float32)).astype(jnp.bfloat16)
    return mixed[None]


def solution(mesh):
    return jax.shard_map(
        local,
        mesh=mesh,
        in_specs=(
            P("frames", "space", None, None),
            P("frames", "space", None, None),
            P("frames", "space", None, None),
            P("frames", "space", None, None),
            P("frames", "space", None, None),
            P("frames", "space"),
            P(),
            P(),
            P(),
        ),
        out_specs=P("frames", "space", None, None),
        check_vma=False,
    )
```

```python
import functools
import math

import jax
import jax.numpy as jnp
from jax import lax
from jax.experimental import pallas as pl
from jax.experimental.pallas import tpu as pltpu
from jax.sharding import PartitionSpec as P

EDGE = 64
HEADS = 16


def shifted(block, axis, distance):
    devices = range(lax.axis_size(axis))
    route = [(i - distance, i) for i in devices if i - distance in devices]
    return lax.ppermute(block, axis, route)


def head_window(h, head_dim, width):
    lo = h * head_dim
    start = min((lo // 128) * 128, width - 256)
    return lo, start


def spatial_kernel(flags_ref, q_ref, k_ref, v_ref, ke_ref, ve_ref,
                   lat_ref, cache_ref, wo_ref, hid_ref, nrm_ref, acc_ref, sp_ref):
    i = pl.program_id(0)
    refreshed = flags_ref[i, 0]
    prev_ok = flags_ref[i, 1]
    next_ok = flags_ref[i, 2]
    width = q_ref.shape[-1]
    head_dim = width // HEADS
    scaling = 1.0 / math.sqrt(head_dim)
    nt = (((1,), (1,)), ((), ()))

    @pl.when(refreshed == 1)
    def _():
        acc_ref[...] = jnp.zeros_like(acc_ref)
        edge_lane = lax.broadcasted_iota(jnp.int32, (1, 2 * EDGE), 1)
        edge_ok = jnp.where(edge_lane < EDGE, prev_ok, next_ok) == 1
        for h in range(HEADS):
            lo, start = head_window(h, head_dim, width)
            win = pl.ds(start, 256)
            lane = lax.broadcasted_iota(jnp.int32, (1, 256), 1) + start
            mask = (lane >= lo) & (lane < lo + head_dim)
            qh = jnp.where(mask, q_ref[0, :, win], jnp.zeros((), q_ref.dtype))
            s_mid = lax.dot_general(qh, k_ref[0, :, win], nt,
                                    preferred_element_type=jnp.float32) * scaling
            s_edge = lax.dot_general(qh, ke_ref[0, :, win], nt,
                                     preferred_element_type=jnp.float32) * scaling
            s_edge = jnp.where(edge_ok, s_edge, -jnp.inf)
            top = jnp.maximum(jnp.max(s_mid, axis=1, keepdims=True),
                              jnp.max(s_edge, axis=1, keepdims=True))
            e_mid = jnp.exp(s_mid - top)
            e_edge = jnp.exp(s_edge - top)
            total = (jnp.sum(e_mid, axis=1, keepdims=True)
                     + jnp.sum(e_edge, axis=1, keepdims=True))
            inv = 1.0 / total
            p_mid = (e_mid * inv).astype(jnp.bfloat16)
            p_edge = (e_edge * inv).astype(jnp.bfloat16)
            out = jnp.dot(p_mid, v_ref[0, :, win], preferred_element_type=jnp.float32)
            out = out + jnp.dot(p_edge, ve_ref[0, :, win], preferred_element_type=jnp.float32)
            acc_ref[:, win] += jnp.where(mask, out, 0.0)
        sp_ref[...] = acc_ref[...].astype(sp_ref.dtype)

    @pl.when(refreshed != 1)
    def _():
        sp_ref[...] = cache_ref[0]

    projected = jnp.dot(sp_ref[...], wo_ref[...], preferred_element_type=jnp.float32)
    hidden = (lat_ref[0].astype(jnp.float32) + projected).astype(jnp.bfloat16)
    hid_ref[0] = hidden
    h32 = hidden.astype(jnp.float32)
    ms = jnp.mean(h32 * h32, axis=-1, keepdims=True)
    nrm_ref[0] = (h32 * lax.rsqrt(ms + 1e-06)).astype(nrm_ref.dtype)


def spatial_block(flags, q, k, v, ke, ve, lat, cache, wo):
    tiles, tok, width = q.shape
    tile_spec = pl.BlockSpec((1, tok, width), lambda i, f: (i, 0, 0))
    edge_spec = pl.BlockSpec((1, 2 * EDGE, width), lambda i, f: (i, 0, 0))
    w_spec = pl.BlockSpec((width, width), lambda i, f: (0, 0))
    out_shape = [jax.ShapeDtypeStruct((tiles, tok, width), jnp.bfloat16)] * 2
    flops = tiles * (HEADS * 4 * tok * (tok + 2 * EDGE) * 256 + 2 * tok * width * width)
    cost = pl.CostEstimate(flops=flops, transcendentals=tiles * HEADS * tok * (tok + 2 * EDGE),
                           bytes_accessed=2 * (7 * tiles * tok * width + width * width))
    return pl.pallas_call(
        spatial_kernel,
        grid_spec=pltpu.PrefetchScalarGridSpec(
            num_scalar_prefetch=1,
            grid=(tiles,),
            in_specs=[tile_spec] * 3 + [edge_spec] * 2 + [tile_spec] * 2 + [w_spec],
            out_specs=[tile_spec, tile_spec],
            scratch_shapes=[pltpu.VMEM((tok, width), jnp.float32),
                            pltpu.VMEM((tok, width), jnp.bfloat16)],
        ),
        out_shape=out_shape,
        compiler_params=pltpu.CompilerParams(dimension_semantics=("arbitrary",),
                                             vmem_limit_bytes=48 * 1024 * 1024),
        cost_estimate=cost,
    )(flags, q, k, v, ke, ve, lat, cache, wo)


def temporal_kernel(qid_ref, fid_ref, bw_ref, q_ref, k_ref, v_ref, ind_ref, indt_ref, o_ref,
                    k32_ref, v32_ref):
    frames, tok, width = k_ref.shape
    queries = q_ref.shape[0]
    k32_ref[...] = k_ref[...].astype(jnp.float32)
    v32_ref[...] = v_ref[...].astype(jnp.float32)
    head_dim = width // HEADS
    scaling = 1.0 / math.sqrt(head_dim)
    bw = bw_ref[...].reshape(1, 1, HEADS)
    ind = ind_ref[...]
    indt = indt_ref[...]
    fids = jnp.concatenate(
        [jnp.full((1, 1, 1), fid_ref[g], jnp.int32) for g in range(frames)], axis=0)

    def body(f, carry):
        qf = q_ref[f].astype(jnp.float32)
        prod = (qf[None] * k32_ref[...]).reshape(frames * tok, width)
        hi = prod.astype(jnp.bfloat16)
        lo = (prod - hi.astype(jnp.float32)).astype(jnp.bfloat16)
        s = (jnp.dot(hi, ind, preferred_element_type=jnp.float32)
             + jnp.dot(lo, ind, preferred_element_type=jnp.float32))
        s = s.reshape(frames, tok, HEADS) * scaling
        allowed = jnp.abs(fids - qid_ref[f]) <= bw
        s = jnp.where(allowed, s, -jnp.inf)
        top = jnp.max(s, axis=0, keepdims=True)
        expo = jnp.exp(s - top)
        total = jnp.sum(expo, axis=0, keepdims=True)
        p = (expo / total).astype(jnp.bfloat16).reshape(frames * tok, HEADS)
        wide = jnp.dot(p, indt, preferred_element_type=jnp.float32).reshape(frames, tok, width)
        out = jnp.sum(wide * v32_ref[...], axis=0)
        o_ref[f] = out.astype(o_ref.dtype)
        return carry

    lax.fori_loop(0, queries, body, 0)


def temporal_attend(packed, band_width, fids, first, count):
    frames, tok, wide = packed.shape
    width = wide // 3
    q = packed[first:first + count, :, :width]
    k = packed[..., width:2 * width]
    v = packed[..., 2 * width:]
    head_dim = width // HEADS
    ind = (jnp.arange(width, dtype=jnp.int32)[:, None] // head_dim
           == jnp.arange(HEADS, dtype=jnp.int32)[None, :])
    vspec = pl.BlockSpec(memory_space=pltpu.VMEM)
    sspec = pl.BlockSpec(memory_space=pltpu.SMEM)
    cost = pl.CostEstimate(flops=count * frames * tok * width * 40,
                           transcendentals=count * frames * tok * HEADS,
                           bytes_accessed=2 * (2 * frames + 2 * count) * tok * width)
    return pl.pallas_call(
        temporal_kernel,
        in_specs=[sspec, sspec] + [vspec] * 6,
        out_specs=vspec,
        out_shape=jax.ShapeDtypeStruct((count, tok, width), jnp.bfloat16),
        scratch_shapes=[pltpu.VMEM((frames, tok, width), jnp.float32)] * 2,
        compiler_params=pltpu.CompilerParams(vmem_limit_bytes=48 * 1024 * 1024),
        cost_estimate=cost,
    )(fids[first:first + count], fids, band_width.reshape(1, HEADS), q, k, v,
      ind.astype(jnp.bfloat16), ind.T.astype(jnp.bfloat16))


OFFSETS = ((0, 1), (-1, 0), (-1, 1), (1, 0), (1, 1), (2, 0), (2, 1))


def frame_dest(d, dy, dc, chips):
    return ((d // 2 + dy) % chips) * 2 + ((d % 2) ^ dc)


def frame_perm(dy, dc, n):
    chips = n // 2
    return [(d, frame_dest(d, dy, dc, chips)) for d in range(n)]


def exchange(send, n):
    recv = {}
    recv[(0, 1)] = lax.ppermute(send[(0, 1)], "frames", frame_perm(0, 1, n))
    for dc in (0, 1):
        recv[(-1, dc)] = lax.ppermute(send[(1, dc)], "frames", frame_perm(1, dc, n))
        recv[(1, dc)] = lax.ppermute(send[(-1, dc)], "frames", frame_perm(-1, dc, n))
    hop = lax.ppermute(send[(2, 0)], "frames", frame_perm(1, 0, n))
    recv[(2, 0)] = lax.ppermute(hop, "frames", frame_perm(1, 0, n))
    hop = lax.ppermute(send[(2, 1)], "frames", frame_perm(-1, 0, n))
    recv[(2, 1)] = lax.ppermute(hop, "frames", frame_perm(-1, 1, n))
    return recv


def local(latent, query_rows, key_rows, value_rows, cached_out, refreshed, band_width,
          out_weight, temporal_weight):
    _, tile_count, tok_count, width = latent.shape
    lat = latent[0]
    q = query_rows[0]
    k = key_rows[0]
    v = value_rows[0]
    cache = cached_out[0]
    last_edges = jnp.stack([k[-1, -EDGE:], v[-1, -EDGE:]])
    first_edges = jnp.stack([k[0, :EDGE], v[0, :EDGE]])
    from_above = shifted(last_edges, "space", 1)
    from_below = shifted(first_edges, "space", -1)
    kp = jnp.concatenate([from_above[0][None], k[:-1, -EDGE:]], axis=0)
    vp = jnp.concatenate([from_above[1][None], v[:-1, -EDGE:]], axis=0)
    kn = jnp.concatenate([k[1:, :EDGE], from_below[0][None]], axis=0)
    vn = jnp.concatenate([v[1:, :EDGE], from_below[1][None]], axis=0)
    total_tiles = tile_count * lax.axis_size("space")
    tile_index = lax.axis_index("space") * tile_count + jnp.arange(tile_count, dtype=jnp.int32)
    flags = jnp.stack([refreshed[0].astype(jnp.int32),
                       (tile_index > 0).astype(jnp.int32),
                       (tile_index < total_tiles - 1).astype(jnp.int32)], axis=1)
    ke = jnp.concatenate([kp, kn], axis=1)
    ve = jnp.concatenate([vp, vn], axis=1)
    hidden, normed = spatial_block(flags, q, k, v, ke, ve, lat, cache, out_weight)

    n = lax.axis_size("frames")
    chips = n // 2
    chunk = tok_count // n
    me = lax.axis_index("frames")
    dests = {o: frame_dest(me, o[0], o[1], chips) for o in OFFSETS}
    send = {o: lax.dynamic_slice_in_dim(normed, dests[o] * chunk, chunk, axis=1) for o in OFFSETS}
    recv = exchange(send, n)
    own = lax.dynamic_slice_in_dim(normed, me * chunk, chunk, axis=1)
    block = jnp.stack([own] + [recv[o] for o in OFFSETS])
    fids = jnp.stack([me] + [dests[o] for o in OFFSETS]).astype(jnp.int32)
    rows = tile_count * chunk
    flat = jnp.dot(block.reshape(-1, width), temporal_weight,
                   preferred_element_type=jnp.float32).astype(jnp.bfloat16)
    packed = flat.reshape(n, rows, 3 * width)
    far = temporal_attend(packed, band_width, fids, n - 2, 2)
    near = temporal_attend(packed, band_width, fids, 0, n - 2)
    attended = jnp.concatenate([near, far], axis=0).reshape(n, tile_count, chunk, width)
    back = exchange({o: attended[1 + i] for i, o in enumerate(OFFSETS)}, n)
    temporal = lax.dynamic_update_slice_in_dim(
        jnp.zeros_like(hidden), attended[0], me * chunk, axis=1)
    for o in OFFSETS:
        temporal = lax.dynamic_update_slice_in_dim(temporal, back[o], dests[o] * chunk, axis=1)
    mixed = (hidden.astype(jnp.float32) + temporal.astype(jnp.float32)).astype(jnp.bfloat16)
    return mixed[None]


def solution(mesh):
    return jax.shard_map(
        local,
        mesh=mesh,
        in_specs=(
            P("frames", "space", None, None),
            P("frames", "space", None, None),
            P("frames", "space", None, None),
            P("frames", "space", None, None),
            P("frames", "space", None, None),
            P("frames", "space"),
            P(),
            P(),
            P(),
        ),
        out_specs=P("frames", "space", None, None),
        check_vma=False,
    )
```

```python
import functools
import math

import jax
import jax.numpy as jnp
from jax import lax
from jax.experimental import pallas as pl
from jax.experimental.pallas import tpu as pltpu
from jax.sharding import PartitionSpec as P

EDGE = 64
HEADS = 16


def shifted(block, axis, distance):
    devices = range(lax.axis_size(axis))
    route = [(i - distance, i) for i in devices if i - distance in devices]
    return lax.ppermute(block, axis, route)


def head_window(h, head_dim, width):
    lo = h * head_dim
    start = min((lo // 128) * 128, width - 256)
    return lo, start


def spatial_kernel(flags_ref, q_ref, k_ref, v_ref, ke_ref, ve_ref,
                   lat_ref, cache_ref, wo_ref, hid_ref, nrm_ref, acc_ref, sp_ref):
    i = pl.program_id(0)
    refreshed = flags_ref[i, 0]
    prev_ok = flags_ref[i, 1]
    next_ok = flags_ref[i, 2]
    width = q_ref.shape[-1]
    head_dim = width // HEADS
    scaling = 1.0 / math.sqrt(head_dim)
    nt = (((1,), (1,)), ((), ()))

    @pl.when(refreshed == 1)
    def _():
        acc_ref[...] = jnp.zeros_like(acc_ref)
        edge_lane = lax.broadcasted_iota(jnp.int32, (1, 2 * EDGE), 1)
        edge_ok = jnp.where(edge_lane < EDGE, prev_ok, next_ok) == 1
        for h in range(HEADS):
            lo, start = head_window(h, head_dim, width)
            win = pl.ds(start, 256)
            lane = lax.broadcasted_iota(jnp.int32, (1, 256), 1) + start
            mask = (lane >= lo) & (lane < lo + head_dim)
            qh = jnp.where(mask, q_ref[0, :, win], jnp.zeros((), q_ref.dtype))
            s_mid = lax.dot_general(qh, k_ref[0, :, win], nt,
                                    preferred_element_type=jnp.float32) * scaling
            s_edge = lax.dot_general(qh, ke_ref[0, :, win], nt,
                                     preferred_element_type=jnp.float32) * scaling
            s_edge = jnp.where(edge_ok, s_edge, -jnp.inf)
            top = jnp.maximum(jnp.max(s_mid, axis=1, keepdims=True),
                              jnp.max(s_edge, axis=1, keepdims=True))
            e_mid = jnp.exp(s_mid - top)
            e_edge = jnp.exp(s_edge - top)
            total = (jnp.sum(e_mid, axis=1, keepdims=True)
                     + jnp.sum(e_edge, axis=1, keepdims=True))
            inv = 1.0 / total
            p_mid = (e_mid * inv).astype(jnp.bfloat16)
            p_edge = (e_edge * inv).astype(jnp.bfloat16)
            out = jnp.dot(p_mid, v_ref[0, :, win], preferred_element_type=jnp.float32)
            out = out + jnp.dot(p_edge, ve_ref[0, :, win], preferred_element_type=jnp.float32)
            acc_ref[:, win] += jnp.where(mask, out, 0.0)
        sp_ref[...] = acc_ref[...].astype(sp_ref.dtype)

    @pl.when(refreshed != 1)
    def _():
        sp_ref[...] = cache_ref[0]

    projected = jnp.dot(sp_ref[...], wo_ref[...], preferred_element_type=jnp.float32)
    hidden = (lat_ref[0].astype(jnp.float32) + projected).astype(jnp.bfloat16)
    hid_ref[0] = hidden
    h32 = hidden.astype(jnp.float32)
    ms = jnp.mean(h32 * h32, axis=-1, keepdims=True)
    nrm_ref[0] = (h32 * lax.rsqrt(ms + 1e-06)).astype(nrm_ref.dtype)


def spatial_block(flags, q, k, v, ke, ve, lat, cache, wo):
    tiles, tok, width = q.shape
    tile_spec = pl.BlockSpec((1, tok, width), lambda i, f: (i, 0, 0))
    edge_spec = pl.BlockSpec((1, 2 * EDGE, width), lambda i, f: (i, 0, 0))
    w_spec = pl.BlockSpec((width, width), lambda i, f: (0, 0))
    out_shape = [jax.ShapeDtypeStruct((tiles, tok, width), jnp.bfloat16)] * 2
    flops = tiles * (HEADS * 4 * tok * (tok + 2 * EDGE) * 256 + 2 * tok * width * width)
    cost = pl.CostEstimate(flops=flops, transcendentals=tiles * HEADS * tok * (tok + 2 * EDGE),
                           bytes_accessed=2 * (7 * tiles * tok * width + width * width))
    return pl.pallas_call(
        spatial_kernel,
        grid_spec=pltpu.PrefetchScalarGridSpec(
            num_scalar_prefetch=1,
            grid=(tiles,),
            in_specs=[tile_spec] * 3 + [edge_spec] * 2 + [tile_spec] * 2 + [w_spec],
            out_specs=[tile_spec, tile_spec],
            scratch_shapes=[pltpu.VMEM((tok, width), jnp.float32),
                            pltpu.VMEM((tok, width), jnp.bfloat16)],
        ),
        out_shape=out_shape,
        compiler_params=pltpu.CompilerParams(dimension_semantics=("arbitrary",),
                                             vmem_limit_bytes=48 * 1024 * 1024),
        cost_estimate=cost,
    )(flags, q, k, v, ke, ve, lat, cache, wo)


def temporal_kernel(fid_ref, bw_ref, q_ref, k_ref, v_ref, ind_ref, indt_ref, o_ref):
    frames, tok, width = q_ref.shape
    head_dim = width // HEADS
    scaling = 1.0 / math.sqrt(head_dim)
    bw = bw_ref[...].reshape(1, 1, HEADS)
    ind = ind_ref[...]
    indt = indt_ref[...]
    fids = jnp.concatenate(
        [jnp.full((1, 1, 1), fid_ref[g], jnp.int32) for g in range(frames)], axis=0)

    def body(f, carry):
        qf = q_ref[f].astype(jnp.float32)
        prod = (qf[None] * k_ref[...].astype(jnp.float32)).reshape(frames * tok, width)
        hi = prod.astype(jnp.bfloat16)
        lo = (prod - hi.astype(jnp.float32)).astype(jnp.bfloat16)
        s = (jnp.dot(hi, ind, preferred_element_type=jnp.float32)
             + jnp.dot(lo, ind, preferred_element_type=jnp.float32))
        s = s.reshape(frames, tok, HEADS) * scaling
        allowed = jnp.abs(fids - fid_ref[f]) <= bw
        s = jnp.where(allowed, s, -jnp.inf)
        top = jnp.max(s, axis=0, keepdims=True)
        expo = jnp.exp(s - top)
        total = jnp.sum(expo, axis=0, keepdims=True)
        p = (expo / total).astype(jnp.bfloat16).reshape(frames * tok, HEADS)
        wide = jnp.dot(p, indt, preferred_element_type=jnp.float32).reshape(frames, tok, width)
        out = jnp.sum(wide * v_ref[...].astype(jnp.float32), axis=0)
        o_ref[f] = out.astype(o_ref.dtype)
        return carry

    lax.fori_loop(0, frames, body, 0)


def temporal_attend(packed, band_width, fids):
    frames, tok, wide = packed.shape
    width = wide // 3
    q = packed[..., :width]
    k = packed[..., width:2 * width]
    v = packed[..., 2 * width:]
    head_dim = width // HEADS
    ind = (jnp.arange(width, dtype=jnp.int32)[:, None] // head_dim
           == jnp.arange(HEADS, dtype=jnp.int32)[None, :])
    vspec = pl.BlockSpec(memory_space=pltpu.VMEM)
    sspec = pl.BlockSpec(memory_space=pltpu.SMEM)
    cost = pl.CostEstimate(flops=frames * frames * tok * width * 40,
                           transcendentals=frames * frames * tok * HEADS,
                           bytes_accessed=2 * 4 * frames * tok * width)
    return pl.pallas_call(
        temporal_kernel,
        in_specs=[sspec] + [vspec] * 6,
        out_specs=vspec,
        out_shape=jax.ShapeDtypeStruct((frames, tok, width), jnp.bfloat16),
        compiler_params=pltpu.CompilerParams(vmem_limit_bytes=48 * 1024 * 1024),
        cost_estimate=cost,
    )(fids, band_width.reshape(1, HEADS), q, k, v, ind.astype(jnp.bfloat16),
      ind.T.astype(jnp.bfloat16))


OFFSETS = ((0, 1), (-1, 0), (-1, 1), (1, 0), (1, 1), (2, 0), (2, 1))


def frame_dest(d, dy, dc, chips):
    return ((d // 2 + dy) % chips) * 2 + ((d % 2) ^ dc)


def frame_perm(dy, dc, n):
    chips = n // 2
    return [(d, frame_dest(d, dy, dc, chips)) for d in range(n)]


def exchange(send, n):
    recv = {}
    recv[(0, 1)] = lax.ppermute(send[(0, 1)], "frames", frame_perm(0, 1, n))
    for dc in (0, 1):
        recv[(-1, dc)] = lax.ppermute(send[(1, dc)], "frames", frame_perm(1, dc, n))
        recv[(1, dc)] = lax.ppermute(send[(-1, dc)], "frames", frame_perm(-1, dc, n))
    for dc in (0, 1):
        recv[(2, dc)] = lax.ppermute(send[(2, dc)], "frames", frame_perm(2, dc, n))
    return recv


def local(latent, query_rows, key_rows, value_rows, cached_out, refreshed, band_width,
          out_weight, temporal_weight):
    _, tile_count, tok_count, width = latent.shape
    lat = latent[0]
    q = query_rows[0]
    k = key_rows[0]
    v = value_rows[0]
    cache = cached_out[0]
    last_edges = jnp.stack([k[-1, -EDGE:], v[-1, -EDGE:]])
    first_edges = jnp.stack([k[0, :EDGE], v[0, :EDGE]])
    from_above = shifted(last_edges, "space", 1)
    from_below = shifted(first_edges, "space", -1)
    kp = jnp.concatenate([from_above[0][None], k[:-1, -EDGE:]], axis=0)
    vp = jnp.concatenate([from_above[1][None], v[:-1, -EDGE:]], axis=0)
    kn = jnp.concatenate([k[1:, :EDGE], from_below[0][None]], axis=0)
    vn = jnp.concatenate([v[1:, :EDGE], from_below[1][None]], axis=0)
    total_tiles = tile_count * lax.axis_size("space")
    tile_index = lax.axis_index("space") * tile_count + jnp.arange(tile_count, dtype=jnp.int32)
    flags = jnp.stack([refreshed[0].astype(jnp.int32),
                       (tile_index > 0).astype(jnp.int32),
                       (tile_index < total_tiles - 1).astype(jnp.int32)], axis=1)
    ke = jnp.concatenate([kp, kn], axis=1)
    ve = jnp.concatenate([vp, vn], axis=1)
    hidden, normed = spatial_block(flags, q, k, v, ke, ve, lat, cache, out_weight)

    n = lax.axis_size("frames")
    chips = n // 2
    chunk = tok_count // n
    me = lax.axis_index("frames")
    dests = {o: frame_dest(me, o[0], o[1], chips) for o in OFFSETS}
    send = {o: lax.dynamic_slice_in_dim(normed, dests[o] * chunk, chunk, axis=1) for o in OFFSETS}
    recv = exchange(send, n)
    own = lax.dynamic_slice_in_dim(normed, me * chunk, chunk, axis=1)
    block = jnp.stack([own] + [recv[o] for o in OFFSETS])
    fids = jnp.stack([me] + [dests[o] for o in OFFSETS]).astype(jnp.int32)
    rows = tile_count * chunk
    flat = jnp.dot(block.reshape(-1, width), temporal_weight,
                   preferred_element_type=jnp.float32).astype(jnp.bfloat16)
    packed = flat.reshape(n, rows, 3 * width)
    attended = temporal_attend(packed, band_width, fids)
    attended = attended.reshape(n, tile_count, chunk, width)
    back = exchange({o: attended[1 + i] for i, o in enumerate(OFFSETS)}, n)
    temporal = lax.dynamic_update_slice_in_dim(
        jnp.zeros_like(hidden), attended[0], me * chunk, axis=1)
    for o in OFFSETS:
        temporal = lax.dynamic_update_slice_in_dim(temporal, back[o], dests[o] * chunk, axis=1)
    mixed = (hidden.astype(jnp.float32) + temporal.astype(jnp.float32)).astype(jnp.bfloat16)
    return mixed[None]


def solution(mesh):
    return jax.shard_map(
        local,
        mesh=mesh,
        in_specs=(
            P("frames", "space", None, None),
            P("frames", "space", None, None),
            P("frames", "space", None, None),
            P("frames", "space", None, None),
            P("frames", "space", None, None),
            P("frames", "space"),
            P(),
            P(),
            P(),
        ),
        out_specs=P("frames", "space", None, None),
        check_vma=False,
    )
```

```python
import functools
import math

import jax
import jax.numpy as jnp
from jax import lax
from jax.experimental import pallas as pl
from jax.experimental.pallas import tpu as pltpu
from jax.sharding import PartitionSpec as P

EDGE = 64
HEADS = 16


def shifted(block, axis, distance):
    devices = range(lax.axis_size(axis))
    route = [(i - distance, i) for i in devices if i - distance in devices]
    return lax.ppermute(block, axis, route)


def head_window(h, head_dim, width):
    lo = h * head_dim
    start = min((lo // 128) * 128, width - 256)
    return lo, start


def spatial_kernel(flags_ref, q_ref, k_ref, v_ref, ke_ref, ve_ref,
                   lat_ref, cache_ref, wo_ref, hid_ref, nrm_ref, acc_ref, sp_ref):
    i = pl.program_id(0)
    refreshed = flags_ref[i, 0]
    prev_ok = flags_ref[i, 1]
    next_ok = flags_ref[i, 2]
    width = q_ref.shape[-1]
    head_dim = width // HEADS
    scaling = 1.0 / math.sqrt(head_dim)
    nt = (((1,), (1,)), ((), ()))

    @pl.when(refreshed == 1)
    def _():
        acc_ref[...] = jnp.zeros_like(acc_ref)
        edge_lane = lax.broadcasted_iota(jnp.int32, (1, 2 * EDGE), 1)
        edge_ok = jnp.where(edge_lane < EDGE, prev_ok, next_ok) == 1
        for h in range(HEADS):
            lo, start = head_window(h, head_dim, width)
            win = pl.ds(start, 256)
            lane = lax.broadcasted_iota(jnp.int32, (1, 256), 1) + start
            mask = (lane >= lo) & (lane < lo + head_dim)
            qh = jnp.where(mask, q_ref[0, :, win], jnp.zeros((), q_ref.dtype))
            s_mid = lax.dot_general(qh, k_ref[0, :, win], nt,
                                    preferred_element_type=jnp.float32) * scaling
            s_edge = lax.dot_general(qh, ke_ref[0, :, win], nt,
                                     preferred_element_type=jnp.float32) * scaling
            s_edge = jnp.where(edge_ok, s_edge, -jnp.inf)
            top = jnp.maximum(jnp.max(s_mid, axis=1, keepdims=True),
                              jnp.max(s_edge, axis=1, keepdims=True))
            e_mid = jnp.exp(s_mid - top)
            e_edge = jnp.exp(s_edge - top)
            total = (jnp.sum(e_mid, axis=1, keepdims=True)
                     + jnp.sum(e_edge, axis=1, keepdims=True))
            inv = 1.0 / total
            p_mid = (e_mid * inv).astype(jnp.bfloat16)
            p_edge = (e_edge * inv).astype(jnp.bfloat16)
            out = jnp.dot(p_mid, v_ref[0, :, win], preferred_element_type=jnp.float32)
            out = out + jnp.dot(p_edge, ve_ref[0, :, win], preferred_element_type=jnp.float32)
            acc_ref[:, win] += jnp.where(mask, out, 0.0)
        sp_ref[...] = acc_ref[...].astype(sp_ref.dtype)

    @pl.when(refreshed != 1)
    def _():
        sp_ref[...] = cache_ref[0]

    projected = jnp.dot(sp_ref[...], wo_ref[...], preferred_element_type=jnp.float32)
    hidden = (lat_ref[0].astype(jnp.float32) + projected).astype(jnp.bfloat16)
    hid_ref[0] = hidden
    h32 = hidden.astype(jnp.float32)
    ms = jnp.mean(h32 * h32, axis=-1, keepdims=True)
    nrm_ref[0] = (h32 * lax.rsqrt(ms + 1e-06)).astype(nrm_ref.dtype)


def spatial_block(flags, q, k, v, ke, ve, lat, cache, wo):
    tiles, tok, width = q.shape
    tile_spec = pl.BlockSpec((1, tok, width), lambda i, f: (i, 0, 0))
    edge_spec = pl.BlockSpec((1, 2 * EDGE, width), lambda i, f: (i, 0, 0))
    w_spec = pl.BlockSpec((width, width), lambda i, f: (0, 0))
    out_shape = [jax.ShapeDtypeStruct((tiles, tok, width), jnp.bfloat16)] * 2
    flops = tiles * (HEADS * 4 * tok * (tok + 2 * EDGE) * 256 + 2 * tok * width * width)
    cost = pl.CostEstimate(flops=flops, transcendentals=tiles * HEADS * tok * (tok + 2 * EDGE),
                           bytes_accessed=2 * (7 * tiles * tok * width + width * width))
    return pl.pallas_call(
        spatial_kernel,
        grid_spec=pltpu.PrefetchScalarGridSpec(
            num_scalar_prefetch=1,
            grid=(tiles,),
            in_specs=[tile_spec] * 3 + [edge_spec] * 2 + [tile_spec] * 2 + [w_spec],
            out_specs=[tile_spec, tile_spec],
            scratch_shapes=[pltpu.VMEM((tok, width), jnp.float32),
                            pltpu.VMEM((tok, width), jnp.bfloat16)],
        ),
        out_shape=out_shape,
        compiler_params=pltpu.CompilerParams(dimension_semantics=("arbitrary",),
                                             vmem_limit_bytes=48 * 1024 * 1024),
        cost_estimate=cost,
    )(flags, q, k, v, ke, ve, lat, cache, wo)


def temporal_kernel(fid_ref, bw_ref, q_ref, k_ref, v_ref, ind_ref, indt_ref, o_ref):
    frames, tok, width = q_ref.shape
    head_dim = width // HEADS
    scaling = 1.0 / math.sqrt(head_dim)
    bw = bw_ref[...].reshape(1, 1, HEADS)
    ind = ind_ref[...]
    indt = indt_ref[...]
    fids = jnp.concatenate(
        [jnp.full((1, 1, 1), fid_ref[g], jnp.int32) for g in range(frames)], axis=0)

    def body(f, carry):
        qf = q_ref[f].astype(jnp.float32)
        prod = (qf[None] * k_ref[...].astype(jnp.float32)).reshape(frames * tok, width)
        hi = prod.astype(jnp.bfloat16)
        lo = (prod - hi.astype(jnp.float32)).astype(jnp.bfloat16)
        s = (jnp.dot(hi, ind, preferred_element_type=jnp.float32)
             + jnp.dot(lo, ind, preferred_element_type=jnp.float32))
        s = s.reshape(frames, tok, HEADS) * scaling
        allowed = jnp.abs(fids - fid_ref[f]) <= bw
        s = jnp.where(allowed, s, -jnp.inf)
        top = jnp.max(s, axis=0, keepdims=True)
        expo = jnp.exp(s - top)
        total = jnp.sum(expo, axis=0, keepdims=True)
        p = (expo / total).astype(jnp.bfloat16).reshape(frames * tok, HEADS)
        wide = jnp.dot(p, indt, preferred_element_type=jnp.float32).reshape(frames, tok, width)
        out = jnp.sum(wide * v_ref[...].astype(jnp.float32), axis=0)
        o_ref[f] = out.astype(o_ref.dtype)
        return carry

    lax.fori_loop(0, frames, body, 0)


def temporal_attend(packed, band_width, fids):
    frames, tok, wide = packed.shape
    width = wide // 3
    q = packed[..., :width]
    k = packed[..., width:2 * width]
    v = packed[..., 2 * width:]
    head_dim = width // HEADS
    ind = (jnp.arange(width, dtype=jnp.int32)[:, None] // head_dim
           == jnp.arange(HEADS, dtype=jnp.int32)[None, :])
    vspec = pl.BlockSpec(memory_space=pltpu.VMEM)
    sspec = pl.BlockSpec(memory_space=pltpu.SMEM)
    cost = pl.CostEstimate(flops=frames * frames * tok * width * 40,
                           transcendentals=frames * frames * tok * HEADS,
                           bytes_accessed=2 * 4 * frames * tok * width)
    return pl.pallas_call(
        temporal_kernel,
        in_specs=[sspec] + [vspec] * 6,
        out_specs=vspec,
        out_shape=jax.ShapeDtypeStruct((frames, tok, width), jnp.bfloat16),
        compiler_params=pltpu.CompilerParams(vmem_limit_bytes=48 * 1024 * 1024),
        cost_estimate=cost,
    )(fids, band_width.reshape(1, HEADS), q, k, v, ind.astype(jnp.bfloat16),
      ind.T.astype(jnp.bfloat16))


OFFSETS = ((0, 1), (-1, 0), (-1, 1), (1, 0), (1, 1), (2, 0), (2, 1))


def frame_dest(d, dy, dc, chips):
    return ((d // 2 + dy) % chips) * 2 + ((d % 2) ^ dc)


def frame_perm(dy, dc, n):
    chips = n // 2
    return [(d, frame_dest(d, dy, dc, chips)) for d in range(n)]


def exchange(send, n):
    across = lax.ppermute(jnp.stack([send[(0, 1)], send[(1, 1)], send[(-1, 1)], send[(2, 1)]]),
                          "frames", frame_perm(0, 1, n))
    recv = {(0, 1): across[0]}
    for slot, dy in enumerate((1, -1, 2)):
        got = lax.ppermute(jnp.stack([send[(dy, 0)], across[1 + slot]]),
                           "frames", frame_perm(dy, 0, n))
        recv[(-dy if dy != 2 else 2, 0)] = got[0]
        recv[(-dy if dy != 2 else 2, 1)] = got[1]
    return recv


def local(latent, query_rows, key_rows, value_rows, cached_out, refreshed, band_width,
          out_weight, temporal_weight):
    _, tile_count, tok_count, width = latent.shape
    lat = latent[0]
    q = query_rows[0]
    k = key_rows[0]
    v = value_rows[0]
    cache = cached_out[0]
    last_edges = jnp.stack([k[-1, -EDGE:], v[-1, -EDGE:]])
    first_edges = jnp.stack([k[0, :EDGE], v[0, :EDGE]])
    from_above = shifted(last_edges, "space", 1)
    from_below = shifted(first_edges, "space", -1)
    kp = jnp.concatenate([from_above[0][None], k[:-1, -EDGE:]], axis=0)
    vp = jnp.concatenate([from_above[1][None], v[:-1, -EDGE:]], axis=0)
    kn = jnp.concatenate([k[1:, :EDGE], from_below[0][None]], axis=0)
    vn = jnp.concatenate([v[1:, :EDGE], from_below[1][None]], axis=0)
    total_tiles = tile_count * lax.axis_size("space")
    tile_index = lax.axis_index("space") * tile_count + jnp.arange(tile_count, dtype=jnp.int32)
    flags = jnp.stack([refreshed[0].astype(jnp.int32),
                       (tile_index > 0).astype(jnp.int32),
                       (tile_index < total_tiles - 1).astype(jnp.int32)], axis=1)
    ke = jnp.concatenate([kp, kn], axis=1)
    ve = jnp.concatenate([vp, vn], axis=1)
    hidden, normed = spatial_block(flags, q, k, v, ke, ve, lat, cache, out_weight)

    n = lax.axis_size("frames")
    chips = n // 2
    chunk = tok_count // n
    me = lax.axis_index("frames")
    dests = {o: frame_dest(me, o[0], o[1], chips) for o in OFFSETS}
    send = {o: lax.dynamic_slice_in_dim(normed, dests[o] * chunk, chunk, axis=1) for o in OFFSETS}
    recv = exchange(send, n)
    own = lax.dynamic_slice_in_dim(normed, me * chunk, chunk, axis=1)
    block = jnp.stack([own] + [recv[o] for o in OFFSETS])
    fids = jnp.stack([me] + [dests[o] for o in OFFSETS]).astype(jnp.int32)
    rows = tile_count * chunk
    flat = jnp.dot(block.reshape(-1, width), temporal_weight,
                   preferred_element_type=jnp.float32).astype(jnp.bfloat16)
    packed = flat.reshape(n, rows, 3 * width)
    attended = temporal_attend(packed, band_width, fids)
    attended = attended.reshape(n, tile_count, chunk, width)
    back = exchange({o: attended[1 + i] for i, o in enumerate(OFFSETS)}, n)
    temporal = lax.dynamic_update_slice_in_dim(
        jnp.zeros_like(hidden), attended[0], me * chunk, axis=1)
    for o in OFFSETS:
        temporal = lax.dynamic_update_slice_in_dim(temporal, back[o], dests[o] * chunk, axis=1)
    mixed = (hidden.astype(jnp.float32) + temporal.astype(jnp.float32)).astype(jnp.bfloat16)
    return mixed[None]


def solution(mesh):
    return jax.shard_map(
        local,
        mesh=mesh,
        in_specs=(
            P("frames", "space", None, None),
            P("frames", "space", None, None),
            P("frames", "space", None, None),
            P("frames", "space", None, None),
            P("frames", "space", None, None),
            P("frames", "space"),
            P(),
            P(),
            P(),
        ),
        out_specs=P("frames", "space", None, None),
        check_vma=False,
    )
```

```python
import functools
import math

import jax
import jax.numpy as jnp
from jax import lax
from jax.experimental import pallas as pl
from jax.experimental.pallas import tpu as pltpu
from jax.sharding import PartitionSpec as P

EDGE = 64
HEADS = 16


def shifted(block, axis, distance):
    devices = range(lax.axis_size(axis))
    route = [(i - distance, i) for i in devices if i - distance in devices]
    return lax.ppermute(block, axis, route)


def head_window(h, head_dim, width):
    lo = h * head_dim
    start = min((lo // 128) * 128, width - 256)
    return lo, start


def spatial_kernel(flags_ref, q_ref, k_ref, v_ref, ke_ref, ve_ref,
                   lat_ref, cache_ref, wo_ref, hid_ref, nrm_ref, acc_ref, sp_ref):
    i = pl.program_id(0)
    refreshed = flags_ref[i, 0]
    prev_ok = flags_ref[i, 1]
    next_ok = flags_ref[i, 2]
    width = q_ref.shape[-1]
    head_dim = width // HEADS
    scaling = 1.0 / math.sqrt(head_dim)
    nt = (((1,), (1,)), ((), ()))

    @pl.when(refreshed == 1)
    def _():
        acc_ref[...] = jnp.zeros_like(acc_ref)
        edge_lane = lax.broadcasted_iota(jnp.int32, (1, 2 * EDGE), 1)
        edge_ok = jnp.where(edge_lane < EDGE, prev_ok, next_ok) == 1
        for h in range(HEADS):
            lo, start = head_window(h, head_dim, width)
            win = pl.ds(start, 256)
            lane = lax.broadcasted_iota(jnp.int32, (1, 256), 1) + start
            mask = (lane >= lo) & (lane < lo + head_dim)
            qh = jnp.where(mask, q_ref[0, :, win], jnp.zeros((), q_ref.dtype))
            s_mid = lax.dot_general(qh, k_ref[0, :, win], nt,
                                    preferred_element_type=jnp.float32) * scaling
            s_edge = lax.dot_general(qh, ke_ref[0, :, win], nt,
                                     preferred_element_type=jnp.float32) * scaling
            s_edge = jnp.where(edge_ok, s_edge, -jnp.inf)
            top = jnp.maximum(jnp.max(s_mid, axis=1, keepdims=True),
                              jnp.max(s_edge, axis=1, keepdims=True))
            e_mid = jnp.exp(s_mid - top)
            e_edge = jnp.exp(s_edge - top)
            total = (jnp.sum(e_mid, axis=1, keepdims=True)
                     + jnp.sum(e_edge, axis=1, keepdims=True))
            inv = 1.0 / total
            p_mid = (e_mid * inv).astype(jnp.bfloat16)
            p_edge = (e_edge * inv).astype(jnp.bfloat16)
            out = jnp.dot(p_mid, v_ref[0, :, win], preferred_element_type=jnp.float32)
            out = out + jnp.dot(p_edge, ve_ref[0, :, win], preferred_element_type=jnp.float32)
            acc_ref[:, win] += jnp.where(mask, out, 0.0)
        sp_ref[...] = acc_ref[...].astype(sp_ref.dtype)

    @pl.when(refreshed != 1)
    def _():
        sp_ref[...] = cache_ref[0]

    projected = jnp.dot(sp_ref[...], wo_ref[...], preferred_element_type=jnp.float32)
    hidden = (lat_ref[0].astype(jnp.float32) + projected).astype(jnp.bfloat16)
    hid_ref[0] = hidden
    h32 = hidden.astype(jnp.float32)
    ms = jnp.mean(h32 * h32, axis=-1, keepdims=True)
    nrm_ref[0] = (h32 * lax.rsqrt(ms + 1e-06)).astype(nrm_ref.dtype)


def spatial_block(flags, q, k, v, ke, ve, lat, cache, wo):
    tiles, tok, width = q.shape
    tile_spec = pl.BlockSpec((1, tok, width), lambda i, f: (i, 0, 0))
    edge_spec = pl.BlockSpec((1, 2 * EDGE, width), lambda i, f: (i, 0, 0))
    w_spec = pl.BlockSpec((width, width), lambda i, f: (0, 0))
    out_shape = [jax.ShapeDtypeStruct((tiles, tok, width), jnp.bfloat16)] * 2
    flops = tiles * (HEADS * 4 * tok * (tok + 2 * EDGE) * 256 + 2 * tok * width * width)
    cost = pl.CostEstimate(flops=flops, transcendentals=tiles * HEADS * tok * (tok + 2 * EDGE),
                           bytes_accessed=2 * (7 * tiles * tok * width + width * width))
    return pl.pallas_call(
        spatial_kernel,
        grid_spec=pltpu.PrefetchScalarGridSpec(
            num_scalar_prefetch=1,
            grid=(tiles,),
            in_specs=[tile_spec] * 3 + [edge_spec] * 2 + [tile_spec] * 2 + [w_spec],
            out_specs=[tile_spec, tile_spec],
            scratch_shapes=[pltpu.VMEM((tok, width), jnp.float32),
                            pltpu.VMEM((tok, width), jnp.bfloat16)],
        ),
        out_shape=out_shape,
        compiler_params=pltpu.CompilerParams(dimension_semantics=("arbitrary",),
                                             vmem_limit_bytes=48 * 1024 * 1024),
        cost_estimate=cost,
    )(flags, q, k, v, ke, ve, lat, cache, wo)


def temporal_kernel(fid_ref, bw_ref, q_ref, k_ref, v_ref, ind_ref, indt_ref, o_ref):
    frames, tok, width = q_ref.shape
    head_dim = width // HEADS
    scaling = 1.0 / math.sqrt(head_dim)
    bw = bw_ref[...].reshape(1, 1, HEADS)
    ind = ind_ref[...]
    indt = indt_ref[...]
    fids = jnp.concatenate(
        [jnp.full((1, 1, 1), fid_ref[g], jnp.int32) for g in range(frames)], axis=0)

    def body(f, carry):
        qf = q_ref[f].astype(jnp.float32)
        prod = (qf[None] * k_ref[...].astype(jnp.float32)).reshape(frames * tok, width)
        hi = prod.astype(jnp.bfloat16)
        lo = (prod - hi.astype(jnp.float32)).astype(jnp.bfloat16)
        s = (jnp.dot(hi, ind, preferred_element_type=jnp.float32)
             + jnp.dot(lo, ind, preferred_element_type=jnp.float32))
        s = s.reshape(frames, tok, HEADS) * scaling
        allowed = jnp.abs(fids - fid_ref[f]) <= bw
        s = jnp.where(allowed, s, -jnp.inf)
        top = jnp.max(s, axis=0, keepdims=True)
        expo = jnp.exp(s - top)
        total = jnp.sum(expo, axis=0, keepdims=True)
        p = (expo / total).astype(jnp.bfloat16).reshape(frames * tok, HEADS)
        wide = jnp.dot(p, indt, preferred_element_type=jnp.float32).reshape(frames, tok, width)
        out = jnp.sum(wide * v_ref[...].astype(jnp.float32), axis=0)
        o_ref[f] = out.astype(o_ref.dtype)
        return carry

    lax.fori_loop(0, frames, body, 0)


def temporal_attend(packed, band_width, fids):
    frames, tok, wide = packed.shape
    width = wide // 3
    q = packed[..., :width]
    k = packed[..., width:2 * width]
    v = packed[..., 2 * width:]
    head_dim = width // HEADS
    ind = (jnp.arange(width, dtype=jnp.int32)[:, None] // head_dim
           == jnp.arange(HEADS, dtype=jnp.int32)[None, :])
    vspec = pl.BlockSpec(memory_space=pltpu.VMEM)
    sspec = pl.BlockSpec(memory_space=pltpu.SMEM)
    cost = pl.CostEstimate(flops=frames * frames * tok * width * 40,
                           transcendentals=frames * frames * tok * HEADS,
                           bytes_accessed=2 * 4 * frames * tok * width)
    return pl.pallas_call(
        temporal_kernel,
        in_specs=[sspec] + [vspec] * 6,
        out_specs=vspec,
        out_shape=jax.ShapeDtypeStruct((frames, tok, width), jnp.bfloat16),
        compiler_params=pltpu.CompilerParams(vmem_limit_bytes=48 * 1024 * 1024),
        cost_estimate=cost,
    )(fids, band_width.reshape(1, HEADS), q, k, v, ind.astype(jnp.bfloat16),
      ind.T.astype(jnp.bfloat16))


OFFSETS = ((0, 1), (-1, 0), (-1, 1), (1, 0), (1, 1), (2, 0), (2, 1))


def frame_dest(d, dy, dc, chips):
    return ((d // 2 + dy) % chips) * 2 + ((d % 2) ^ dc)


def frame_perm(dy, dc, n):
    chips = n // 2
    return [(d, frame_dest(d, dy, dc, chips)) for d in range(n)]


def exchange(send, n):
    recv = {}
    recv[(0, 1)] = lax.ppermute(send[(0, 1)], "frames", frame_perm(0, 1, n))
    for dc in (0, 1):
        recv[(-1, dc)] = lax.ppermute(send[(1, dc)], "frames", frame_perm(1, dc, n))
        recv[(1, dc)] = lax.ppermute(send[(-1, dc)], "frames", frame_perm(-1, dc, n))
    for dc in (0, 1):
        recv[(2, dc)] = lax.ppermute(send[(2, dc)], "frames", frame_perm(2, dc, n))
    return recv


def local(latent, query_rows, key_rows, value_rows, cached_out, refreshed, band_width,
          out_weight, temporal_weight):
    _, tile_count, tok_count, width = latent.shape
    lat = latent[0]
    q = query_rows[0]
    k = key_rows[0]
    v = value_rows[0]
    cache = cached_out[0]
    last_edges = jnp.stack([k[-1, -EDGE:], v[-1, -EDGE:]])
    first_edges = jnp.stack([k[0, :EDGE], v[0, :EDGE]])
    from_above = shifted(last_edges, "space", 1)
    from_below = shifted(first_edges, "space", -1)
    kp = jnp.concatenate([from_above[0][None], k[:-1, -EDGE:]], axis=0)
    vp = jnp.concatenate([from_above[1][None], v[:-1, -EDGE:]], axis=0)
    kn = jnp.concatenate([k[1:, :EDGE], from_below[0][None]], axis=0)
    vn = jnp.concatenate([v[1:, :EDGE], from_below[1][None]], axis=0)
    total_tiles = tile_count * lax.axis_size("space")
    tile_index = lax.axis_index("space") * tile_count + jnp.arange(tile_count, dtype=jnp.int32)
    flags = jnp.stack([refreshed[0].astype(jnp.int32),
                       (tile_index > 0).astype(jnp.int32),
                       (tile_index < total_tiles - 1).astype(jnp.int32)], axis=1)
    ke = jnp.concatenate([kp, kn], axis=1)
    ve = jnp.concatenate([vp, vn], axis=1)
    hidden, normed = spatial_block(flags, q, k, v, ke, ve, lat, cache, out_weight)

    n = lax.axis_size("frames")
    chips = n // 2
    chunk = tok_count // n
    me = lax.axis_index("frames")
    dests = {o: frame_dest(me, o[0], o[1], chips) for o in OFFSETS}
    send = {o: lax.dynamic_slice_in_dim(normed, dests[o] * chunk, chunk, axis=1) for o in OFFSETS}
    recv = exchange(send, n)
    own = lax.dynamic_slice_in_dim(normed, me * chunk, chunk, axis=1)
    fids = jnp.stack([me] + [dests[o] for o in OFFSETS]).astype(jnp.int32)
    rows = tile_count * chunk
    early = jnp.stack([own, recv[(0, 1)]])
    late = jnp.stack([recv[o] for o in OFFSETS[1:]])
    flat_early = jnp.dot(early.reshape(-1, width), temporal_weight,
                         preferred_element_type=jnp.float32).astype(jnp.bfloat16)
    flat_late = jnp.dot(late.reshape(-1, width), temporal_weight,
                        preferred_element_type=jnp.float32).astype(jnp.bfloat16)
    packed = jnp.concatenate([flat_early, flat_late], axis=0).reshape(n, rows, 3 * width)
    attended = temporal_attend(packed, band_width, fids)
    attended = attended.reshape(n, tile_count, chunk, width)
    back = exchange({o: attended[1 + i] for i, o in enumerate(OFFSETS)}, n)
    temporal = lax.dynamic_update_slice_in_dim(
        jnp.zeros_like(hidden), attended[0], me * chunk, axis=1)
    for o in OFFSETS:
        temporal = lax.dynamic_update_slice_in_dim(temporal, back[o], dests[o] * chunk, axis=1)
    mixed = (hidden.astype(jnp.float32) + temporal.astype(jnp.float32)).astype(jnp.bfloat16)
    return mixed[None]


def solution(mesh):
    return jax.shard_map(
        local,
        mesh=mesh,
        in_specs=(
            P("frames", "space", None, None),
            P("frames", "space", None, None),
            P("frames", "space", None, None),
            P("frames", "space", None, None),
            P("frames", "space", None, None),
            P("frames", "space"),
            P(),
            P(),
            P(),
        ),
        out_specs=P("frames", "space", None, None),
        check_vma=False,
    )
```

```python
import functools
import math

import jax
import jax.numpy as jnp
from jax import lax
from jax.experimental import pallas as pl
from jax.experimental.pallas import tpu as pltpu
from jax.sharding import PartitionSpec as P

EDGE = 64
HEADS = 16


def shifted(block, axis, distance):
    devices = range(lax.axis_size(axis))
    route = [(i - distance, i) for i in devices if i - distance in devices]
    return lax.ppermute(block, axis, route)


def head_window(h, head_dim, width):
    lo = h * head_dim
    start = min((lo // 128) * 128, width - 256)
    return lo, start


def spatial_kernel(flags_ref, q_ref, k_ref, v_ref, ke_ref, ve_ref,
                   lat_ref, cache_ref, wo_ref, hid_ref, nrm_ref, acc_ref, sp_ref):
    i = pl.program_id(0)
    refreshed = flags_ref[i, 0]
    prev_ok = flags_ref[i, 1]
    next_ok = flags_ref[i, 2]
    width = q_ref.shape[-1]
    head_dim = width // HEADS
    scaling = 1.0 / math.sqrt(head_dim)
    nt = (((1,), (1,)), ((), ()))

    @pl.when(refreshed == 1)
    def _():
        acc_ref[...] = jnp.zeros_like(acc_ref)
        edge_lane = lax.broadcasted_iota(jnp.int32, (1, 2 * EDGE), 1)
        edge_ok = jnp.where(edge_lane < EDGE, prev_ok, next_ok) == 1
        for h in range(HEADS):
            lo, start = head_window(h, head_dim, width)
            win = pl.ds(start, 256)
            lane = lax.broadcasted_iota(jnp.int32, (1, 256), 1) + start
            mask = (lane >= lo) & (lane < lo + head_dim)
            qh = jnp.where(mask, q_ref[0, :, win], jnp.zeros((), q_ref.dtype))
            s_mid = lax.dot_general(qh, k_ref[0, :, win], nt,
                                    preferred_element_type=jnp.float32) * scaling
            s_edge = lax.dot_general(qh, ke_ref[0, :, win], nt,
                                     preferred_element_type=jnp.float32) * scaling
            s_edge = jnp.where(edge_ok, s_edge, -jnp.inf)
            top = jnp.maximum(jnp.max(s_mid, axis=1, keepdims=True),
                              jnp.max(s_edge, axis=1, keepdims=True))
            e_mid = jnp.exp(s_mid - top)
            e_edge = jnp.exp(s_edge - top)
            total = (jnp.sum(e_mid, axis=1, keepdims=True)
                     + jnp.sum(e_edge, axis=1, keepdims=True))
            inv = 1.0 / total
            p_mid = (e_mid * inv).astype(jnp.bfloat16)
            p_edge = (e_edge * inv).astype(jnp.bfloat16)
            out = jnp.dot(p_mid, v_ref[0, :, win], preferred_element_type=jnp.float32)
            out = out + jnp.dot(p_edge, ve_ref[0, :, win], preferred_element_type=jnp.float32)
            acc_ref[:, win] += jnp.where(mask, out, 0.0)
        sp_ref[...] = acc_ref[...].astype(sp_ref.dtype)

    @pl.when(refreshed != 1)
    def _():
        sp_ref[...] = cache_ref[0]

    projected = jnp.dot(sp_ref[...], wo_ref[...], preferred_element_type=jnp.float32)
    hidden = (lat_ref[0].astype(jnp.float32) + projected).astype(jnp.bfloat16)
    hid_ref[0] = hidden
    h32 = hidden.astype(jnp.float32)
    ms = jnp.mean(h32 * h32, axis=-1, keepdims=True)
    nrm_ref[0] = (h32 * lax.rsqrt(ms + 1e-06)).astype(nrm_ref.dtype)


def spatial_block(flags, q, k, v, ke, ve, lat, cache, wo):
    tiles, tok, width = q.shape
    tile_spec = pl.BlockSpec((1, tok, width), lambda i, f: (i, 0, 0))
    edge_spec = pl.BlockSpec((1, 2 * EDGE, width), lambda i, f: (i, 0, 0))
    w_spec = pl.BlockSpec((width, width), lambda i, f: (0, 0))
    out_shape = [jax.ShapeDtypeStruct((tiles, tok, width), jnp.bfloat16)] * 2
    flops = tiles * (HEADS * 4 * tok * (tok + 2 * EDGE) * 256 + 2 * tok * width * width)
    cost = pl.CostEstimate(flops=flops, transcendentals=tiles * HEADS * tok * (tok + 2 * EDGE),
                           bytes_accessed=2 * (7 * tiles * tok * width + width * width))
    return pl.pallas_call(
        spatial_kernel,
        grid_spec=pltpu.PrefetchScalarGridSpec(
            num_scalar_prefetch=1,
            grid=(tiles,),
            in_specs=[tile_spec] * 3 + [edge_spec] * 2 + [tile_spec] * 2 + [w_spec],
            out_specs=[tile_spec, tile_spec],
            scratch_shapes=[pltpu.VMEM((tok, width), jnp.float32),
                            pltpu.VMEM((tok, width), jnp.bfloat16)],
        ),
        out_shape=out_shape,
        compiler_params=pltpu.CompilerParams(dimension_semantics=("arbitrary",),
                                             vmem_limit_bytes=48 * 1024 * 1024),
        cost_estimate=cost,
    )(flags, q, k, v, ke, ve, lat, cache, wo)


def temporal_kernel(fid_ref, bw_ref, q_ref, k_ref, v_ref, ind_ref, indt_ref, o_ref):
    frames, tok, width = q_ref.shape
    head_dim = width // HEADS
    scaling = 1.0 / math.sqrt(head_dim)
    bw = bw_ref[...].reshape(1, 1, HEADS)
    ind = ind_ref[...]
    indt = indt_ref[...]
    fids = jnp.concatenate(
        [jnp.full((1, 1, 1), fid_ref[g], jnp.int32) for g in range(frames)], axis=0)

    def body(f, carry):
        qf = q_ref[f].astype(jnp.float32)
        prod = (qf[None] * k_ref[...].astype(jnp.float32)).reshape(frames * tok, width)
        hi = prod.astype(jnp.bfloat16)
        lo = (prod - hi.astype(jnp.float32)).astype(jnp.bfloat16)
        s = (jnp.dot(hi, ind, preferred_element_type=jnp.float32)
             + jnp.dot(lo, ind, preferred_element_type=jnp.float32))
        s = s.reshape(frames, tok, HEADS) * scaling
        allowed = jnp.abs(fids - fid_ref[f]) <= bw
        s = jnp.where(allowed, s, -jnp.inf)
        top = jnp.max(s, axis=0, keepdims=True)
        expo = jnp.exp(s - top)
        total = jnp.sum(expo, axis=0, keepdims=True)
        p = (expo / total).astype(jnp.bfloat16).reshape(frames * tok, HEADS)
        wide = jnp.dot(p, indt, preferred_element_type=jnp.float32).reshape(frames, tok, width)
        out = jnp.sum(wide * v_ref[...].astype(jnp.float32), axis=0)
        o_ref[f] = out.astype(o_ref.dtype)
        return carry

    lax.fori_loop(0, frames, body, 0)


def temporal_attend(packed, band_width, fids):
    frames, tok, wide = packed.shape
    width = wide // 3
    q = packed[..., :width]
    k = packed[..., width:2 * width]
    v = packed[..., 2 * width:]
    head_dim = width // HEADS
    ind = (jnp.arange(width, dtype=jnp.int32)[:, None] // head_dim
           == jnp.arange(HEADS, dtype=jnp.int32)[None, :])
    vspec = pl.BlockSpec(memory_space=pltpu.VMEM)
    sspec = pl.BlockSpec(memory_space=pltpu.SMEM)
    cost = pl.CostEstimate(flops=frames * frames * tok * width * 40,
                           transcendentals=frames * frames * tok * HEADS,
                           bytes_accessed=2 * 4 * frames * tok * width)
    return pl.pallas_call(
        temporal_kernel,
        in_specs=[sspec] + [vspec] * 6,
        out_specs=vspec,
        out_shape=jax.ShapeDtypeStruct((frames, tok, width), jnp.bfloat16),
        compiler_params=pltpu.CompilerParams(vmem_limit_bytes=48 * 1024 * 1024),
        cost_estimate=cost,
    )(fids, band_width.reshape(1, HEADS), q, k, v, ind.astype(jnp.bfloat16),
      ind.T.astype(jnp.bfloat16))


OFFSETS = ((0, 1), (-1, 0), (-1, 1), (1, 0), (1, 1), (2, 0), (2, 1))


def frame_dest(d, dy, dc, chips):
    return ((d // 2 + dy) % chips) * 2 + ((d % 2) ^ dc)


def frame_perm(dy, dc, n):
    chips = n // 2
    return [(d, frame_dest(d, dy, dc, chips)) for d in range(n)]


def exchange(send, n):
    recv = {}
    recv[(0, 1)] = lax.ppermute(send[(0, 1)], "frames", frame_perm(0, 1, n))
    for dc in (0, 1):
        recv[(-1, dc)] = lax.ppermute(send[(1, dc)], "frames", frame_perm(1, dc, n))
        recv[(1, dc)] = lax.ppermute(send[(-1, dc)], "frames", frame_perm(-1, dc, n))
    for dc in (0, 1):
        recv[(2, dc)] = lax.ppermute(send[(2, dc)], "frames", frame_perm(2, dc, n))
    return recv


def local(latent, query_rows, key_rows, value_rows, cached_out, refreshed, band_width,
          out_weight, temporal_weight):
    _, tile_count, tok_count, width = latent.shape
    lat = latent[0]
    q = query_rows[0]
    k = key_rows[0]
    v = value_rows[0]
    cache = cached_out[0]
    last_edges = jnp.stack([k[-1, -EDGE:], v[-1, -EDGE:]])
    first_edges = jnp.stack([k[0, :EDGE], v[0, :EDGE]])
    from_above = shifted(last_edges, "space", 1)
    from_below = shifted(first_edges, "space", -1)
    kp = jnp.concatenate([from_above[0][None], k[:-1, -EDGE:]], axis=0)
    vp = jnp.concatenate([from_above[1][None], v[:-1, -EDGE:]], axis=0)
    kn = jnp.concatenate([k[1:, :EDGE], from_below[0][None]], axis=0)
    vn = jnp.concatenate([v[1:, :EDGE], from_below[1][None]], axis=0)
    total_tiles = tile_count * lax.axis_size("space")
    tile_index = lax.axis_index("space") * tile_count + jnp.arange(tile_count, dtype=jnp.int32)
    flags = jnp.stack([refreshed[0].astype(jnp.int32),
                       (tile_index > 0).astype(jnp.int32),
                       (tile_index < total_tiles - 1).astype(jnp.int32)], axis=1)
    ke = jnp.concatenate([kp, kn], axis=1)
    ve = jnp.concatenate([vp, vn], axis=1)
    hidden, normed = spatial_block(flags, q, k, v, ke, ve, lat, cache, out_weight)

    n = lax.axis_size("frames")
    chips = n // 2
    chunk = tok_count // n
    me = lax.axis_index("frames")
    dests = {o: frame_dest(me, o[0], o[1], chips) for o in OFFSETS}
    send = {o: lax.dynamic_slice_in_dim(normed, dests[o] * chunk, chunk, axis=1) for o in OFFSETS}
    recv = exchange(send, n)
    own = lax.dynamic_slice_in_dim(normed, me * chunk, chunk, axis=1)
    fids = jnp.stack([me] + [dests[o] for o in OFFSETS]).astype(jnp.int32)
    rows = tile_count * chunk
    early = jnp.stack([own, recv[(0, 1)]])
    late = jnp.stack([recv[o] for o in OFFSETS[1:]])
    flat_early = jnp.dot(early.reshape(-1, width), temporal_weight,
                         preferred_element_type=jnp.float32).astype(jnp.bfloat16)
    flat_late = jnp.dot(late.reshape(-1, width), temporal_weight,
                        preferred_element_type=jnp.float32).astype(jnp.bfloat16)
    packed = jnp.concatenate([flat_early, flat_late], axis=0).reshape(n, rows, 3 * width)
    attended = temporal_attend(packed, band_width, fids)
    attended = attended.reshape(n, tile_count, chunk, width)
    back = exchange({o: attended[1 + i] for i, o in enumerate(OFFSETS)}, n)
    def mix(out, piece, frame):
        part = lax.dynamic_slice_in_dim(hidden, frame * chunk, chunk, axis=1)
        total = (part.astype(jnp.float32) + piece.astype(jnp.float32)).astype(jnp.bfloat16)
        return lax.dynamic_update_slice_in_dim(out, total, frame * chunk, axis=1)

    mixed = mix(hidden, attended[0], me)
    for o in OFFSETS:
        mixed = mix(mixed, back[o], dests[o])
    return mixed[None]


def solution(mesh):
    return jax.shard_map(
        local,
        mesh=mesh,
        in_specs=(
            P("frames", "space", None, None),
            P("frames", "space", None, None),
            P("frames", "space", None, None),
            P("frames", "space", None, None),
            P("frames", "space", None, None),
            P("frames", "space"),
            P(),
            P(),
            P(),
        ),
        out_specs=P("frames", "space", None, None),
        check_vma=False,
    )
```

```python
import functools
import math

import jax
import jax.numpy as jnp
from jax import lax
from jax.experimental import pallas as pl
from jax.experimental.pallas import tpu as pltpu
from jax.sharding import PartitionSpec as P

EDGE = 64
HEADS = 16


def shifted(block, axis, distance):
    devices = range(lax.axis_size(axis))
    route = [(i - distance, i) for i in devices if i - distance in devices]
    return lax.ppermute(block, axis, route)


def head_window(h, head_dim, width):
    lo = h * head_dim
    start = min((lo // 128) * 128, width - 256)
    return lo, start


def spatial_kernel(flags_ref, q_ref, k_ref, v_ref, ke_ref, ve_ref,
                   lat_ref, cache_ref, wo_ref, hid_ref, nrm_ref, acc_ref, sp_ref):
    i = pl.program_id(0)
    refreshed = flags_ref[i, 0]
    prev_ok = flags_ref[i, 1]
    next_ok = flags_ref[i, 2]
    width = q_ref.shape[-1]
    head_dim = width // HEADS
    scaling = 1.0 / math.sqrt(head_dim)
    nt = (((1,), (1,)), ((), ()))

    @pl.when(refreshed == 1)
    def _():
        acc_ref[...] = jnp.zeros_like(acc_ref)
        edge_lane = lax.broadcasted_iota(jnp.int32, (1, 2 * EDGE), 1)
        edge_ok = jnp.where(edge_lane < EDGE, prev_ok, next_ok) == 1
        for h in range(HEADS):
            lo, start = head_window(h, head_dim, width)
            win = pl.ds(start, 256)
            lane = lax.broadcasted_iota(jnp.int32, (1, 256), 1) + start
            mask = (lane >= lo) & (lane < lo + head_dim)
            qh = jnp.where(mask, q_ref[0, :, win], jnp.zeros((), q_ref.dtype))
            s_mid = lax.dot_general(qh, k_ref[0, :, win], nt,
                                    preferred_element_type=jnp.float32) * scaling
            s_edge = lax.dot_general(qh, ke_ref[0, :, win], nt,
                                     preferred_element_type=jnp.float32) * scaling
            s_edge = jnp.where(edge_ok, s_edge, -jnp.inf)
            top = jnp.maximum(jnp.max(s_mid, axis=1, keepdims=True),
                              jnp.max(s_edge, axis=1, keepdims=True))
            e_mid = jnp.exp(s_mid - top)
            e_edge = jnp.exp(s_edge - top)
            total = (jnp.sum(e_mid, axis=1, keepdims=True)
                     + jnp.sum(e_edge, axis=1, keepdims=True))
            inv = 1.0 / total
            p_mid = (e_mid * inv).astype(jnp.bfloat16)
            p_edge = (e_edge * inv).astype(jnp.bfloat16)
            out = jnp.dot(p_mid, v_ref[0, :, win], preferred_element_type=jnp.float32)
            out = out + jnp.dot(p_edge, ve_ref[0, :, win], preferred_element_type=jnp.float32)
            acc_ref[:, win] += jnp.where(mask, out, 0.0)
        sp_ref[...] = acc_ref[...].astype(sp_ref.dtype)

    @pl.when(refreshed != 1)
    def _():
        sp_ref[...] = cache_ref[0]

    projected = jnp.dot(sp_ref[...], wo_ref[...], preferred_element_type=jnp.float32)
    hidden = (lat_ref[0].astype(jnp.float32) + projected).astype(jnp.bfloat16)
    hid_ref[0] = hidden
    h32 = hidden.astype(jnp.float32)
    ms = jnp.mean(h32 * h32, axis=-1, keepdims=True)
    nrm_ref[0] = (h32 * lax.rsqrt(ms + 1e-06)).astype(nrm_ref.dtype)


def spatial_block(flags, q, k, v, ke, ve, lat, cache, wo):
    tiles, tok, width = q.shape
    tile_spec = pl.BlockSpec((1, tok, width), lambda i, f: (i, 0, 0))
    edge_spec = pl.BlockSpec((1, 2 * EDGE, width), lambda i, f: (i, 0, 0))
    w_spec = pl.BlockSpec((width, width), lambda i, f: (0, 0))
    out_shape = [jax.ShapeDtypeStruct((tiles, tok, width), jnp.bfloat16)] * 2
    flops = tiles * (HEADS * 4 * tok * (tok + 2 * EDGE) * 256 + 2 * tok * width * width)
    cost = pl.CostEstimate(flops=flops, transcendentals=tiles * HEADS * tok * (tok + 2 * EDGE),
                           bytes_accessed=2 * (7 * tiles * tok * width + width * width))
    return pl.pallas_call(
        spatial_kernel,
        grid_spec=pltpu.PrefetchScalarGridSpec(
            num_scalar_prefetch=1,
            grid=(tiles,),
            in_specs=[tile_spec] * 3 + [edge_spec] * 2 + [tile_spec] * 2 + [w_spec],
            out_specs=[tile_spec, tile_spec],
            scratch_shapes=[pltpu.VMEM((tok, width), jnp.float32),
                            pltpu.VMEM((tok, width), jnp.bfloat16)],
        ),
        out_shape=out_shape,
        compiler_params=pltpu.CompilerParams(dimension_semantics=("arbitrary",),
                                             vmem_limit_bytes=48 * 1024 * 1024),
        cost_estimate=cost,
    )(flags, q, k, v, ke, ve, lat, cache, wo)


def temporal_kernel(fid_ref, bw_ref, q_ref, k_ref, v_ref, ind_ref, indt_ref, o_ref):
    frames, tok, width = q_ref.shape
    head_dim = width // HEADS
    scaling = 1.0 / math.sqrt(head_dim)
    bw = bw_ref[...].reshape(1, 1, HEADS)
    ind = ind_ref[...]
    indt = indt_ref[...]
    fids = jnp.concatenate(
        [jnp.full((1, 1, 1), fid_ref[g], jnp.int32) for g in range(frames)], axis=0)

    def body(f, carry):
        qf = q_ref[f].astype(jnp.float32)
        prod = (qf[None] * k_ref[...].astype(jnp.float32)).reshape(frames * tok, width)
        hi = prod.astype(jnp.bfloat16)
        lo = (prod - hi.astype(jnp.float32)).astype(jnp.bfloat16)
        s = (jnp.dot(hi, ind, preferred_element_type=jnp.float32)
             + jnp.dot(lo, ind, preferred_element_type=jnp.float32))
        s = s.reshape(frames, tok, HEADS) * scaling
        allowed = jnp.abs(fids - fid_ref[f]) <= bw
        s = jnp.where(allowed, s, -jnp.inf)
        top = jnp.max(s, axis=0, keepdims=True)
        expo = jnp.exp(s - top)
        total = jnp.sum(expo, axis=0, keepdims=True)
        p = (expo / total).astype(jnp.bfloat16).reshape(frames * tok, HEADS)
        wide = jnp.dot(p, indt, preferred_element_type=jnp.float32).reshape(frames, tok, width)
        out = jnp.sum(wide * v_ref[...].astype(jnp.float32), axis=0)
        o_ref[f] = out.astype(o_ref.dtype)
        return carry

    lax.fori_loop(0, frames, body, 0)


def temporal_attend(packed, band_width, fids):
    frames, tok, wide = packed.shape
    width = wide // 3
    q = packed[..., :width]
    k = packed[..., width:2 * width]
    v = packed[..., 2 * width:]
    head_dim = width // HEADS
    ind = (jnp.arange(width, dtype=jnp.int32)[:, None] // head_dim
           == jnp.arange(HEADS, dtype=jnp.int32)[None, :])
    vspec = pl.BlockSpec(memory_space=pltpu.VMEM)
    sspec = pl.BlockSpec(memory_space=pltpu.SMEM)
    cost = pl.CostEstimate(flops=frames * frames * tok * width * 40,
                           transcendentals=frames * frames * tok * HEADS,
                           bytes_accessed=2 * 4 * frames * tok * width)
    return pl.pallas_call(
        temporal_kernel,
        in_specs=[sspec] + [vspec] * 6,
        out_specs=vspec,
        out_shape=jax.ShapeDtypeStruct((frames, tok, width), jnp.bfloat16),
        compiler_params=pltpu.CompilerParams(vmem_limit_bytes=48 * 1024 * 1024),
        cost_estimate=cost,
    )(fids, band_width.reshape(1, HEADS), q, k, v, ind.astype(jnp.bfloat16),
      ind.T.astype(jnp.bfloat16))


OFFSETS = ((0, 1), (-1, 0), (-1, 1), (1, 0), (1, 1), (2, 0), (2, 1))


def frame_dest(d, dy, dc, chips):
    return ((d // 2 + dy) % chips) * 2 + ((d % 2) ^ dc)


def frame_perm(dy, dc, n):
    chips = n // 2
    return [(d, frame_dest(d, dy, dc, chips)) for d in range(n)]


def exchange(send, n):
    recv = {}
    recv[(0, 1)] = lax.ppermute(send[(0, 1)], "frames", frame_perm(0, 1, n))
    for dc in (0, 1):
        recv[(-1, dc)] = lax.ppermute(send[(1, dc)], "frames", frame_perm(1, dc, n))
        recv[(1, dc)] = lax.ppermute(send[(-1, dc)], "frames", frame_perm(-1, dc, n))
    for dc in (0, 1):
        recv[(2, dc)] = lax.ppermute(send[(2, dc)], "frames", frame_perm(2, dc, n))
    return recv


def local(latent, query_rows, key_rows, value_rows, cached_out, refreshed, band_width,
          out_weight, temporal_weight):
    _, tile_count, tok_count, width = latent.shape
    lat = latent[0]
    q = query_rows[0]
    k = key_rows[0]
    v = value_rows[0]
    cache = cached_out[0]
    last_edges = jnp.stack([k[-1, -EDGE:], v[-1, -EDGE:]])
    first_edges = jnp.stack([k[0, :EDGE], v[0, :EDGE]])
    from_above = shifted(last_edges, "space", 1)
    from_below = shifted(first_edges, "space", -1)
    k, v = lax.optimization_barrier((k, v))
    kp = jnp.concatenate([from_above[0][None], k[:-1, -EDGE:]], axis=0)
    vp = jnp.concatenate([from_above[1][None], v[:-1, -EDGE:]], axis=0)
    kn = jnp.concatenate([k[1:, :EDGE], from_below[0][None]], axis=0)
    vn = jnp.concatenate([v[1:, :EDGE], from_below[1][None]], axis=0)
    total_tiles = tile_count * lax.axis_size("space")
    tile_index = lax.axis_index("space") * tile_count + jnp.arange(tile_count, dtype=jnp.int32)
    flags = jnp.stack([refreshed[0].astype(jnp.int32),
                       (tile_index > 0).astype(jnp.int32),
                       (tile_index < total_tiles - 1).astype(jnp.int32)], axis=1)
    ke = jnp.concatenate([kp, kn], axis=1)
    ve = jnp.concatenate([vp, vn], axis=1)
    hidden, normed = spatial_block(flags, q, k, v, ke, ve, lat, cache, out_weight)

    n = lax.axis_size("frames")
    chips = n // 2
    chunk = tok_count // n
    me = lax.axis_index("frames")
    dests = {o: frame_dest(me, o[0], o[1], chips) for o in OFFSETS}
    send = {o: lax.dynamic_slice_in_dim(normed, dests[o] * chunk, chunk, axis=1) for o in OFFSETS}
    recv = exchange(send, n)
    own = lax.dynamic_slice_in_dim(normed, me * chunk, chunk, axis=1)
    fids = jnp.stack([me] + [dests[o] for o in OFFSETS]).astype(jnp.int32)
    rows = tile_count * chunk
    early = jnp.stack([own, recv[(0, 1)]])
    late = jnp.stack([recv[o] for o in OFFSETS[1:]])
    flat_early = jnp.dot(early.reshape(-1, width), temporal_weight,
                         preferred_element_type=jnp.float32).astype(jnp.bfloat16)
    flat_late = jnp.dot(late.reshape(-1, width), temporal_weight,
                        preferred_element_type=jnp.float32).astype(jnp.bfloat16)
    packed = jnp.concatenate([flat_early, flat_late], axis=0).reshape(n, rows, 3 * width)
    attended = temporal_attend(packed, band_width, fids)
    attended = attended.reshape(n, tile_count, chunk, width)
    back = exchange({o: attended[1 + i] for i, o in enumerate(OFFSETS)}, n)
    def mix(out, piece, frame):
        part = lax.dynamic_slice_in_dim(hidden, frame * chunk, chunk, axis=1)
        total = (part.astype(jnp.float32) + piece.astype(jnp.float32)).astype(jnp.bfloat16)
        return lax.dynamic_update_slice_in_dim(out, total, frame * chunk, axis=1)

    mixed = mix(hidden, attended[0], me)
    for o in OFFSETS:
        mixed = mix(mixed, back[o], dests[o])
    return mixed[None]


def solution(mesh):
    return jax.shard_map(
        local,
        mesh=mesh,
        in_specs=(
            P("frames", "space", None, None),
            P("frames", "space", None, None),
            P("frames", "space", None, None),
            P("frames", "space", None, None),
            P("frames", "space", None, None),
            P("frames", "space"),
            P(),
            P(),
            P(),
        ),
        out_specs=P("frames", "space", None, None),
        check_vma=False,
    )
```

```python
import functools
import math

import jax
import jax.numpy as jnp
from jax import lax
from jax.experimental import pallas as pl
from jax.experimental.pallas import tpu as pltpu
from jax.sharding import PartitionSpec as P

EDGE = 64
HEADS = 16


def shifted(block, axis, distance):
    devices = range(lax.axis_size(axis))
    route = [(i - distance, i) for i in devices if i - distance in devices]
    return lax.ppermute(block, axis, route)


def head_window(h, head_dim, width):
    lo = h * head_dim
    start = min((lo // 128) * 128, width - 256)
    return lo, start


def spatial_kernel(flags_ref, q_ref, k_ref, v_ref, ke_ref, ve_ref,
                   lat_ref, cache_ref, wo_ref, hid_ref, nrm_ref, acc_ref, sp_ref):
    i = pl.program_id(0)
    refreshed = flags_ref[i, 0]
    prev_ok = flags_ref[i, 1]
    next_ok = flags_ref[i, 2]
    width = q_ref.shape[-1]
    head_dim = width // HEADS
    scaling = 1.0 / math.sqrt(head_dim)
    nt = (((1,), (1,)), ((), ()))

    @pl.when(refreshed == 1)
    def _():
        acc_ref[...] = jnp.zeros_like(acc_ref)
        edge_lane = lax.broadcasted_iota(jnp.int32, (1, 2 * EDGE), 1)
        edge_ok = jnp.where(edge_lane < EDGE, prev_ok, next_ok) == 1
        for h in range(HEADS):
            lo, start = head_window(h, head_dim, width)
            win = pl.ds(start, 256)
            lane = lax.broadcasted_iota(jnp.int32, (1, 256), 1) + start
            mask = (lane >= lo) & (lane < lo + head_dim)
            qh = jnp.where(mask, q_ref[0, :, win], jnp.zeros((), q_ref.dtype))
            s_mid = lax.dot_general(qh, k_ref[0, :, win], nt,
                                    preferred_element_type=jnp.float32) * scaling
            s_edge = lax.dot_general(qh, ke_ref[0, :, win], nt,
                                     preferred_element_type=jnp.float32) * scaling
            s_edge = jnp.where(edge_ok, s_edge, -jnp.inf)
            top = jnp.maximum(jnp.max(s_mid, axis=1, keepdims=True),
                              jnp.max(s_edge, axis=1, keepdims=True))
            e_mid = jnp.exp(s_mid - top)
            e_edge = jnp.exp(s_edge - top)
            total = (jnp.sum(e_mid, axis=1, keepdims=True)
                     + jnp.sum(e_edge, axis=1, keepdims=True))
            inv = 1.0 / total
            p_mid = (e_mid * inv).astype(jnp.bfloat16)
            p_edge = (e_edge * inv).astype(jnp.bfloat16)
            out = jnp.dot(p_mid, v_ref[0, :, win], preferred_element_type=jnp.float32)
            out = out + jnp.dot(p_edge, ve_ref[0, :, win], preferred_element_type=jnp.float32)
            acc_ref[:, win] += jnp.where(mask, out, 0.0)
        sp_ref[...] = acc_ref[...].astype(sp_ref.dtype)

    @pl.when(refreshed != 1)
    def _():
        sp_ref[...] = cache_ref[0]

    projected = jnp.dot(sp_ref[...], wo_ref[...], preferred_element_type=jnp.float32)
    hidden = (lat_ref[0].astype(jnp.float32) + projected).astype(jnp.bfloat16)
    hid_ref[0] = hidden
    h32 = hidden.astype(jnp.float32)
    ms = jnp.mean(h32 * h32, axis=-1, keepdims=True)
    nrm_ref[0] = (h32 * lax.rsqrt(ms + 1e-06)).astype(nrm_ref.dtype)


def spatial_block(flags, q, k, v, ke, ve, lat, cache, wo):
    tiles, tok, width = q.shape
    tile_spec = pl.BlockSpec((1, tok, width), lambda i, f: (i, 0, 0))
    edge_spec = pl.BlockSpec((1, 2 * EDGE, width), lambda i, f: (i, 0, 0))
    w_spec = pl.BlockSpec((width, width), lambda i, f: (0, 0))
    out_shape = [jax.ShapeDtypeStruct((tiles, tok, width), jnp.bfloat16)] * 2
    flops = tiles * (HEADS * 4 * tok * (tok + 2 * EDGE) * 256 + 2 * tok * width * width)
    cost = pl.CostEstimate(flops=flops, transcendentals=tiles * HEADS * tok * (tok + 2 * EDGE),
                           bytes_accessed=2 * (7 * tiles * tok * width + width * width))
    return pl.pallas_call(
        spatial_kernel,
        grid_spec=pltpu.PrefetchScalarGridSpec(
            num_scalar_prefetch=1,
            grid=(tiles,),
            in_specs=[tile_spec] * 3 + [edge_spec] * 2 + [tile_spec] * 2 + [w_spec],
            out_specs=[tile_spec, tile_spec],
            scratch_shapes=[pltpu.VMEM((tok, width), jnp.float32),
                            pltpu.VMEM((tok, width), jnp.bfloat16)],
        ),
        out_shape=out_shape,
        compiler_params=pltpu.CompilerParams(dimension_semantics=("arbitrary",),
                                             vmem_limit_bytes=48 * 1024 * 1024),
        cost_estimate=cost,
    )(flags, q, k, v, ke, ve, lat, cache, wo)


def temporal_kernel(fid_ref, bw_ref, q_ref, k_ref, v_ref, ind_ref, indt_ref, o_ref):
    frames, tok, width = q_ref.shape
    head_dim = width // HEADS
    scaling = 1.0 / math.sqrt(head_dim)
    bw = bw_ref[...].reshape(1, 1, HEADS)
    ind = ind_ref[...]
    indt = indt_ref[...]
    fids = jnp.concatenate(
        [jnp.full((1, 1, 1), fid_ref[g], jnp.int32) for g in range(frames)], axis=0)

    def body(f, carry):
        qf = q_ref[f].astype(jnp.float32)
        prod = (qf[None] * k_ref[...].astype(jnp.float32)).reshape(frames * tok, width)
        hi = prod.astype(jnp.bfloat16)
        lo = (prod - hi.astype(jnp.float32)).astype(jnp.bfloat16)
        s = (jnp.dot(hi, ind, preferred_element_type=jnp.float32)
             + jnp.dot(lo, ind, preferred_element_type=jnp.float32))
        s = s.reshape(frames, tok, HEADS) * scaling
        allowed = jnp.abs(fids - fid_ref[f]) <= bw
        s = jnp.where(allowed, s, -jnp.inf)
        top = jnp.max(s, axis=0, keepdims=True)
        expo = jnp.exp(s - top)
        total = jnp.sum(expo, axis=0, keepdims=True)
        p = (expo / total).astype(jnp.bfloat16).reshape(frames * tok, HEADS)
        wide = jnp.dot(p, indt, preferred_element_type=jnp.float32).reshape(frames, tok, width)
        out = jnp.sum(wide * v_ref[...].astype(jnp.float32), axis=0)
        o_ref[f] = out.astype(o_ref.dtype)
        return carry

    lax.fori_loop(0, frames, body, 0)


def temporal_attend(packed, band_width, fids):
    frames, tok, wide = packed.shape
    width = wide // 3
    q = packed[..., :width]
    k = packed[..., width:2 * width]
    v = packed[..., 2 * width:]
    head_dim = width // HEADS
    ind = (jnp.arange(width, dtype=jnp.int32)[:, None] // head_dim
           == jnp.arange(HEADS, dtype=jnp.int32)[None, :])
    vspec = pl.BlockSpec(memory_space=pltpu.VMEM)
    sspec = pl.BlockSpec(memory_space=pltpu.SMEM)
    cost = pl.CostEstimate(flops=frames * frames * tok * width * 40,
                           transcendentals=frames * frames * tok * HEADS,
                           bytes_accessed=2 * 4 * frames * tok * width)
    return pl.pallas_call(
        temporal_kernel,
        in_specs=[sspec] + [vspec] * 6,
        out_specs=vspec,
        out_shape=jax.ShapeDtypeStruct((frames, tok, width), jnp.bfloat16),
        compiler_params=pltpu.CompilerParams(vmem_limit_bytes=48 * 1024 * 1024),
        cost_estimate=cost,
    )(fids, band_width.reshape(1, HEADS), q, k, v, ind.astype(jnp.bfloat16),
      ind.T.astype(jnp.bfloat16))


OFFSETS = ((0, 1), (-1, 0), (-1, 1), (1, 0), (1, 1), (2, 0), (2, 1))


def frame_dest(d, dy, dc, chips):
    return ((d // 2 + dy) % chips) * 2 + ((d % 2) ^ dc)


def frame_perm(dy, dc, n):
    chips = n // 2
    return [(d, frame_dest(d, dy, dc, chips)) for d in range(n)]


def exchange(send, n):
    recv = {}
    recv[(0, 1)] = lax.ppermute(send[(0, 1)], "frames", frame_perm(0, 1, n))
    for dc in (0, 1):
        recv[(-1, dc)] = lax.ppermute(send[(1, dc)], "frames", frame_perm(1, dc, n))
        recv[(1, dc)] = lax.ppermute(send[(-1, dc)], "frames", frame_perm(-1, dc, n))
    for dc in (0, 1):
        recv[(2, dc)] = lax.ppermute(send[(2, dc)], "frames", frame_perm(2, dc, n))
    return recv


def local(latent, query_rows, key_rows, value_rows, cached_out, refreshed, band_width,
          out_weight, temporal_weight):
    _, tile_count, tok_count, width = latent.shape
    lat = latent[0]
    q = query_rows[0]
    k = key_rows[0]
    v = value_rows[0]
    cache = cached_out[0]
    last_edges = jnp.stack([k[-1, -EDGE:], v[-1, -EDGE:]])
    first_edges = jnp.stack([k[0, :EDGE], v[0, :EDGE]])
    from_above = shifted(last_edges, "space", 1)
    from_below = shifted(first_edges, "space", -1)
    kp = jnp.concatenate([from_above[0][None], k[:-1, -EDGE:]], axis=0)
    vp = jnp.concatenate([from_above[1][None], v[:-1, -EDGE:]], axis=0)
    kn = jnp.concatenate([k[1:, :EDGE], from_below[0][None]], axis=0)
    vn = jnp.concatenate([v[1:, :EDGE], from_below[1][None]], axis=0)
    total_tiles = tile_count * lax.axis_size("space")
    tile_index = lax.axis_index("space") * tile_count + jnp.arange(tile_count, dtype=jnp.int32)
    flags = jnp.stack([refreshed[0].astype(jnp.int32),
                       (tile_index > 0).astype(jnp.int32),
                       (tile_index < total_tiles - 1).astype(jnp.int32)], axis=1)
    ke = jnp.concatenate([kp, kn], axis=1)
    ve = jnp.concatenate([vp, vn], axis=1)
    hidden, normed = spatial_block(flags, q, k, v, ke, ve, lat, cache, out_weight)

    n = lax.axis_size("frames")
    chips = n // 2
    chunk = tok_count // n
    me = lax.axis_index("frames")
    dests = {o: frame_dest(me, o[0], o[1], chips) for o in OFFSETS}
    send = {o: lax.dynamic_slice_in_dim(normed, dests[o] * chunk, chunk, axis=1) for o in OFFSETS}
    recv = exchange(send, n)
    own = lax.dynamic_slice_in_dim(normed, me * chunk, chunk, axis=1)
    fids = jnp.stack([me] + [dests[o] for o in OFFSETS]).astype(jnp.int32)
    rows = tile_count * chunk
    early = jnp.stack([own, recv[(0, 1)]])
    near = jnp.stack([recv[o] for o in OFFSETS[1:5]])
    far = jnp.stack([recv[o] for o in OFFSETS[5:]])
    flats = [jnp.dot(group.reshape(-1, width), temporal_weight,
                     preferred_element_type=jnp.float32).astype(jnp.bfloat16)
             for group in (early, near, far)]
    packed = jnp.concatenate(flats, axis=0).reshape(n, rows, 3 * width)
    attended = temporal_attend(packed, band_width, fids)
    attended = attended.reshape(n, tile_count, chunk, width)
    back = exchange({o: attended[1 + i] for i, o in enumerate(OFFSETS)}, n)
    temporal = lax.dynamic_update_slice_in_dim(
        jnp.zeros_like(hidden), attended[0], me * chunk, axis=1)
    for o in OFFSETS:
        temporal = lax.dynamic_update_slice_in_dim(temporal, back[o], dests[o] * chunk, axis=1)
    mixed = (hidden.astype(jnp.float32) + temporal.astype(jnp.float32)).astype(jnp.bfloat16)
    return mixed[None]


def solution(mesh):
    return jax.shard_map(
        local,
        mesh=mesh,
        in_specs=(
            P("frames", "space", None, None),
            P("frames", "space", None, None),
            P("frames", "space", None, None),
            P("frames", "space", None, None),
            P("frames", "space", None, None),
            P("frames", "space"),
            P(),
            P(),
            P(),
        ),
        out_specs=P("frames", "space", None, None),
        check_vma=False,
    )
```

```python
import functools
import math

import jax
import jax.numpy as jnp
from jax import lax
from jax.experimental import pallas as pl
from jax.experimental.pallas import tpu as pltpu
from jax.sharding import PartitionSpec as P

EDGE = 64
HEADS = 16


def shifted(block, axis, distance):
    devices = range(lax.axis_size(axis))
    route = [(i - distance, i) for i in devices if i - distance in devices]
    return lax.ppermute(block, axis, route)


def head_window(h, head_dim, width):
    lo = h * head_dim
    start = min((lo // 128) * 128, width - 256)
    return lo, start


def spatial_kernel(flags_ref, q_ref, k_ref, v_ref, ke_ref, ve_ref,
                   lat_ref, cache_ref, wo_ref, hid_ref, nrm_ref, acc_ref, sp_ref):
    i = pl.program_id(0)
    refreshed = flags_ref[i, 0]
    prev_ok = flags_ref[i, 1]
    next_ok = flags_ref[i, 2]
    width = q_ref.shape[-1]
    head_dim = width // HEADS
    scaling = 1.0 / math.sqrt(head_dim)
    nt = (((1,), (1,)), ((), ()))

    @pl.when(refreshed == 1)
    def _():
        acc_ref[...] = jnp.zeros_like(acc_ref)
        edge_lane = lax.broadcasted_iota(jnp.int32, (1, 2 * EDGE), 1)
        edge_ok = jnp.where(edge_lane < EDGE, prev_ok, next_ok) == 1
        for h in range(HEADS):
            lo, start = head_window(h, head_dim, width)
            win = pl.ds(start, 256)
            lane = lax.broadcasted_iota(jnp.int32, (1, 256), 1) + start
            mask = (lane >= lo) & (lane < lo + head_dim)
            qh = jnp.where(mask, q_ref[0, :, win], jnp.zeros((), q_ref.dtype))
            s_mid = lax.dot_general(qh, k_ref[0, :, win], nt,
                                    preferred_element_type=jnp.float32) * scaling
            s_edge = lax.dot_general(qh, ke_ref[0, :, win], nt,
                                     preferred_element_type=jnp.float32) * scaling
            s_edge = jnp.where(edge_ok, s_edge, -jnp.inf)
            top = jnp.maximum(jnp.max(s_mid, axis=1, keepdims=True),
                              jnp.max(s_edge, axis=1, keepdims=True))
            e_mid = jnp.exp(s_mid - top)
            e_edge = jnp.exp(s_edge - top)
            total = (jnp.sum(e_mid, axis=1, keepdims=True)
                     + jnp.sum(e_edge, axis=1, keepdims=True))
            inv = 1.0 / total
            p_mid = (e_mid * inv).astype(jnp.bfloat16)
            p_edge = (e_edge * inv).astype(jnp.bfloat16)
            out = jnp.dot(p_mid, v_ref[0, :, win], preferred_element_type=jnp.float32)
            out = out + jnp.dot(p_edge, ve_ref[0, :, win], preferred_element_type=jnp.float32)
            acc_ref[:, win] += jnp.where(mask, out, 0.0)
        sp_ref[...] = acc_ref[...].astype(sp_ref.dtype)

    @pl.when(refreshed != 1)
    def _():
        sp_ref[...] = cache_ref[0]

    projected = jnp.dot(sp_ref[...], wo_ref[...], preferred_element_type=jnp.float32)
    hidden = (lat_ref[0].astype(jnp.float32) + projected).astype(jnp.bfloat16)
    hid_ref[0] = hidden
    h32 = hidden.astype(jnp.float32)
    ms = jnp.mean(h32 * h32, axis=-1, keepdims=True)
    nrm_ref[0] = (h32 * lax.rsqrt(ms + 1e-06)).astype(nrm_ref.dtype)


def spatial_block(flags, q, k, v, ke, ve, lat, cache, wo):
    tiles, tok, width = q.shape
    tile_spec = pl.BlockSpec((1, tok, width), lambda i, f: (i, 0, 0))
    edge_spec = pl.BlockSpec((1, 2 * EDGE, width), lambda i, f: (i, 0, 0))
    w_spec = pl.BlockSpec((width, width), lambda i, f: (0, 0))
    out_shape = [jax.ShapeDtypeStruct((tiles, tok, width), jnp.bfloat16)] * 2
    flops = tiles * (HEADS * 4 * tok * (tok + 2 * EDGE) * 256 + 2 * tok * width * width)
    cost = pl.CostEstimate(flops=flops, transcendentals=tiles * HEADS * tok * (tok + 2 * EDGE),
                           bytes_accessed=2 * (7 * tiles * tok * width + width * width))
    return pl.pallas_call(
        spatial_kernel,
        grid_spec=pltpu.PrefetchScalarGridSpec(
            num_scalar_prefetch=1,
            grid=(tiles,),
            in_specs=[tile_spec] * 3 + [edge_spec] * 2 + [tile_spec] * 2 + [w_spec],
            out_specs=[tile_spec, tile_spec],
            scratch_shapes=[pltpu.VMEM((tok, width), jnp.float32),
                            pltpu.VMEM((tok, width), jnp.bfloat16)],
        ),
        out_shape=out_shape,
        compiler_params=pltpu.CompilerParams(dimension_semantics=("arbitrary",),
                                             vmem_limit_bytes=48 * 1024 * 1024),
        cost_estimate=cost,
    )(flags, q, k, v, ke, ve, lat, cache, wo)


def temporal_kernel(fid_ref, bw_ref, q_ref, k_ref, v_ref, ind_ref, indt_ref, o_ref):
    frames, tok, width = q_ref.shape
    head_dim = width // HEADS
    scaling = 1.0 / math.sqrt(head_dim)
    bw = bw_ref[...].reshape(1, 1, HEADS)
    ind = ind_ref[...]
    indt = indt_ref[...]
    fids = jnp.concatenate(
        [jnp.full((1, 1, 1), fid_ref[g], jnp.int32) for g in range(frames)], axis=0)

    def body(f, carry):
        qf = q_ref[f].astype(jnp.float32)
        prod = (qf[None] * k_ref[...].astype(jnp.float32)).reshape(frames * tok, width)
        hi = prod.astype(jnp.bfloat16)
        lo = (prod - hi.astype(jnp.float32)).astype(jnp.bfloat16)
        s = (jnp.dot(hi, ind, preferred_element_type=jnp.float32)
             + jnp.dot(lo, ind, preferred_element_type=jnp.float32))
        s = s.reshape(frames, tok, HEADS) * scaling
        allowed = jnp.abs(fids - fid_ref[f]) <= bw
        s = jnp.where(allowed, s, -jnp.inf)
        top = jnp.max(s, axis=0, keepdims=True)
        expo = jnp.exp(s - top)
        total = jnp.sum(expo, axis=0, keepdims=True)
        p = (expo / total).astype(jnp.bfloat16).reshape(frames * tok, HEADS)
        wide = jnp.dot(p, indt, preferred_element_type=jnp.float32).reshape(frames, tok, width)
        out = jnp.sum(wide * v_ref[...].astype(jnp.float32), axis=0)
        o_ref[f] = out.astype(o_ref.dtype)
        return carry

    lax.fori_loop(0, frames, body, 0, unroll=2)


def temporal_attend(packed, band_width, fids):
    frames, tok, wide = packed.shape
    width = wide // 3
    q = packed[..., :width]
    k = packed[..., width:2 * width]
    v = packed[..., 2 * width:]
    head_dim = width // HEADS
    ind = (jnp.arange(width, dtype=jnp.int32)[:, None] // head_dim
           == jnp.arange(HEADS, dtype=jnp.int32)[None, :])
    vspec = pl.BlockSpec(memory_space=pltpu.VMEM)
    sspec = pl.BlockSpec(memory_space=pltpu.SMEM)
    cost = pl.CostEstimate(flops=frames * frames * tok * width * 40,
                           transcendentals=frames * frames * tok * HEADS,
                           bytes_accessed=2 * 4 * frames * tok * width)
    return pl.pallas_call(
        temporal_kernel,
        in_specs=[sspec] + [vspec] * 6,
        out_specs=vspec,
        out_shape=jax.ShapeDtypeStruct((frames, tok, width), jnp.bfloat16),
        compiler_params=pltpu.CompilerParams(vmem_limit_bytes=48 * 1024 * 1024),
        cost_estimate=cost,
    )(fids, band_width.reshape(1, HEADS), q, k, v, ind.astype(jnp.bfloat16),
      ind.T.astype(jnp.bfloat16))


OFFSETS = ((0, 1), (-1, 0), (-1, 1), (1, 0), (1, 1), (2, 0), (2, 1))


def frame_dest(d, dy, dc, chips):
    return ((d // 2 + dy) % chips) * 2 + ((d % 2) ^ dc)


def frame_perm(dy, dc, n):
    chips = n // 2
    return [(d, frame_dest(d, dy, dc, chips)) for d in range(n)]


def exchange(send, n):
    recv = {}
    recv[(0, 1)] = lax.ppermute(send[(0, 1)], "frames", frame_perm(0, 1, n))
    for dc in (0, 1):
        recv[(-1, dc)] = lax.ppermute(send[(1, dc)], "frames", frame_perm(1, dc, n))
        recv[(1, dc)] = lax.ppermute(send[(-1, dc)], "frames", frame_perm(-1, dc, n))
    for dc in (0, 1):
        recv[(2, dc)] = lax.ppermute(send[(2, dc)], "frames", frame_perm(2, dc, n))
    return recv


def local(latent, query_rows, key_rows, value_rows, cached_out, refreshed, band_width,
          out_weight, temporal_weight):
    _, tile_count, tok_count, width = latent.shape
    lat = latent[0]
    q = query_rows[0]
    k = key_rows[0]
    v = value_rows[0]
    cache = cached_out[0]
    last_edges = jnp.stack([k[-1, -EDGE:], v[-1, -EDGE:]])
    first_edges = jnp.stack([k[0, :EDGE], v[0, :EDGE]])
    from_above = shifted(last_edges, "space", 1)
    from_below = shifted(first_edges, "space", -1)
    kp = jnp.concatenate([from_above[0][None], k[:-1, -EDGE:]], axis=0)
    vp = jnp.concatenate([from_above[1][None], v[:-1, -EDGE:]], axis=0)
    kn = jnp.concatenate([k[1:, :EDGE], from_below[0][None]], axis=0)
    vn = jnp.concatenate([v[1:, :EDGE], from_below[1][None]], axis=0)
    total_tiles = tile_count * lax.axis_size("space")
    tile_index = lax.axis_index("space") * tile_count + jnp.arange(tile_count, dtype=jnp.int32)
    flags = jnp.stack([refreshed[0].astype(jnp.int32),
                       (tile_index > 0).astype(jnp.int32),
                       (tile_index < total_tiles - 1).astype(jnp.int32)], axis=1)
    ke = jnp.concatenate([kp, kn], axis=1)
    ve = jnp.concatenate([vp, vn], axis=1)
    hidden, normed = spatial_block(flags, q, k, v, ke, ve, lat, cache, out_weight)

    n = lax.axis_size("frames")
    chips = n // 2
    chunk = tok_count // n
    me = lax.axis_index("frames")
    dests = {o: frame_dest(me, o[0], o[1], chips) for o in OFFSETS}
    send = {o: lax.dynamic_slice_in_dim(normed, dests[o] * chunk, chunk, axis=1) for o in OFFSETS}
    recv = exchange(send, n)
    own = lax.dynamic_slice_in_dim(normed, me * chunk, chunk, axis=1)
    fids = jnp.stack([me] + [dests[o] for o in OFFSETS]).astype(jnp.int32)
    rows = tile_count * chunk
    early = jnp.stack([own, recv[(0, 1)]])
    late = jnp.stack([recv[o] for o in OFFSETS[1:]])
    flat_early = jnp.dot(early.reshape(-1, width), temporal_weight,
                         preferred_element_type=jnp.float32).astype(jnp.bfloat16)
    flat_late = jnp.dot(late.reshape(-1, width), temporal_weight,
                        preferred_element_type=jnp.float32).astype(jnp.bfloat16)
    packed = jnp.concatenate([flat_early, flat_late], axis=0).reshape(n, rows, 3 * width)
    attended = temporal_attend(packed, band_width, fids)
    attended = attended.reshape(n, tile_count, chunk, width)
    back = exchange({o: attended[1 + i] for i, o in enumerate(OFFSETS)}, n)
    temporal = lax.dynamic_update_slice_in_dim(
        jnp.zeros_like(hidden), attended[0], me * chunk, axis=1)
    for o in OFFSETS:
        temporal = lax.dynamic_update_slice_in_dim(temporal, back[o], dests[o] * chunk, axis=1)
    mixed = (hidden.astype(jnp.float32) + temporal.astype(jnp.float32)).astype(jnp.bfloat16)
    return mixed[None]


def solution(mesh):
    return jax.shard_map(
        local,
        mesh=mesh,
        in_specs=(
            P("frames", "space", None, None),
            P("frames", "space", None, None),
            P("frames", "space", None, None),
            P("frames", "space", None, None),
            P("frames", "space", None, None),
            P("frames", "space"),
            P(),
            P(),
            P(),
        ),
        out_specs=P("frames", "space", None, None),
        check_vma=False,
    )
```

```python
import functools
import math

import jax
import jax.numpy as jnp
from jax import lax
from jax.experimental import pallas as pl
from jax.experimental.pallas import tpu as pltpu
from jax.sharding import PartitionSpec as P

EDGE = 64
HEADS = 16


def shifted(block, axis, distance):
    devices = range(lax.axis_size(axis))
    route = [(i - distance, i) for i in devices if i - distance in devices]
    return lax.ppermute(block, axis, route)


def head_window(h, head_dim, width):
    lo = h * head_dim
    start = min((lo // 128) * 128, width - 256)
    return lo, start


def spatial_kernel(flags_ref, q_ref, k_ref, v_ref, ke_ref, ve_ref,
                   lat_ref, cache_ref, wo_ref, hid_ref, nrm_ref, acc_ref, sp_ref):
    i = pl.program_id(0)
    refreshed = flags_ref[i, 0]
    prev_ok = flags_ref[i, 1]
    next_ok = flags_ref[i, 2]
    width = q_ref.shape[-1]
    head_dim = width // HEADS
    scaling = 1.0 / math.sqrt(head_dim)
    nt = (((1,), (1,)), ((), ()))

    @pl.when(refreshed == 1)
    def _():
        acc_ref[...] = jnp.zeros_like(acc_ref)
        edge_lane = lax.broadcasted_iota(jnp.int32, (1, 2 * EDGE), 1)
        edge_ok = jnp.where(edge_lane < EDGE, prev_ok, next_ok) == 1
        for h in range(HEADS):
            lo, start = head_window(h, head_dim, width)
            win = pl.ds(start, 256)
            lane = lax.broadcasted_iota(jnp.int32, (1, 256), 1) + start
            mask = (lane >= lo) & (lane < lo + head_dim)
            qh = jnp.where(mask, q_ref[0, :, win], jnp.zeros((), q_ref.dtype))
            s_mid = lax.dot_general(qh, k_ref[0, :, win], nt,
                                    preferred_element_type=jnp.float32) * scaling
            s_edge = lax.dot_general(qh, ke_ref[0, :, win], nt,
                                     preferred_element_type=jnp.float32) * scaling
            s_edge = jnp.where(edge_ok, s_edge, -jnp.inf)
            top = jnp.maximum(jnp.max(s_mid, axis=1, keepdims=True),
                              jnp.max(s_edge, axis=1, keepdims=True))
            e_mid = jnp.exp(s_mid - top)
            e_edge = jnp.exp(s_edge - top)
            total = (jnp.sum(e_mid, axis=1, keepdims=True)
                     + jnp.sum(e_edge, axis=1, keepdims=True))
            inv = 1.0 / total
            p_mid = (e_mid * inv).astype(jnp.bfloat16)
            p_edge = (e_edge * inv).astype(jnp.bfloat16)
            out = jnp.dot(p_mid, v_ref[0, :, win], preferred_element_type=jnp.float32)
            out = out + jnp.dot(p_edge, ve_ref[0, :, win], preferred_element_type=jnp.float32)
            acc_ref[:, win] += jnp.where(mask, out, 0.0)
        sp_ref[...] = acc_ref[...].astype(sp_ref.dtype)

    @pl.when(refreshed != 1)
    def _():
        sp_ref[...] = cache_ref[0]

    projected = jnp.dot(sp_ref[...], wo_ref[...], preferred_element_type=jnp.float32)
    hidden = (lat_ref[0].astype(jnp.float32) + projected).astype(jnp.bfloat16)
    hid_ref[0] = hidden
    h32 = hidden.astype(jnp.float32)
    ms = jnp.mean(h32 * h32, axis=-1, keepdims=True)
    nrm_ref[0] = (h32 * lax.rsqrt(ms + 1e-06)).astype(nrm_ref.dtype)


def spatial_block(flags, q, k, v, ke, ve, lat, cache, wo):
    tiles, tok, width = q.shape
    tile_spec = pl.BlockSpec((1, tok, width), lambda i, f: (i, 0, 0))
    edge_spec = pl.BlockSpec((1, 2 * EDGE, width), lambda i, f: (i, 0, 0))
    w_spec = pl.BlockSpec((width, width), lambda i, f: (0, 0))
    out_shape = [jax.ShapeDtypeStruct((tiles, tok, width), jnp.bfloat16)] * 2
    flops = tiles * (HEADS * 4 * tok * (tok + 2 * EDGE) * 256 + 2 * tok * width * width)
    cost = pl.CostEstimate(flops=flops, transcendentals=tiles * HEADS * tok * (tok + 2 * EDGE),
                           bytes_accessed=2 * (7 * tiles * tok * width + width * width))
    return pl.pallas_call(
        spatial_kernel,
        grid_spec=pltpu.PrefetchScalarGridSpec(
            num_scalar_prefetch=1,
            grid=(tiles,),
            in_specs=[tile_spec] * 3 + [edge_spec] * 2 + [tile_spec] * 2 + [w_spec],
            out_specs=[tile_spec, tile_spec],
            scratch_shapes=[pltpu.VMEM((tok, width), jnp.float32),
                            pltpu.VMEM((tok, width), jnp.bfloat16)],
        ),
        out_shape=out_shape,
        compiler_params=pltpu.CompilerParams(dimension_semantics=("arbitrary",),
                                             vmem_limit_bytes=48 * 1024 * 1024),
        cost_estimate=cost,
    )(flags, q, k, v, ke, ve, lat, cache, wo)


def temporal_kernel(fid_ref, bw_ref, q_ref, k_ref, v_ref, ind_ref, indt_ref, o_ref):
    frames, tok, width = q_ref.shape
    head_dim = width // HEADS
    scaling = 1.0 / math.sqrt(head_dim)
    bw = bw_ref[...].reshape(1, 1, HEADS)
    ind = ind_ref[...]
    indt = indt_ref[...]
    fids = jnp.concatenate(
        [jnp.full((1, 1, 1), fid_ref[g], jnp.int32) for g in range(frames)], axis=0)

    def body(f, carry):
        qf = q_ref[f].astype(jnp.float32)
        prod = (qf[None] * k_ref[...].astype(jnp.float32)).reshape(frames * tok, width)
        hi = prod.astype(jnp.bfloat16)
        lo = (prod - hi.astype(jnp.float32)).astype(jnp.bfloat16)
        s = (jnp.dot(hi, ind, preferred_element_type=jnp.float32)
             + jnp.dot(lo, ind, preferred_element_type=jnp.float32))
        s = s.reshape(frames, tok, HEADS) * scaling
        allowed = jnp.abs(fids - fid_ref[f]) <= bw
        s = jnp.where(allowed, s, -jnp.inf)
        top = jnp.max(s, axis=0, keepdims=True)
        expo = jnp.exp(s - top)
        total = jnp.sum(expo, axis=0, keepdims=True)
        p = (expo / total).astype(jnp.bfloat16).reshape(frames * tok, HEADS)
        wide = jnp.dot(p, indt, preferred_element_type=jnp.float32).reshape(frames, tok, width)
        out = jnp.sum(wide * v_ref[...].astype(jnp.float32), axis=0)
        o_ref[f] = out.astype(o_ref.dtype)
        return carry

    lax.fori_loop(0, frames, body, 0, unroll=4)


def temporal_attend(packed, band_width, fids):
    frames, tok, wide = packed.shape
    width = wide // 3
    q = packed[..., :width]
    k = packed[..., width:2 * width]
    v = packed[..., 2 * width:]
    head_dim = width // HEADS
    ind = (jnp.arange(width, dtype=jnp.int32)[:, None] // head_dim
           == jnp.arange(HEADS, dtype=jnp.int32)[None, :])
    vspec = pl.BlockSpec(memory_space=pltpu.VMEM)
    sspec = pl.BlockSpec(memory_space=pltpu.SMEM)
    cost = pl.CostEstimate(flops=frames * frames * tok * width * 40,
                           transcendentals=frames * frames * tok * HEADS,
                           bytes_accessed=2 * 4 * frames * tok * width)
    return pl.pallas_call(
        temporal_kernel,
        in_specs=[sspec] + [vspec] * 6,
        out_specs=vspec,
        out_shape=jax.ShapeDtypeStruct((frames, tok, width), jnp.bfloat16),
        compiler_params=pltpu.CompilerParams(vmem_limit_bytes=48 * 1024 * 1024),
        cost_estimate=cost,
    )(fids, band_width.reshape(1, HEADS), q, k, v, ind.astype(jnp.bfloat16),
      ind.T.astype(jnp.bfloat16))


OFFSETS = ((0, 1), (-1, 0), (-1, 1), (1, 0), (1, 1), (2, 0), (2, 1))


def frame_dest(d, dy, dc, chips):
    return ((d // 2 + dy) % chips) * 2 + ((d % 2) ^ dc)


def frame_perm(dy, dc, n):
    chips = n // 2
    return [(d, frame_dest(d, dy, dc, chips)) for d in range(n)]


def exchange(send, n):
    recv = {}
    recv[(0, 1)] = lax.ppermute(send[(0, 1)], "frames", frame_perm(0, 1, n))
    for dc in (0, 1):
        recv[(-1, dc)] = lax.ppermute(send[(1, dc)], "frames", frame_perm(1, dc, n))
        recv[(1, dc)] = lax.ppermute(send[(-1, dc)], "frames", frame_perm(-1, dc, n))
    for dc in (0, 1):
        recv[(2, dc)] = lax.ppermute(send[(2, dc)], "frames", frame_perm(2, dc, n))
    return recv


def local(latent, query_rows, key_rows, value_rows, cached_out, refreshed, band_width,
          out_weight, temporal_weight):
    _, tile_count, tok_count, width = latent.shape
    lat = latent[0]
    q = query_rows[0]
    k = key_rows[0]
    v = value_rows[0]
    cache = cached_out[0]
    last_edges = jnp.stack([k[-1, -EDGE:], v[-1, -EDGE:]])
    first_edges = jnp.stack([k[0, :EDGE], v[0, :EDGE]])
    from_above = shifted(last_edges, "space", 1)
    from_below = shifted(first_edges, "space", -1)
    kp = jnp.concatenate([from_above[0][None], k[:-1, -EDGE:]], axis=0)
    vp = jnp.concatenate([from_above[1][None], v[:-1, -EDGE:]], axis=0)
    kn = jnp.concatenate([k[1:, :EDGE], from_below[0][None]], axis=0)
    vn = jnp.concatenate([v[1:, :EDGE], from_below[1][None]], axis=0)
    total_tiles = tile_count * lax.axis_size("space")
    tile_index = lax.axis_index("space") * tile_count + jnp.arange(tile_count, dtype=jnp.int32)
    flags = jnp.stack([refreshed[0].astype(jnp.int32),
                       (tile_index > 0).astype(jnp.int32),
                       (tile_index < total_tiles - 1).astype(jnp.int32)], axis=1)
    ke = jnp.concatenate([kp, kn], axis=1)
    ve = jnp.concatenate([vp, vn], axis=1)
    hidden, normed = spatial_block(flags, q, k, v, ke, ve, lat, cache, out_weight)

    n = lax.axis_size("frames")
    chips = n // 2
    chunk = tok_count // n
    me = lax.axis_index("frames")
    dests = {o: frame_dest(me, o[0], o[1], chips) for o in OFFSETS}
    send = {o: lax.dynamic_slice_in_dim(normed, dests[o] * chunk, chunk, axis=1) for o in OFFSETS}
    recv = exchange(send, n)
    own = lax.dynamic_slice_in_dim(normed, me * chunk, chunk, axis=1)
    fids = jnp.stack([me] + [dests[o] for o in OFFSETS]).astype(jnp.int32)
    rows = tile_count * chunk
    early = jnp.stack([own, recv[(0, 1)]])
    late = jnp.stack([recv[o] for o in OFFSETS[1:]])
    flat_early = jnp.dot(early.reshape(-1, width), temporal_weight,
                         preferred_element_type=jnp.float32).astype(jnp.bfloat16)
    flat_late = jnp.dot(late.reshape(-1, width), temporal_weight,
                        preferred_element_type=jnp.float32).astype(jnp.bfloat16)
    packed = jnp.concatenate([flat_early, flat_late], axis=0).reshape(n, rows, 3 * width)
    attended = temporal_attend(packed, band_width, fids)
    attended = attended.reshape(n, tile_count, chunk, width)
    back = exchange({o: attended[1 + i] for i, o in enumerate(OFFSETS)}, n)
    temporal = lax.dynamic_update_slice_in_dim(
        jnp.zeros_like(hidden), attended[0], me * chunk, axis=1)
    for o in OFFSETS:
        temporal = lax.dynamic_update_slice_in_dim(temporal, back[o], dests[o] * chunk, axis=1)
    mixed = (hidden.astype(jnp.float32) + temporal.astype(jnp.float32)).astype(jnp.bfloat16)
    return mixed[None]


def solution(mesh):
    return jax.shard_map(
        local,
        mesh=mesh,
        in_specs=(
            P("frames", "space", None, None),
            P("frames", "space", None, None),
            P("frames", "space", None, None),
            P("frames", "space", None, None),
            P("frames", "space", None, None),
            P("frames", "space"),
            P(),
            P(),
            P(),
        ),
        out_specs=P("frames", "space", None, None),
        check_vma=False,
    )
```

```python
import functools
import math

import jax
import jax.numpy as jnp
from jax import lax
from jax.experimental import pallas as pl
from jax.experimental.pallas import tpu as pltpu
from jax.sharding import PartitionSpec as P

EDGE = 64
HEADS = 16


def shifted(block, axis, distance):
    devices = range(lax.axis_size(axis))
    route = [(i - distance, i) for i in devices if i - distance in devices]
    return lax.ppermute(block, axis, route)


def head_window(h, head_dim, width):
    lo = h * head_dim
    start = min((lo // 128) * 128, width - 256)
    return lo, start


def spatial_kernel(flags_ref, q_ref, k_ref, v_ref, ke_ref, ve_ref,
                   lat_ref, cache_ref, wo_ref, hid_ref, nrm_ref, acc_ref, sp_ref):
    i = pl.program_id(0)
    refreshed = flags_ref[i, 0]
    prev_ok = flags_ref[i, 1]
    next_ok = flags_ref[i, 2]
    width = q_ref.shape[-1]
    head_dim = width // HEADS
    scaling = 1.0 / math.sqrt(head_dim)
    nt = (((1,), (1,)), ((), ()))

    @pl.when(refreshed == 1)
    def _():
        acc_ref[...] = jnp.zeros_like(acc_ref)
        edge_lane = lax.broadcasted_iota(jnp.int32, (1, 2 * EDGE), 1)
        edge_ok = jnp.where(edge_lane < EDGE, prev_ok, next_ok) == 1
        for h in range(HEADS):
            lo, start = head_window(h, head_dim, width)
            win = pl.ds(start, 256)
            lane = lax.broadcasted_iota(jnp.int32, (1, 256), 1) + start
            mask = (lane >= lo) & (lane < lo + head_dim)
            qh = jnp.where(mask, q_ref[0, :, win], jnp.zeros((), q_ref.dtype))
            s_mid = lax.dot_general(qh, k_ref[0, :, win], nt,
                                    preferred_element_type=jnp.float32) * scaling
            s_edge = lax.dot_general(qh, ke_ref[0, :, win], nt,
                                     preferred_element_type=jnp.float32) * scaling
            s_edge = jnp.where(edge_ok, s_edge, -jnp.inf)
            top = jnp.maximum(jnp.max(s_mid, axis=1, keepdims=True),
                              jnp.max(s_edge, axis=1, keepdims=True))
            e_mid = jnp.exp(s_mid - top)
            e_edge = jnp.exp(s_edge - top)
            total = (jnp.sum(e_mid, axis=1, keepdims=True)
                     + jnp.sum(e_edge, axis=1, keepdims=True))
            inv = 1.0 / total
            p_mid = (e_mid * inv).astype(jnp.bfloat16)
            p_edge = (e_edge * inv).astype(jnp.bfloat16)
            out = jnp.dot(p_mid, v_ref[0, :, win], preferred_element_type=jnp.float32)
            out = out + jnp.dot(p_edge, ve_ref[0, :, win], preferred_element_type=jnp.float32)
            acc_ref[:, win] += jnp.where(mask, out, 0.0)
        sp_ref[...] = acc_ref[...].astype(sp_ref.dtype)

    @pl.when(refreshed != 1)
    def _():
        sp_ref[...] = cache_ref[0]

    projected = jnp.dot(sp_ref[...], wo_ref[...], preferred_element_type=jnp.float32)
    hidden = (lat_ref[0].astype(jnp.float32) + projected).astype(jnp.bfloat16)
    hid_ref[0] = hidden
    h32 = hidden.astype(jnp.float32)
    ms = jnp.mean(h32 * h32, axis=-1, keepdims=True)
    nrm_ref[0] = (h32 * lax.rsqrt(ms + 1e-06)).astype(nrm_ref.dtype)


def spatial_block(flags, q, k, v, ke, ve, lat, cache, wo):
    tiles, tok, width = q.shape
    tile_spec = pl.BlockSpec((1, tok, width), lambda i, f: (i, 0, 0))
    edge_spec = pl.BlockSpec((1, 2 * EDGE, width), lambda i, f: (i, 0, 0))
    w_spec = pl.BlockSpec((width, width), lambda i, f: (0, 0))
    out_shape = [jax.ShapeDtypeStruct((tiles, tok, width), jnp.bfloat16)] * 2
    flops = tiles * (HEADS * 4 * tok * (tok + 2 * EDGE) * 256 + 2 * tok * width * width)
    cost = pl.CostEstimate(flops=flops, transcendentals=tiles * HEADS * tok * (tok + 2 * EDGE),
                           bytes_accessed=2 * (7 * tiles * tok * width + width * width))
    return pl.pallas_call(
        spatial_kernel,
        grid_spec=pltpu.PrefetchScalarGridSpec(
            num_scalar_prefetch=1,
            grid=(tiles,),
            in_specs=[tile_spec] * 3 + [edge_spec] * 2 + [tile_spec] * 2 + [w_spec],
            out_specs=[tile_spec, tile_spec],
            scratch_shapes=[pltpu.VMEM((tok, width), jnp.float32),
                            pltpu.VMEM((tok, width), jnp.bfloat16)],
        ),
        out_shape=out_shape,
        compiler_params=pltpu.CompilerParams(dimension_semantics=("arbitrary",),
                                             vmem_limit_bytes=48 * 1024 * 1024),
        cost_estimate=cost,
    )(flags, q, k, v, ke, ve, lat, cache, wo)


def temporal_kernel(fid_ref, bw_ref, q_ref, k_ref, v_ref, ind_ref, indt_ref, o_ref):
    frames, tok, width = q_ref.shape
    head_dim = width // HEADS
    scaling = 1.0 / math.sqrt(head_dim)
    bw = bw_ref[...].reshape(1, 1, HEADS)
    ind = ind_ref[...]
    indt = indt_ref[...]
    fids = jnp.concatenate(
        [jnp.full((1, 1, 1), fid_ref[g], jnp.int32) for g in range(frames)], axis=0)

    def body(f, carry):
        qf = q_ref[f].astype(jnp.float32)
        prod = (qf[None] * k_ref[...].astype(jnp.float32)).reshape(frames * tok, width)
        hi = prod.astype(jnp.bfloat16)
        lo = (prod - hi.astype(jnp.float32)).astype(jnp.bfloat16)
        s = (jnp.dot(hi, ind, preferred_element_type=jnp.float32)
             + jnp.dot(lo, ind, preferred_element_type=jnp.float32))
        s = s.reshape(frames, tok, HEADS) * scaling
        allowed = jnp.abs(fids - fid_ref[f]) <= bw
        s = jnp.where(allowed, s, -jnp.inf)
        top = jnp.max(s, axis=0, keepdims=True)
        expo = jnp.exp(s - top)
        total = jnp.sum(expo, axis=0, keepdims=True)
        p = (expo / total).astype(jnp.bfloat16).reshape(frames * tok, HEADS)
        wide = jnp.dot(p, indt, preferred_element_type=jnp.float32).reshape(frames, tok, width)
        out = jnp.sum(wide * v_ref[...].astype(jnp.float32), axis=0)
        o_ref[f] = out.astype(o_ref.dtype)
        return carry

    lax.fori_loop(0, frames, body, 0, unroll=8)


def temporal_attend(packed, band_width, fids):
    frames, tok, wide = packed.shape
    width = wide // 3
    q = packed[..., :width]
    k = packed[..., width:2 * width]
    v = packed[..., 2 * width:]
    head_dim = width // HEADS
    ind = (jnp.arange(width, dtype=jnp.int32)[:, None] // head_dim
           == jnp.arange(HEADS, dtype=jnp.int32)[None, :])
    vspec = pl.BlockSpec(memory_space=pltpu.VMEM)
    sspec = pl.BlockSpec(memory_space=pltpu.SMEM)
    cost = pl.CostEstimate(flops=frames * frames * tok * width * 40,
                           transcendentals=frames * frames * tok * HEADS,
                           bytes_accessed=2 * 4 * frames * tok * width)
    return pl.pallas_call(
        temporal_kernel,
        in_specs=[sspec] + [vspec] * 6,
        out_specs=vspec,
        out_shape=jax.ShapeDtypeStruct((frames, tok, width), jnp.bfloat16),
        compiler_params=pltpu.CompilerParams(vmem_limit_bytes=48 * 1024 * 1024),
        cost_estimate=cost,
    )(fids, band_width.reshape(1, HEADS), q, k, v, ind.astype(jnp.bfloat16),
      ind.T.astype(jnp.bfloat16))


OFFSETS = ((0, 1), (-1, 0), (-1, 1), (1, 0), (1, 1), (2, 0), (2, 1))


def frame_dest(d, dy, dc, chips):
    return ((d // 2 + dy) % chips) * 2 + ((d % 2) ^ dc)


def frame_perm(dy, dc, n):
    chips = n // 2
    return [(d, frame_dest(d, dy, dc, chips)) for d in range(n)]


def exchange(send, n):
    recv = {}
    recv[(0, 1)] = lax.ppermute(send[(0, 1)], "frames", frame_perm(0, 1, n))
    for dc in (0, 1):
        recv[(-1, dc)] = lax.ppermute(send[(1, dc)], "frames", frame_perm(1, dc, n))
        recv[(1, dc)] = lax.ppermute(send[(-1, dc)], "frames", frame_perm(-1, dc, n))
    for dc in (0, 1):
        recv[(2, dc)] = lax.ppermute(send[(2, dc)], "frames", frame_perm(2, dc, n))
    return recv


def local(latent, query_rows, key_rows, value_rows, cached_out, refreshed, band_width,
          out_weight, temporal_weight):
    _, tile_count, tok_count, width = latent.shape
    lat = latent[0]
    q = query_rows[0]
    k = key_rows[0]
    v = value_rows[0]
    cache = cached_out[0]
    last_edges = jnp.stack([k[-1, -EDGE:], v[-1, -EDGE:]])
    first_edges = jnp.stack([k[0, :EDGE], v[0, :EDGE]])
    from_above = shifted(last_edges, "space", 1)
    from_below = shifted(first_edges, "space", -1)
    kp = jnp.concatenate([from_above[0][None], k[:-1, -EDGE:]], axis=0)
    vp = jnp.concatenate([from_above[1][None], v[:-1, -EDGE:]], axis=0)
    kn = jnp.concatenate([k[1:, :EDGE], from_below[0][None]], axis=0)
    vn = jnp.concatenate([v[1:, :EDGE], from_below[1][None]], axis=0)
    total_tiles = tile_count * lax.axis_size("space")
    tile_index = lax.axis_index("space") * tile_count + jnp.arange(tile_count, dtype=jnp.int32)
    flags = jnp.stack([refreshed[0].astype(jnp.int32),
                       (tile_index > 0).astype(jnp.int32),
                       (tile_index < total_tiles - 1).astype(jnp.int32)], axis=1)
    ke = jnp.concatenate([kp, kn], axis=1)
    ve = jnp.concatenate([vp, vn], axis=1)
    hidden, normed = spatial_block(flags, q, k, v, ke, ve, lat, cache, out_weight)

    n = lax.axis_size("frames")
    chips = n // 2
    chunk = tok_count // n
    me = lax.axis_index("frames")
    dests = {o: frame_dest(me, o[0], o[1], chips) for o in OFFSETS}
    send = {o: lax.dynamic_slice_in_dim(normed, dests[o] * chunk, chunk, axis=1) for o in OFFSETS}
    recv = exchange(send, n)
    own = lax.dynamic_slice_in_dim(normed, me * chunk, chunk, axis=1)
    fids = jnp.stack([me] + [dests[o] for o in OFFSETS]).astype(jnp.int32)
    rows = tile_count * chunk
    early = jnp.stack([own, recv[(0, 1)]])
    late = jnp.stack([recv[o] for o in OFFSETS[1:]])
    flat_early = jnp.dot(early.reshape(-1, width), temporal_weight,
                         preferred_element_type=jnp.float32).astype(jnp.bfloat16)
    flat_late = jnp.dot(late.reshape(-1, width), temporal_weight,
                        preferred_element_type=jnp.float32).astype(jnp.bfloat16)
    packed = jnp.concatenate([flat_early, flat_late], axis=0).reshape(n, rows, 3 * width)
    attended = temporal_attend(packed, band_width, fids)
    attended = attended.reshape(n, tile_count, chunk, width)
    back = exchange({o: attended[1 + i] for i, o in enumerate(OFFSETS)}, n)
    temporal = lax.dynamic_update_slice_in_dim(
        jnp.zeros_like(hidden), attended[0], me * chunk, axis=1)
    for o in OFFSETS:
        temporal = lax.dynamic_update_slice_in_dim(temporal, back[o], dests[o] * chunk, axis=1)
    mixed = (hidden.astype(jnp.float32) + temporal.astype(jnp.float32)).astype(jnp.bfloat16)
    return mixed[None]


def solution(mesh):
    return jax.shard_map(
        local,
        mesh=mesh,
        in_specs=(
            P("frames", "space", None, None),
            P("frames", "space", None, None),
            P("frames", "space", None, None),
            P("frames", "space", None, None),
            P("frames", "space", None, None),
            P("frames", "space"),
            P(),
            P(),
            P(),
        ),
        out_specs=P("frames", "space", None, None),
        check_vma=False,
    )
```

```python
import functools
import math

import jax
import jax.numpy as jnp
from jax import lax
from jax.experimental import pallas as pl
from jax.experimental.pallas import tpu as pltpu
from jax.sharding import PartitionSpec as P

EDGE = 64
HEADS = 16


def shifted(block, axis, distance):
    devices = range(lax.axis_size(axis))
    route = [(i - distance, i) for i in devices if i - distance in devices]
    return lax.ppermute(block, axis, route)


def head_window(h, head_dim, width):
    lo = h * head_dim
    start = min((lo // 128) * 128, width - 256)
    return lo, start


def spatial_kernel(flags_ref, q_ref, k_ref, v_ref, ke_ref, ve_ref,
                   lat_ref, cache_ref, wo_ref, hid_ref, nrm_ref, acc_ref, sp_ref):
    i = pl.program_id(0)
    refreshed = flags_ref[i, 0]
    prev_ok = flags_ref[i, 1]
    next_ok = flags_ref[i, 2]
    width = q_ref.shape[-1]
    head_dim = width // HEADS
    scaling = 1.0 / math.sqrt(head_dim)
    nt = (((1,), (1,)), ((), ()))

    @pl.when(refreshed == 1)
    def _():
        acc_ref[...] = jnp.zeros_like(acc_ref)
        edge_lane = lax.broadcasted_iota(jnp.int32, (1, 2 * EDGE), 1)
        edge_ok = jnp.where(edge_lane < EDGE, prev_ok, next_ok) == 1
        for h in range(HEADS):
            lo, start = head_window(h, head_dim, width)
            win = pl.ds(start, 256)
            lane = lax.broadcasted_iota(jnp.int32, (1, 256), 1) + start
            mask = (lane >= lo) & (lane < lo + head_dim)
            qh = jnp.where(mask, q_ref[0, :, win], jnp.zeros((), q_ref.dtype))
            s_mid = lax.dot_general(qh, k_ref[0, :, win], nt,
                                    preferred_element_type=jnp.float32) * scaling
            s_edge = lax.dot_general(qh, ke_ref[0, :, win], nt,
                                     preferred_element_type=jnp.float32) * scaling
            s_edge = jnp.where(edge_ok, s_edge, -jnp.inf)
            top = jnp.maximum(jnp.max(s_mid, axis=1, keepdims=True),
                              jnp.max(s_edge, axis=1, keepdims=True))
            e_mid = jnp.exp(s_mid - top)
            e_edge = jnp.exp(s_edge - top)
            total = (jnp.sum(e_mid, axis=1, keepdims=True)
                     + jnp.sum(e_edge, axis=1, keepdims=True))
            inv = 1.0 / total
            p_mid = (e_mid * inv).astype(jnp.bfloat16)
            p_edge = (e_edge * inv).astype(jnp.bfloat16)
            zero = jnp.zeros((), v_ref.dtype)
            vh = jnp.where(mask, v_ref[0, :, win], zero)
            veh = jnp.where(mask, ve_ref[0, :, win], zero)
            out = jnp.dot(p_mid, vh, preferred_element_type=jnp.float32)
            out = out + jnp.dot(p_edge, veh, preferred_element_type=jnp.float32)
            acc_ref[:, win] += out
        sp_ref[...] = acc_ref[...].astype(sp_ref.dtype)

    @pl.when(refreshed != 1)
    def _():
        sp_ref[...] = cache_ref[0]

    projected = jnp.dot(sp_ref[...], wo_ref[...], preferred_element_type=jnp.float32)
    hidden = (lat_ref[0].astype(jnp.float32) + projected).astype(jnp.bfloat16)
    hid_ref[0] = hidden
    h32 = hidden.astype(jnp.float32)
    ms = jnp.mean(h32 * h32, axis=-1, keepdims=True)
    nrm_ref[0] = (h32 * lax.rsqrt(ms + 1e-06)).astype(nrm_ref.dtype)


def spatial_block(flags, q, k, v, ke, ve, lat, cache, wo):
    tiles, tok, width = q.shape
    tile_spec = pl.BlockSpec((1, tok, width), lambda i, f: (i, 0, 0))
    edge_spec = pl.BlockSpec((1, 2 * EDGE, width), lambda i, f: (i, 0, 0))
    w_spec = pl.BlockSpec((width, width), lambda i, f: (0, 0))
    out_shape = [jax.ShapeDtypeStruct((tiles, tok, width), jnp.bfloat16)] * 2
    flops = tiles * (HEADS * 4 * tok * (tok + 2 * EDGE) * 256 + 2 * tok * width * width)
    cost = pl.CostEstimate(flops=flops, transcendentals=tiles * HEADS * tok * (tok + 2 * EDGE),
                           bytes_accessed=2 * (7 * tiles * tok * width + width * width))
    return pl.pallas_call(
        spatial_kernel,
        grid_spec=pltpu.PrefetchScalarGridSpec(
            num_scalar_prefetch=1,
            grid=(tiles,),
            in_specs=[tile_spec] * 3 + [edge_spec] * 2 + [tile_spec] * 2 + [w_spec],
            out_specs=[tile_spec, tile_spec],
            scratch_shapes=[pltpu.VMEM((tok, width), jnp.float32),
                            pltpu.VMEM((tok, width), jnp.bfloat16)],
        ),
        out_shape=out_shape,
        compiler_params=pltpu.CompilerParams(dimension_semantics=("arbitrary",),
                                             vmem_limit_bytes=48 * 1024 * 1024),
        cost_estimate=cost,
    )(flags, q, k, v, ke, ve, lat, cache, wo)


def temporal_kernel(fid_ref, bw_ref, q_ref, k_ref, v_ref, ind_ref, indt_ref, o_ref):
    frames, tok, width = q_ref.shape
    head_dim = width // HEADS
    scaling = 1.0 / math.sqrt(head_dim)
    bw = bw_ref[...].reshape(1, 1, HEADS)
    ind = ind_ref[...]
    indt = indt_ref[...]
    fids = jnp.concatenate(
        [jnp.full((1, 1, 1), fid_ref[g], jnp.int32) for g in range(frames)], axis=0)

    def body(f, carry):
        qf = q_ref[f].astype(jnp.float32)
        prod = (qf[None] * k_ref[...].astype(jnp.float32)).reshape(frames * tok, width)
        hi = prod.astype(jnp.bfloat16)
        lo = (prod - hi.astype(jnp.float32)).astype(jnp.bfloat16)
        s = (jnp.dot(hi, ind, preferred_element_type=jnp.float32)
             + jnp.dot(lo, ind, preferred_element_type=jnp.float32))
        s = s.reshape(frames, tok, HEADS) * scaling
        allowed = jnp.abs(fids - fid_ref[f]) <= bw
        s = jnp.where(allowed, s, -jnp.inf)
        top = jnp.max(s, axis=0, keepdims=True)
        expo = jnp.exp(s - top)
        total = jnp.sum(expo, axis=0, keepdims=True)
        p = (expo / total).astype(jnp.bfloat16).reshape(frames * tok, HEADS)
        wide = jnp.dot(p, indt, preferred_element_type=jnp.float32).reshape(frames, tok, width)
        out = jnp.sum(wide * v_ref[...].astype(jnp.float32), axis=0)
        o_ref[f] = out.astype(o_ref.dtype)
        return carry

    lax.fori_loop(0, frames, body, 0, unroll=8)


def temporal_attend(packed, band_width, fids):
    frames, tok, wide = packed.shape
    width = wide // 3
    q = packed[..., :width]
    k = packed[..., width:2 * width]
    v = packed[..., 2 * width:]
    head_dim = width // HEADS
    ind = (jnp.arange(width, dtype=jnp.int32)[:, None] // head_dim
           == jnp.arange(HEADS, dtype=jnp.int32)[None, :])
    vspec = pl.BlockSpec(memory_space=pltpu.VMEM)
    sspec = pl.BlockSpec(memory_space=pltpu.SMEM)
    cost = pl.CostEstimate(flops=frames * frames * tok * width * 40,
                           transcendentals=frames * frames * tok * HEADS,
                           bytes_accessed=2 * 4 * frames * tok * width)
    return pl.pallas_call(
        temporal_kernel,
        in_specs=[sspec] + [vspec] * 6,
        out_specs=vspec,
        out_shape=jax.ShapeDtypeStruct((frames, tok, width), jnp.bfloat16),
        compiler_params=pltpu.CompilerParams(vmem_limit_bytes=48 * 1024 * 1024),
        cost_estimate=cost,
    )(fids, band_width.reshape(1, HEADS), q, k, v, ind.astype(jnp.bfloat16),
      ind.T.astype(jnp.bfloat16))


OFFSETS = ((0, 1), (-1, 0), (-1, 1), (1, 0), (1, 1), (2, 0), (2, 1))


def frame_dest(d, dy, dc, chips):
    return ((d // 2 + dy) % chips) * 2 + ((d % 2) ^ dc)


def frame_perm(dy, dc, n):
    chips = n // 2
    return [(d, frame_dest(d, dy, dc, chips)) for d in range(n)]


def exchange(send, n):
    recv = {}
    recv[(0, 1)] = lax.ppermute(send[(0, 1)], "frames", frame_perm(0, 1, n))
    for dc in (0, 1):
        recv[(-1, dc)] = lax.ppermute(send[(1, dc)], "frames", frame_perm(1, dc, n))
        recv[(1, dc)] = lax.ppermute(send[(-1, dc)], "frames", frame_perm(-1, dc, n))
    for dc in (0, 1):
        recv[(2, dc)] = lax.ppermute(send[(2, dc)], "frames", frame_perm(2, dc, n))
    return recv


def local(latent, query_rows, key_rows, value_rows, cached_out, refreshed, band_width,
          out_weight, temporal_weight):
    _, tile_count, tok_count, width = latent.shape
    lat = latent[0]
    q = query_rows[0]
    k = key_rows[0]
    v = value_rows[0]
    cache = cached_out[0]
    last_edges = jnp.stack([k[-1, -EDGE:], v[-1, -EDGE:]])
    first_edges = jnp.stack([k[0, :EDGE], v[0, :EDGE]])
    from_above = shifted(last_edges, "space", 1)
    from_below = shifted(first_edges, "space", -1)
    kp = jnp.concatenate([from_above[0][None], k[:-1, -EDGE:]], axis=0)
    vp = jnp.concatenate([from_above[1][None], v[:-1, -EDGE:]], axis=0)
    kn = jnp.concatenate([k[1:, :EDGE], from_below[0][None]], axis=0)
    vn = jnp.concatenate([v[1:, :EDGE], from_below[1][None]], axis=0)
    total_tiles = tile_count * lax.axis_size("space")
    tile_index = lax.axis_index("space") * tile_count + jnp.arange(tile_count, dtype=jnp.int32)
    flags = jnp.stack([refreshed[0].astype(jnp.int32),
                       (tile_index > 0).astype(jnp.int32),
                       (tile_index < total_tiles - 1).astype(jnp.int32)], axis=1)
    ke = jnp.concatenate([kp, kn], axis=1)
    ve = jnp.concatenate([vp, vn], axis=1)
    hidden, normed = spatial_block(flags, q, k, v, ke, ve, lat, cache, out_weight)

    n = lax.axis_size("frames")
    chips = n // 2
    chunk = tok_count // n
    me = lax.axis_index("frames")
    dests = {o: frame_dest(me, o[0], o[1], chips) for o in OFFSETS}
    send = {o: lax.dynamic_slice_in_dim(normed, dests[o] * chunk, chunk, axis=1) for o in OFFSETS}
    recv = exchange(send, n)
    own = lax.dynamic_slice_in_dim(normed, me * chunk, chunk, axis=1)
    fids = jnp.stack([me] + [dests[o] for o in OFFSETS]).astype(jnp.int32)
    rows = tile_count * chunk
    early = jnp.stack([own, recv[(0, 1)]])
    late = jnp.stack([recv[o] for o in OFFSETS[1:]])
    flat_early = jnp.dot(early.reshape(-1, width), temporal_weight,
                         preferred_element_type=jnp.float32).astype(jnp.bfloat16)
    flat_late = jnp.dot(late.reshape(-1, width), temporal_weight,
                        preferred_element_type=jnp.float32).astype(jnp.bfloat16)
    packed = jnp.concatenate([flat_early, flat_late], axis=0).reshape(n, rows, 3 * width)
    attended = temporal_attend(packed, band_width, fids)
    attended = attended.reshape(n, tile_count, chunk, width)
    back = exchange({o: attended[1 + i] for i, o in enumerate(OFFSETS)}, n)
    temporal = lax.dynamic_update_slice_in_dim(
        jnp.zeros_like(hidden), attended[0], me * chunk, axis=1)
    for o in OFFSETS:
        temporal = lax.dynamic_update_slice_in_dim(temporal, back[o], dests[o] * chunk, axis=1)
    mixed = (hidden.astype(jnp.float32) + temporal.astype(jnp.float32)).astype(jnp.bfloat16)
    return mixed[None]


def solution(mesh):
    return jax.shard_map(
        local,
        mesh=mesh,
        in_specs=(
            P("frames", "space", None, None),
            P("frames", "space", None, None),
            P("frames", "space", None, None),
            P("frames", "space", None, None),
            P("frames", "space", None, None),
            P("frames", "space"),
            P(),
            P(),
            P(),
        ),
        out_specs=P("frames", "space", None, None),
        check_vma=False,
    )
```
